512 devices in a mesh: head: 8 (over y), blk: 64 (over z, x, core).
Axes of the slice: x: 4, y: 8, z: 8, core: 2. Of those that a mesh axis runs over, the one named last changes fastest.
Arguments:
- inputs: bfloat16 [4, 64, 7168], P(None, None, 'blk'), may hold values from -40 to 40
- ln_gain: bfloat16 [7168], P('blk'), may hold values from 0.099609375 to 1.8984375
- ln_bias: bfloat16 [7168], P('blk'), may hold values from -3 to 3
- w_query: bfloat16 [7168, 7168], P('blk', 'head'), may hold values from -0.0625 to 0.0625
- w_key: bfloat16 [7168, 7168], P('blk', 'head'), may hold values from -0.0625 to 0.0625
- w_value: bfloat16 [7168, 7168], P('blk', 'head'), may hold values from -0.0625 to 0.0625
- b_query: bfloat16 [7168], P('head'), may hold values from -3 to 3
- b_key: bfloat16 [7168], P('head'), may hold values from -4 to 4
- b_value: bfloat16 [7168], P('head'), may hold values from -3 to 3
- w_out: bfloat16 [7168, 7168], P('head', 'blk'), may hold values from -0.5 to 0.5
- b_out: bfloat16 [7168], P('blk'), may hold values from -3 to 3
- prefix_keys: bfloat16 [1536, 16, 7168], P('blk', None, 'head'), may hold values from -110 to 110
- prefix_values: bfloat16 [1536, 16, 7168], P('blk', None, 'head'), may hold values from -6 to 6
- suffix_keys: bfloat16 [64, 256, 7168], P('blk', None, 'head'), may hold values from -110 to 110
- suffix_values: bfloat16 [64, 256, 7168], P('blk', None, 'head'), may hold values from -6 to 6
- page_table: int32 [8, 288], replicated, may hold values from 0 to 1535, as said below
- prompt_len: int32 [8], replicated, may hold values from 1 to 4608, as said below
- gen_len: int32 [8], replicated, may hold values from 1 to 252, as said below
- parents: int32 [4, 64], replicated, may hold values from 0 to 63, as said below
Outputs:
- hidden: bfloat16 [4, 64, 7168], P(None, None, 'blk')
- final_keys: bfloat16 [64, 256, 7168], P('blk', None, 'head')
- final_values: bfloat16 [64, 256, 7168], P('blk', None, 'head')
The draws below stay inside these ranges and needn't reach their ends.
Inputs may be any that keep to these rules, and one draw needn't show every extreme that they name: `page_table`: the first ceil(prompt_len[r] / 16) entries of row r are distinct pages that no other request lists; later entries are 0 and hold no tokens of r. `prompt_len`: the longest request has exactly 4608 tokens. `gen_len`: some request has exactly 252. parents[s, b] is a beam of the same request as b.
All inputs are finite; a program needn't handle non-finite values.
Results may differ from the reference program's by a relative error of at most 0.0065.
The reference program's roundings to bfloat16 on the way count: a program that leaves them out, or rounds other values in their place, can miss the bound.
Values may be sent and summed in bfloat16 or wider, within the bound.
No kernel may reach another device: no remote copies, remote signals or barrier semaphores. Data moves between devices by JAX's collectives and lax.ppermute only.
A program may use at most 128 MiB of HBM per device.

```python
import math
import jax
import jax.numpy as jnp
from jax import lax

D = 7168
HEADS = 56
HEAD_DIM = 128
FEAT = 7168
BEAMS = 8
BATCH = 64
REQS = 8
PAGE = 16
NPAGES = 1536
MAXP = 288
GEN = 256
STEPS = 4


def key_field(key, shape):
    noise_key = jax.random.fold_in(key, 0)
    field = jnp.clip(2.0 * jax.random.normal(noise_key, shape), -12.0, 12.0)
    return field.astype(jnp.bfloat16)


def draw_prefix_keys(key, part):
    return key_field(jax.random.fold_in(key, 3), (NPAGES, PAGE, HEADS * HEAD_DIM))


def draw_suffix_keys(key, part):
    return key_field(jax.random.fold_in(key, 5), (BATCH, GEN, HEADS * HEAD_DIM))


def draw_inputs(key, part):
    noise_key, scale_key = jax.random.split(jax.random.fold_in(key, 2), 2)
    position = jnp.arange(D, dtype=jnp.float32) / D
    feature_scale = 0.6 * jnp.exp(position * math.log(3.0)) * jax.random.uniform(scale_key, (D,), minval=0.7, maxval=1.4)
    field = jnp.clip(jax.random.normal(noise_key, (STEPS, BATCH, D)), -6.0, 6.0) * feature_scale
    return field.astype(jnp.bfloat16)


def page_plan(key):
    plan_key = jax.random.fold_in(key, 7)
    count_key, long_key, perm_key, trim_key = jax.random.split(plan_key, 4)
    spare = (NPAGES - MAXP) // (REQS - 1)
    counts = jax.random.randint(count_key, (REQS,), 1, spare + 1)
    longest = jax.random.randint(long_key, (), 0, REQS)
    is_long = jnp.arange(REQS) == longest
    counts = jnp.where(is_long, MAXP, counts)
    page_order = jax.random.permutation(perm_key, NPAGES)
    starts = jnp.cumsum(counts) - counts
    slot_ids = jnp.arange(MAXP)
    pool_index = jnp.minimum(starts[:, None] + slot_ids[None, :], NPAGES - 1)
    page_rows = jnp.where(slot_ids[None, :] < counts[:, None], page_order[pool_index], 0)
    trimmed = jnp.where(is_long, 0, jax.random.randint(trim_key, (REQS,), 0, PAGE))
    lengths = counts * PAGE - trimmed
    return (page_rows.astype(jnp.int32), lengths.astype(jnp.int32))


def draw_page_table(key, part):
    return page_plan(key)[0]


def draw_prompt_len(key, part):
    return page_plan(key)[1]


def draw_gen_len(key, part):
    count_key, long_key = jax.random.split(jax.random.fold_in(key, 11), 2)
    counts = jax.random.randint(count_key, (REQS,), 1, GEN - STEPS + 1)
    longest = jax.random.randint(long_key, (), 0, REQS)
    return jnp.where(jnp.arange(REQS) == longest, GEN - STEPS, counts).astype(jnp.int32)


def draw_parents(key, part):
    choice_key = jax.random.fold_in(key, 13)
    group_start = jnp.arange(BATCH) // BEAMS * BEAMS
    return (group_start[None, :] + jax.random.randint(choice_key, (STEPS, BATCH), 0, BEAMS)).astype(jnp.int32)


def shard_levels(rng, extent, shards, least, top_value):
    loudness = 1.0
    for dim, blocks in shards:
        draws = jax.random.uniform(jax.random.fold_in(jax.random.fold_in(rng, 6), dim), (blocks,), jnp.float32, least / len(shards), top_value / len(shards))
        loudness = loudness * jnp.repeat(jnp.exp(draws), extent[dim] // blocks).reshape((-1,) + (1,) * (len(extent) - 1 - dim))
    return loudness


def centred(own_key, dims, width, reach, cuts=(), kind=jnp.bfloat16):
    entries = width * jax.random.normal(own_key, dims, jnp.float32)
    if cuts:
        entries = entries * shard_levels(own_key, dims, cuts, -0.22, 0.18)
    return jnp.clip(entries, -reach, reach).astype(kind)


def setup_inputs(seed: int = 0) -> dict:
    arg_keys = jax.random.split(jax.random.key(seed), 20)
    return {
        "inputs": draw_inputs(jax.random.fold_in(arg_keys[19], 71), 0),
        "ln_gain": jnp.clip(1.0 + 0.18 * jax.random.normal(arg_keys[1], (D,), jnp.float32), 0.099609375, 1.8984375).astype(jnp.bfloat16),
        "ln_bias": centred(arg_keys[2], (D,), 0.5, 3.0, ((0, 64),)),
        "w_query": centred(arg_keys[3], (D, FEAT), D ** -0.5, 0.0625, ((0, 64), (1, 8))),
        "w_key": centred(arg_keys[4], (D, FEAT), D ** -0.5, 0.0625, ((0, 64), (1, 8))),
        "w_value": centred(arg_keys[5], (D, FEAT), D ** -0.5, 0.0625, ((0, 64), (1, 8))),
        "b_query": centred(arg_keys[6], (FEAT,), 0.5, 3.0, ((0, 8),)),
        "b_key": centred(arg_keys[7], (FEAT,), 1.0, 4.0, ((0, 8),)),
        "b_value": centred(arg_keys[8], (FEAT,), 0.5, 3.0, ((0, 8),)),
        "w_out": centred(arg_keys[9], (FEAT, D), HEAD_DIM ** -0.5, 0.5, ((0, 8), (1, 64))),
        "b_out": centred(arg_keys[10], (D,), 0.5, 3.0, ((0, 64),)),
        "prefix_keys": draw_prefix_keys(jax.random.fold_in(arg_keys[19], 71), 0),
        "prefix_values": centred(arg_keys[12], (NPAGES, PAGE, FEAT), 1.0, 6.0, ((0, 64), (2, 8))),
        "suffix_keys": draw_suffix_keys(jax.random.fold_in(arg_keys[19], 71), 0),
        "suffix_values": centred(arg_keys[14], (BATCH, GEN, FEAT), 1.0, 6.0, ((0, 64), (2, 8))),
        "page_table": draw_page_table(jax.random.fold_in(arg_keys[19], 71), 0),
        "prompt_len": draw_prompt_len(jax.random.fold_in(arg_keys[19], 71), 0),
        "gen_len": draw_gen_len(jax.random.fold_in(arg_keys[19], 71), 0),
        "parents": draw_parents(jax.random.fold_in(arg_keys[19], 71), 0),
    }


MASKED = -1e+30
NORM_EPSILON = 1e-05

def reference(inputs, ln_gain, ln_bias, w_query, w_key, w_value, b_query, b_key, b_value, w_out, b_out, prefix_keys, prefix_values, suffix_keys, suffix_values, page_table, prompt_len, gen_len, parents):
    score_scale = 1.0 / math.sqrt(HEAD_DIM)
    feat_all = HEADS * HEAD_DIM
    beam_request = jnp.arange(BATCH, dtype=jnp.int32) // BEAMS
    gen_rows = jnp.arange(GEN, dtype=jnp.int32)
    token_pos = jnp.arange(MAXP * PAGE, dtype=jnp.int32)
    norm_gain = ln_gain.astype(jnp.float32)
    norm_shift = ln_bias.astype(jnp.float32)
    beam_keys = suffix_keys
    beam_values = suffix_values
    hidden_steps = []
    for step_index in range(STEPS):
        rows_in = inputs[step_index].astype(jnp.float32)
        row_mean = lax.optimization_barrier(jnp.sum(rows_in, axis=1)) / D
        variance = lax.optimization_barrier(jnp.sum(rows_in * rows_in, axis=1)) / D - row_mean * row_mean
        normed = ((rows_in - row_mean[:, None]) * lax.rsqrt(variance + NORM_EPSILON)[:, None] * norm_gain + norm_shift).astype(jnp.bfloat16)
        queries = (jnp.dot(normed, w_query, preferred_element_type=jnp.float32) + b_query.astype(jnp.float32)).astype(jnp.bfloat16)
        new_keys = (jnp.dot(normed, w_key, preferred_element_type=jnp.float32) + b_key.astype(jnp.float32)).astype(jnp.bfloat16)
        new_values = (jnp.dot(normed, w_value, preferred_element_type=jnp.float32) + b_value.astype(jnp.float32)).astype(jnp.bfloat16)
        beam_keys = jnp.take(beam_keys, parents[step_index], axis=0)
        beam_values = jnp.take(beam_values, parents[step_index], axis=0)
        write_pos = jnp.take(gen_len, beam_request) + step_index
        written = (gen_rows[None, :] == write_pos[:, None])[:, :, None]
        beam_keys = jnp.where(written, new_keys[:, None, :], beam_keys)
        beam_values = jnp.where(written, new_values[:, None, :], beam_values)

        def attend(request):
            page_rows = page_table[request]
            page_keys = jnp.take(prefix_keys, page_rows, axis=0).reshape(MAXP * PAGE, HEADS, HEAD_DIM).astype(jnp.float32)
            page_values = jnp.take(prefix_values, page_rows, axis=0).reshape(MAXP * PAGE, HEADS, HEAD_DIM).astype(jnp.float32)
            first_beam = (request * BEAMS).astype(jnp.int32)
            own_queries = lax.dynamic_slice_in_dim(queries, first_beam, BEAMS, 0).reshape(BEAMS, HEADS, HEAD_DIM).astype(jnp.float32)
            own_keys = lax.dynamic_slice_in_dim(beam_keys, first_beam, BEAMS, 0).reshape(BEAMS, GEN, HEADS, HEAD_DIM).astype(jnp.float32)
            own_values = lax.dynamic_slice_in_dim(beam_values, first_beam, BEAMS, 0).reshape(BEAMS, GEN, HEADS, HEAD_DIM).astype(jnp.float32)
            prompt_scores = jnp.einsum('bhd,thd->bht', own_queries, page_keys) * score_scale
            prompt_live = (token_pos < prompt_len[request])[None, None, :]
            beam_scores = jnp.einsum('bhd,bthd->bht', own_queries, own_keys) * score_scale
            beam_live = (gen_rows <= gen_len[request] + step_index)[None, None, :]
            top_score = jnp.maximum(lax.optimization_barrier(jnp.max(jnp.where(prompt_live, prompt_scores, MASKED), axis=2)), lax.optimization_barrier(jnp.max(jnp.where(beam_live, beam_scores, MASKED), axis=2)))
            prompt_weights = jnp.where(prompt_live, jnp.exp(prompt_scores - top_score[:, :, None]), 0.0).astype(jnp.bfloat16)
            prompt_weights = lax.optimization_barrier(prompt_weights).astype(jnp.float32)
            beam_weights = jnp.where(beam_live, jnp.exp(beam_scores - top_score[:, :, None]), 0.0).astype(jnp.bfloat16)
            beam_weights = lax.optimization_barrier(beam_weights).astype(jnp.float32)
            totals = lax.optimization_barrier(jnp.sum(prompt_weights, axis=2)) + lax.optimization_barrier(jnp.sum(beam_weights, axis=2))
            weighted = jnp.einsum('bht,thd->bhd', prompt_weights, page_values) + jnp.einsum('bht,bthd->bhd', beam_weights, own_values)
            return (weighted / totals[:, :, None]).reshape(BEAMS, feat_all)
        attention = lax.map(attend, jnp.arange(REQS, dtype=jnp.int32)).reshape(BATCH, feat_all).astype(jnp.bfloat16)
        hidden_steps.append((jnp.dot(attention, w_out, preferred_element_type=jnp.float32) + b_out.astype(jnp.float32)).astype(jnp.bfloat16))
    return (jnp.stack(hidden_steps, axis=0), beam_keys, beam_values)
```

```python
import math

import jax
import jax.numpy as jnp
import numpy as np
from jax import lax
from jax.sharding import Mesh
from jax.sharding import PartitionSpec as P

D = 7168
HEAD_DIM = 128
BEAMS = 8
PAGE = 16
GEN = 256
STEPS = 4

MASKED = -1e30
NORM_EPSILON = 1e-05

BLK_PARTS = ("z", "x", "core")
GROUP = ("x", "core")


def nested(reduce, value):
    for axis in reversed(BLK_PARTS):
        value = reduce(value, axis)
    return value


def blk_index():
    index = lax.axis_index("z")
    for axis in BLK_PARTS[1:]:
        index = index * lax.axis_size(axis) + lax.axis_index(axis)
    return index


def body(
    inputs,
    ln_gain,
    ln_bias,
    w_query,
    w_key,
    w_value,
    b_query,
    b_key,
    b_value,
    w_out,
    b_out,
    prefix_keys,
    prefix_values,
    suffix_keys,
    suffix_values,
    page_table,
    prompt_len,
    gen_len,
    parents,
):
    blocks = 1
    for axis in BLK_PARTS:
        blocks *= lax.axis_size(axis)
    me = blk_index()
    steps = inputs.shape[0]
    batch = inputs.shape[1]
    feat_here = w_query.shape[1]
    heads_here = feat_here // HEAD_DIM
    pages_here = prefix_keys.shape[0]
    requests = page_table.shape[0]
    slot_count = page_table.shape[1]
    rows = steps * batch
    score_scale = 1.0 / math.sqrt(HEAD_DIM)
    my_request = me // BEAMS
    first_beam = my_request * BEAMS
    my_gen = gen_len[my_request]

    beam_ids = jnp.arange(batch, dtype=jnp.int32)
    anc = {}
    for s in range(steps):
        x = beam_ids
        anc[(s, s)] = x
        for t in range(s, -1, -1):
            x = jnp.take(parents[t], x)
            anc[(t - 1, s)] = x
    origin = jnp.stack([anc[(-1, s)] for s in range(steps)])

    rows_in = inputs.astype(jnp.float32).reshape(rows, -1)
    stats = jnp.stack([jnp.sum(rows_in, axis=1), jnp.sum(rows_in * rows_in, axis=1)], axis=1)
    stats = nested(lax.psum, stats)
    row_mean = stats[:, 0] / D
    variance = stats[:, 1] / D - row_mean * row_mean
    normed = (
        (rows_in - row_mean[:, None]) * lax.rsqrt(variance + NORM_EPSILON)[:, None]
        * ln_gain.astype(jnp.float32)
        + ln_bias.astype(jnp.float32)
    ).astype(jnp.bfloat16)
    weights_all = jnp.concatenate([w_query, w_key, w_value], axis=1)
    bias_all = jnp.concatenate([b_query, b_key, b_value]).astype(jnp.float32)
    partial = jnp.dot(normed, weights_all, preferred_element_type=jnp.float32)
    projected = (nested(lax.psum, partial) + bias_all[None, :]).astype(jnp.bfloat16)
    queries = projected[:, :feat_here].reshape(steps, batch, heads_here, HEAD_DIM)
    key_new = projected[:, feat_here : 2 * feat_here].reshape(steps, batch, feat_here)
    value_new = projected[:, 2 * feat_here :].reshape(steps, batch, feat_here)

    beam_request = beam_ids // BEAMS
    beam_prompt = jnp.take(prompt_len, beam_request)
    page_ids = me * pages_here + jnp.arange(pages_here, dtype=jnp.int32)
    slot_ids = jnp.arange(slot_count, dtype=jnp.int32)
    slot_live = slot_ids[None, :] * PAGE < prompt_len[:, None]
    page_match = (
        (page_table[:, :, None] == page_ids[None, None, :]) & slot_live[:, :, None]
    ).astype(jnp.int32)
    request_ids = jnp.arange(requests, dtype=jnp.int32)
    page_request = jnp.sum(page_match * request_ids[:, None, None], axis=(0, 1))
    page_slot = jnp.sum(page_match * slot_ids[None, :, None], axis=(0, 1))
    page_used = jnp.sum(page_match, axis=(0, 1)) > 0
    token_pos = (page_slot[:, None] * PAGE + jnp.arange(PAGE, dtype=jnp.int32)[None, :]).reshape(-1)
    token_request = jnp.repeat(page_request, PAGE)
    token_used = jnp.repeat(page_used, PAGE)
    prefix_live = (
        token_used[None, :]
        & (token_request[None, :] == beam_request[:, None])
        & (token_pos[None, :] < beam_prompt[:, None])
    )
    page_keys = prefix_keys.reshape(pages_here * PAGE, heads_here, HEAD_DIM)
    page_values = prefix_values.reshape(pages_here * PAGE, heads_here, HEAD_DIM)
    flat_queries = queries.reshape(rows, heads_here, HEAD_DIM)
    prompt_scores = (
        jnp.einsum("rhd,thd->rht", flat_queries, page_keys, preferred_element_type=jnp.float32)
        * score_scale
    ).reshape(steps, batch, heads_here, -1)
    prompt_live = prefix_live[None, :, None, :]
    prompt_top = jnp.max(jnp.where(prompt_live, prompt_scores, MASKED), axis=3)

    group_queries = lax.dynamic_slice_in_dim(queries, first_beam, BEAMS, axis=1)
    group_origin = lax.dynamic_slice_in_dim(origin, first_beam, BEAMS, axis=1)
    own_keys = suffix_keys[0].reshape(GEN, heads_here, HEAD_DIM)
    own_values = suffix_values[0].reshape(GEN, heads_here, HEAD_DIM)
    cache_scores = (
        jnp.einsum("sbhd,jhd->sbhj", group_queries, own_keys, preferred_element_type=jnp.float32)
        * score_scale
    )
    gen_rows = jnp.arange(GEN, dtype=jnp.int32)
    cache_live = (group_origin == me)[:, :, None, None] & (gen_rows < my_gen)[None, None, None, :]
    cache_top = jnp.max(jnp.where(cache_live, cache_scores, MASKED), axis=3)

    own_beam = me
    own_queries = lax.dynamic_index_in_dim(queries, own_beam, axis=1, keepdims=False)
    new_src = jnp.stack(
        [jnp.stack([anc[(t, s)][own_beam] if t <= s else own_beam for t in range(steps)]) for s in range(steps)]
    )
    step_ids = jnp.arange(steps, dtype=jnp.int32)
    new_keys_here = key_new[step_ids[None, :], new_src].reshape(steps, steps, heads_here, HEAD_DIM)
    new_values_here = value_new[step_ids[None, :], new_src].reshape(steps, steps, heads_here, HEAD_DIM)
    new_scores = (
        jnp.einsum("shd,sthd->sht", own_queries, new_keys_here, preferred_element_type=jnp.float32)
        * score_scale
    )
    new_live = (step_ids[None, :] <= step_ids[:, None])[:, None, :]
    new_top = jnp.max(jnp.where(new_live, new_scores, MASKED), axis=2)

    local_top = prompt_top
    group_top = jnp.maximum(
        lax.dynamic_slice_in_dim(local_top, first_beam, BEAMS, axis=1), cache_top
    )
    local_top = lax.dynamic_update_slice_in_dim(local_top, group_top, first_beam, axis=1)
    own_top = jnp.maximum(lax.dynamic_index_in_dim(local_top, own_beam, axis=1, keepdims=True), new_top[:, None])
    local_top = lax.dynamic_update_slice_in_dim(local_top, own_top, own_beam, axis=1)
    top = nested(lax.pmax, local_top)

    prompt_weights = jnp.where(
        prompt_live, jnp.exp(prompt_scores - top[:, :, :, None]), 0.0
    ).astype(jnp.bfloat16)
    weighted = jnp.einsum(
        "rht,thd->rhd",
        prompt_weights.reshape(rows, heads_here, -1),
        page_values,
        preferred_element_type=jnp.float32,
    ).reshape(steps, batch, heads_here, HEAD_DIM)
    totals = jnp.sum(prompt_weights.astype(jnp.float32), axis=3)

    group_top_all = lax.dynamic_slice_in_dim(top, first_beam, BEAMS, axis=1)
    cache_weights = jnp.where(
        cache_live, jnp.exp(cache_scores - group_top_all[:, :, :, None]), 0.0
    ).astype(jnp.bfloat16)
    cache_weighted = jnp.einsum(
        "sbhj,jhd->sbhd", cache_weights, own_values, preferred_element_type=jnp.float32
    )
    cache_totals = jnp.sum(cache_weights.astype(jnp.float32), axis=3)

    own_top_all = lax.dynamic_index_in_dim(top, own_beam, axis=1, keepdims=False)
    new_weights = jnp.where(
        new_live, jnp.exp(new_scores - own_top_all[:, :, None]), 0.0
    ).astype(jnp.bfloat16)
    new_weighted = jnp.einsum(
        "sht,sthd->shd", new_weights, new_values_here, preferred_element_type=jnp.float32
    )
    new_totals = jnp.sum(new_weights.astype(jnp.float32), axis=2)

    group_weighted = lax.dynamic_slice_in_dim(weighted, first_beam, BEAMS, axis=1) + cache_weighted
    weighted = lax.dynamic_update_slice_in_dim(weighted, group_weighted, first_beam, axis=1)
    group_totals = lax.dynamic_slice_in_dim(totals, first_beam, BEAMS, axis=1) + cache_totals
    totals = lax.dynamic_update_slice_in_dim(totals, group_totals, first_beam, axis=1)
    own_weighted = lax.dynamic_index_in_dim(weighted, own_beam, axis=1, keepdims=True) + new_weighted[:, None]
    weighted = lax.dynamic_update_slice_in_dim(weighted, own_weighted, own_beam, axis=1)
    own_totals = lax.dynamic_index_in_dim(totals, own_beam, axis=1, keepdims=True) + new_totals[:, None]
    totals = lax.dynamic_update_slice_in_dim(totals, own_totals, own_beam, axis=1)

    lanes = 128
    packed = jnp.concatenate(
        [
            weighted.reshape(rows, feat_here),
            jnp.pad(totals.reshape(rows, heads_here), ((0, 0), (0, lanes - heads_here))),
        ],
        axis=1,
    )
    packed = nested(lax.psum, packed)
    weighted = packed[:, :feat_here].reshape(rows, heads_here, HEAD_DIM)
    totals = packed[:, feat_here : feat_here + heads_here]
    attention = (weighted / totals[:, :, None]).reshape(rows, feat_here).astype(jnp.bfloat16)
    head_terms = jnp.dot(attention, w_out, preferred_element_type=jnp.float32)
    head_total = lax.psum(head_terms, "head")
    hidden = (head_total + b_out.astype(jnp.float32)[None, :]).astype(jnp.bfloat16)
    hidden = hidden.reshape(steps, batch, -1)

    final_origin = origin[steps - 1]
    pick = lax.dynamic_slice_in_dim(final_origin, first_beam, BEAMS) - first_beam
    my_final_src = [anc[(t, steps - 1)][own_beam] for t in range(steps)]
    write_rows = my_gen + step_ids

    def reorder(cache, fresh):
        chunks = cache[0].reshape(BEAMS, GEN // BEAMS, feat_here)
        spread = lax.all_to_all(chunks, GROUP, 0, 0, tiled=True)
        picked = jnp.take(spread, pick, axis=0)
        back = lax.all_to_all(picked, GROUP, 0, 0, tiled=True).reshape(GEN, feat_here)
        new_rows = jnp.stack([fresh[t, my_final_src[t]] for t in range(steps)])
        hit = gen_rows[:, None] == write_rows[None, :]
        chosen = jnp.argmax(hit, axis=1)
        out = jnp.where(jnp.any(hit, axis=1)[:, None], jnp.take(new_rows, chosen, axis=0), back)
        return out[None]

    final_keys = reorder(suffix_keys, key_new)
    final_values = reorder(suffix_values, value_new)
    return hidden, final_keys, final_values


def solution(mesh):
    heads = mesh.shape["head"]
    blocks = mesh.shape["blk"]
    cores = 2
    group_chips = BEAMS // cores
    devices = np.asarray(mesh.devices).reshape(heads, blocks // BEAMS, group_chips, cores)
    fine = Mesh(devices, ("head",) + BLK_PARTS)
    blk = BLK_PARTS
    in_specs = (
        P(None, None, blk),
        P(blk),
        P(blk),
        P(blk, "head"),
        P(blk, "head"),
        P(blk, "head"),
        P("head"),
        P("head"),
        P("head"),
        P("head", blk),
        P(blk),
        P(blk, None, "head"),
        P(blk, None, "head"),
        P(blk, None, "head"),
        P(blk, None, "head"),
        P(),
        P(),
        P(),
        P(),
    )
    out_specs = (P(None, None, blk), P(blk, None, "head"), P(blk, None, "head"))
    return jax.shard_map(body, mesh=fine, in_specs=in_specs, out_specs=out_specs, check_vma=False)
```

```python
import math

import jax
import jax.numpy as jnp
import numpy as np
from jax import lax
from jax.sharding import Mesh
from jax.sharding import PartitionSpec as P

D = 7168
HEAD_DIM = 128
BEAMS = 8
PAGE = 16
GEN = 256
STEPS = 4

MASKED = -1e30
NORM_EPSILON = 1e-05

BLK_PARTS = ("z", "x", "core")
GROUP = ("x", "core")


def nested(reduce, value):
    for axis in reversed(BLK_PARTS):
        value = reduce(value, axis)
    return value


def halving_stages(axes):
    stages = []
    for axis in axes:
        size = lax.axis_size(axis)
        bit = 1
        while bit < size:
            stages.append((axis, bit))
            bit *= 2
    return stages


def exchange(value, axis, bit):
    size = lax.axis_size(axis)
    return lax.ppermute(value, axis, [(i, i ^ bit) for i in range(size)])


def upper_half(axis, bit):
    return (lax.axis_index(axis) // bit) % 2 == 1


def scatter_sum(value, stages, combine=jnp.add):
    for axis, bit in stages:
        half = value.shape[0] // 2
        low, high = value[:half], value[half:]
        upper = upper_half(axis, bit)
        keep = jnp.where(upper, high, low)
        send = jnp.where(upper, low, high)
        value = combine(keep, exchange(send, axis, bit))
    return value


def gather_rows(value, stages):
    for axis, bit in reversed(stages):
        other = exchange(value, axis, bit)
        upper = upper_half(axis, bit)
        value = jnp.where(upper, jnp.concatenate([other, value]), jnp.concatenate([value, other]))
    return value


def blk_index():
    index = lax.axis_index("z")
    for axis in BLK_PARTS[1:]:
        index = index * lax.axis_size(axis) + lax.axis_index(axis)
    return index


def body(
    inputs,
    ln_gain,
    ln_bias,
    w_query,
    w_key,
    w_value,
    b_query,
    b_key,
    b_value,
    w_out,
    b_out,
    prefix_keys,
    prefix_values,
    suffix_keys,
    suffix_values,
    page_table,
    prompt_len,
    gen_len,
    parents,
):
    blocks = 1
    for axis in BLK_PARTS:
        blocks *= lax.axis_size(axis)
    me = blk_index()
    steps = inputs.shape[0]
    batch = inputs.shape[1]
    feat_here = w_query.shape[1]
    heads_here = feat_here // HEAD_DIM
    pages_here = prefix_keys.shape[0]
    requests = page_table.shape[0]
    slot_count = page_table.shape[1]
    rows = steps * batch
    score_scale = 1.0 / math.sqrt(HEAD_DIM)
    my_request = me // BEAMS
    first_beam = my_request * BEAMS
    my_gen = gen_len[my_request]

    beam_ids = jnp.arange(batch, dtype=jnp.int32)
    anc = {}
    for s in range(steps):
        x = beam_ids
        anc[(s, s)] = x
        for t in range(s, -1, -1):
            x = jnp.take(parents[t], x)
            anc[(t - 1, s)] = x
    origin = jnp.stack([anc[(-1, s)] for s in range(steps)])

    rows_in = inputs.astype(jnp.float32).reshape(rows, -1)
    stats = jnp.stack([jnp.sum(rows_in, axis=1), jnp.sum(rows_in * rows_in, axis=1)], axis=1)
    stats = nested(lax.psum, stats)
    row_mean = stats[:, 0] / D
    variance = stats[:, 1] / D - row_mean * row_mean
    normed = (
        (rows_in - row_mean[:, None]) * lax.rsqrt(variance + NORM_EPSILON)[:, None]
        * ln_gain.astype(jnp.float32)
        + ln_bias.astype(jnp.float32)
    ).astype(jnp.bfloat16)
    weights_all = jnp.concatenate([w_query, w_key, w_value], axis=1)
    bias_all = jnp.concatenate([b_query, b_key, b_value]).astype(jnp.float32)
    partial = jnp.dot(normed, weights_all, preferred_element_type=jnp.float32)
    blk_stages = halving_stages(("core",) + GROUP[:1] + ("z",))
    projected = (scatter_sum(partial, blk_stages) + bias_all[None, :]).astype(jnp.bfloat16)
    projected = gather_rows(projected, blk_stages)
    queries = projected[:, :feat_here].reshape(steps, batch, heads_here, HEAD_DIM)
    key_new = projected[:, feat_here : 2 * feat_here].reshape(steps, batch, feat_here)
    value_new = projected[:, 2 * feat_here :].reshape(steps, batch, feat_here)

    beam_request = beam_ids // BEAMS
    beam_prompt = jnp.take(prompt_len, beam_request)
    page_ids = me * pages_here + jnp.arange(pages_here, dtype=jnp.int32)
    slot_ids = jnp.arange(slot_count, dtype=jnp.int32)
    slot_live = slot_ids[None, :] * PAGE < prompt_len[:, None]
    page_match = (
        (page_table[:, :, None] == page_ids[None, None, :]) & slot_live[:, :, None]
    ).astype(jnp.int32)
    request_ids = jnp.arange(requests, dtype=jnp.int32)
    page_request = jnp.sum(page_match * request_ids[:, None, None], axis=(0, 1))
    page_slot = jnp.sum(page_match * slot_ids[None, :, None], axis=(0, 1))
    page_used = jnp.sum(page_match, axis=(0, 1)) > 0
    token_pos = (page_slot[:, None] * PAGE + jnp.arange(PAGE, dtype=jnp.int32)[None, :]).reshape(-1)
    token_request = jnp.repeat(page_request, PAGE)
    token_used = jnp.repeat(page_used, PAGE)
    prefix_live = (
        token_used[None, :]
        & (token_request[None, :] == beam_request[:, None])
        & (token_pos[None, :] < beam_prompt[:, None])
    )
    page_keys = prefix_keys.reshape(pages_here * PAGE, heads_here, HEAD_DIM)
    page_values = prefix_values.reshape(pages_here * PAGE, heads_here, HEAD_DIM)
    flat_queries = queries.reshape(rows, heads_here, HEAD_DIM)
    prompt_scores = (
        jnp.einsum("rhd,thd->rht", flat_queries, page_keys, preferred_element_type=jnp.float32)
        * score_scale
    ).reshape(steps, batch, heads_here, -1)
    prompt_live = prefix_live[None, :, None, :]
    prompt_top = jnp.max(jnp.where(prompt_live, prompt_scores, MASKED), axis=3)

    group_queries = lax.dynamic_slice_in_dim(queries, first_beam, BEAMS, axis=1)
    group_origin = lax.dynamic_slice_in_dim(origin, first_beam, BEAMS, axis=1)
    own_keys = suffix_keys[0].reshape(GEN, heads_here, HEAD_DIM)
    own_values = suffix_values[0].reshape(GEN, heads_here, HEAD_DIM)
    cache_scores = (
        jnp.einsum("sbhd,jhd->sbhj", group_queries, own_keys, preferred_element_type=jnp.float32)
        * score_scale
    )
    gen_rows = jnp.arange(GEN, dtype=jnp.int32)
    cache_live = (group_origin == me)[:, :, None, None] & (gen_rows < my_gen)[None, None, None, :]
    cache_top = jnp.max(jnp.where(cache_live, cache_scores, MASKED), axis=3)

    own_beam = me
    own_queries = lax.dynamic_index_in_dim(queries, own_beam, axis=1, keepdims=False)
    new_src = jnp.stack(
        [jnp.stack([anc[(t, s)][own_beam] if t <= s else own_beam for t in range(steps)]) for s in range(steps)]
    )
    step_ids = jnp.arange(steps, dtype=jnp.int32)
    new_keys_here = key_new[step_ids[None, :], new_src].reshape(steps, steps, heads_here, HEAD_DIM)
    new_values_here = value_new[step_ids[None, :], new_src].reshape(steps, steps, heads_here, HEAD_DIM)
    new_scores = (
        jnp.einsum("shd,sthd->sht", own_queries, new_keys_here, preferred_element_type=jnp.float32)
        * score_scale
    )
    new_live = (step_ids[None, :] <= step_ids[:, None])[:, None, :]
    new_top = jnp.max(jnp.where(new_live, new_scores, MASKED), axis=2)

    local_top = prompt_top
    group_top = jnp.maximum(
        lax.dynamic_slice_in_dim(local_top, first_beam, BEAMS, axis=1), cache_top
    )
    local_top = lax.dynamic_update_slice_in_dim(local_top, group_top, first_beam, axis=1)
    own_top = jnp.maximum(lax.dynamic_index_in_dim(local_top, own_beam, axis=1, keepdims=True), new_top[:, None])
    local_top = lax.dynamic_update_slice_in_dim(local_top, own_top, own_beam, axis=1)
    top = nested(lax.pmax, local_top)

    prompt_weights = jnp.where(
        prompt_live, jnp.exp(prompt_scores - top[:, :, :, None]), 0.0
    ).astype(jnp.bfloat16)
    weighted = jnp.einsum(
        "rht,thd->rhd",
        prompt_weights.reshape(rows, heads_here, -1),
        page_values,
        preferred_element_type=jnp.float32,
    ).reshape(steps, batch, heads_here, HEAD_DIM)
    totals = jnp.sum(prompt_weights.astype(jnp.float32), axis=3)

    group_top_all = lax.dynamic_slice_in_dim(top, first_beam, BEAMS, axis=1)
    cache_weights = jnp.where(
        cache_live, jnp.exp(cache_scores - group_top_all[:, :, :, None]), 0.0
    ).astype(jnp.bfloat16)
    cache_weighted = jnp.einsum(
        "sbhj,jhd->sbhd", cache_weights, own_values, preferred_element_type=jnp.float32
    )
    cache_totals = jnp.sum(cache_weights.astype(jnp.float32), axis=3)

    own_top_all = lax.dynamic_index_in_dim(top, own_beam, axis=1, keepdims=False)
    new_weights = jnp.where(
        new_live, jnp.exp(new_scores - own_top_all[:, :, None]), 0.0
    ).astype(jnp.bfloat16)
    new_weighted = jnp.einsum(
        "sht,sthd->shd", new_weights, new_values_here, preferred_element_type=jnp.float32
    )
    new_totals = jnp.sum(new_weights.astype(jnp.float32), axis=2)

    group_weighted = lax.dynamic_slice_in_dim(weighted, first_beam, BEAMS, axis=1) + cache_weighted
    weighted = lax.dynamic_update_slice_in_dim(weighted, group_weighted, first_beam, axis=1)
    group_totals = lax.dynamic_slice_in_dim(totals, first_beam, BEAMS, axis=1) + cache_totals
    totals = lax.dynamic_update_slice_in_dim(totals, group_totals, first_beam, axis=1)
    own_weighted = lax.dynamic_index_in_dim(weighted, own_beam, axis=1, keepdims=True) + new_weighted[:, None]
    weighted = lax.dynamic_update_slice_in_dim(weighted, own_weighted, own_beam, axis=1)
    own_totals = lax.dynamic_index_in_dim(totals, own_beam, axis=1, keepdims=True) + new_totals[:, None]
    totals = lax.dynamic_update_slice_in_dim(totals, own_totals, own_beam, axis=1)

    lanes = 128
    packed = jnp.concatenate(
        [
            weighted.reshape(rows, feat_here),
            jnp.pad(totals.reshape(rows, heads_here), ((0, 0), (0, lanes - heads_here))),
        ],
        axis=1,
    )
    packed = scatter_sum(packed, blk_stages)
    part_rows = packed.shape[0]
    weighted = packed[:, :feat_here].reshape(part_rows, heads_here, HEAD_DIM)
    totals = packed[:, feat_here : feat_here + heads_here]
    attention = (weighted / totals[:, :, None]).reshape(part_rows, feat_here).astype(jnp.bfloat16)
    attention = gather_rows(attention, blk_stages)
    head_terms = jnp.dot(attention, w_out, preferred_element_type=jnp.float32)
    head_stages = halving_stages(("head",))
    head_total = gather_rows(scatter_sum(head_terms, head_stages), head_stages)
    hidden = (head_total + b_out.astype(jnp.float32)[None, :]).astype(jnp.bfloat16)
    hidden = hidden.reshape(steps, batch, -1)

    final_origin = origin[steps - 1]
    pick = lax.dynamic_slice_in_dim(final_origin, first_beam, BEAMS) - first_beam
    my_final_src = [anc[(t, steps - 1)][own_beam] for t in range(steps)]
    write_rows = my_gen + step_ids

    def reorder(cache, fresh):
        chunks = cache[0].reshape(BEAMS, GEN // BEAMS, feat_here)
        spread = lax.all_to_all(chunks, GROUP, 0, 0, tiled=True)
        picked = jnp.take(spread, pick, axis=0)
        back = lax.all_to_all(picked, GROUP, 0, 0, tiled=True).reshape(GEN, feat_here)
        new_rows = jnp.stack([fresh[t, my_final_src[t]] for t in range(steps)])
        hit = gen_rows[:, None] == write_rows[None, :]
        chosen = jnp.argmax(hit, axis=1)
        out = jnp.where(jnp.any(hit, axis=1)[:, None], jnp.take(new_rows, chosen, axis=0), back)
        return out[None]

    final_keys = reorder(suffix_keys, key_new)
    final_values = reorder(suffix_values, value_new)
    return hidden, final_keys, final_values


def solution(mesh):
    heads = mesh.shape["head"]
    blocks = mesh.shape["blk"]
    cores = 2
    group_chips = BEAMS // cores
    devices = np.asarray(mesh.devices).reshape(heads, blocks // BEAMS, group_chips, cores)
    fine = Mesh(devices, ("head",) + BLK_PARTS)
    blk = BLK_PARTS
    in_specs = (
        P(None, None, blk),
        P(blk),
        P(blk),
        P(blk, "head"),
        P(blk, "head"),
        P(blk, "head"),
        P("head"),
        P("head"),
        P("head"),
        P("head", blk),
        P(blk),
        P(blk, None, "head"),
        P(blk, None, "head"),
        P(blk, None, "head"),
        P(blk, None, "head"),
        P(),
        P(),
        P(),
        P(),
    )
    out_specs = (P(None, None, blk), P(blk, None, "head"), P(blk, None, "head"))
    return jax.shard_map(body, mesh=fine, in_specs=in_specs, out_specs=out_specs, check_vma=False)
```

```python
import math

import jax
import jax.numpy as jnp
import numpy as np
from jax import lax
from jax.sharding import Mesh
from jax.sharding import PartitionSpec as P

D = 7168
HEAD_DIM = 128
BEAMS = 8
PAGE = 16
GEN = 256
STEPS = 4

MASKED = -1e30
NORM_EPSILON = 1e-05

BLK_PARTS = ("z", "x", "core")
GROUP = ("x", "core")


def nested(reduce, value):
    for axis in reversed(BLK_PARTS):
        value = reduce(value, axis)
    return value


def axes_size(axes):
    size = 1
    for axis in axes:
        size *= lax.axis_size(axis)
    return size


def scatter_sum(value, axes):
    n = axes_size(axes)
    got = lax.all_to_all(value, axes, 0, 0, tiled=True)
    return jnp.sum(got.reshape((n, value.shape[0] // n) + value.shape[1:]), axis=0)


def gather_rows(value, axes):
    n = axes_size(axes)
    copies = jnp.broadcast_to(value[None], (n,) + value.shape).reshape((n * value.shape[0],) + value.shape[1:])
    return lax.all_to_all(copies, axes, 0, 0, tiled=True)


def all_combine(value, axes, combine):
    n = axes_size(axes)
    got = gather_rows(value[None], axes)
    return combine(got.reshape((n,) + value.shape), axis=0)


def blk_index():
    index = lax.axis_index("z")
    for axis in BLK_PARTS[1:]:
        index = index * lax.axis_size(axis) + lax.axis_index(axis)
    return index


def body(
    inputs,
    ln_gain,
    ln_bias,
    w_query,
    w_key,
    w_value,
    b_query,
    b_key,
    b_value,
    w_out,
    b_out,
    prefix_keys,
    prefix_values,
    suffix_keys,
    suffix_values,
    page_table,
    prompt_len,
    gen_len,
    parents,
):
    blocks = 1
    for axis in BLK_PARTS:
        blocks *= lax.axis_size(axis)
    me = blk_index()
    steps = inputs.shape[0]
    batch = inputs.shape[1]
    feat_here = w_query.shape[1]
    heads_here = feat_here // HEAD_DIM
    pages_here = prefix_keys.shape[0]
    requests = page_table.shape[0]
    slot_count = page_table.shape[1]
    rows = steps * batch
    score_scale = 1.0 / math.sqrt(HEAD_DIM)
    my_request = me // BEAMS
    first_beam = my_request * BEAMS
    my_gen = gen_len[my_request]

    beam_ids = jnp.arange(batch, dtype=jnp.int32)
    anc = {}
    for s in range(steps):
        x = beam_ids
        anc[(s, s)] = x
        for t in range(s, -1, -1):
            x = jnp.take(parents[t], x)
            anc[(t - 1, s)] = x
    origin = jnp.stack([anc[(-1, s)] for s in range(steps)])

    rows_in = inputs.astype(jnp.float32).reshape(rows, -1)
    stats = jnp.stack([jnp.sum(rows_in, axis=1), jnp.sum(rows_in * rows_in, axis=1)], axis=1)
    stats = all_combine(stats, BLK_PARTS, jnp.sum)
    row_mean = stats[:, 0] / D
    variance = stats[:, 1] / D - row_mean * row_mean
    normed = (
        (rows_in - row_mean[:, None]) * lax.rsqrt(variance + NORM_EPSILON)[:, None]
        * ln_gain.astype(jnp.float32)
        + ln_bias.astype(jnp.float32)
    ).astype(jnp.bfloat16)
    weights_all = jnp.concatenate([w_query, w_key, w_value], axis=1)
    bias_all = jnp.concatenate([b_query, b_key, b_value]).astype(jnp.float32)
    partial = jnp.dot(normed, weights_all, preferred_element_type=jnp.float32)
    blk_stages = BLK_PARTS
    projected = (scatter_sum(partial, blk_stages) + bias_all[None, :]).astype(jnp.bfloat16)
    projected = gather_rows(projected, blk_stages)
    queries = projected[:, :feat_here].reshape(steps, batch, heads_here, HEAD_DIM)
    key_new = projected[:, feat_here : 2 * feat_here].reshape(steps, batch, feat_here)
    value_new = projected[:, 2 * feat_here :].reshape(steps, batch, feat_here)

    beam_request = beam_ids // BEAMS
    beam_prompt = jnp.take(prompt_len, beam_request)
    page_ids = me * pages_here + jnp.arange(pages_here, dtype=jnp.int32)
    slot_ids = jnp.arange(slot_count, dtype=jnp.int32)
    slot_live = slot_ids[None, :] * PAGE < prompt_len[:, None]
    page_match = (
        (page_table[:, :, None] == page_ids[None, None, :]) & slot_live[:, :, None]
    ).astype(jnp.int32)
    request_ids = jnp.arange(requests, dtype=jnp.int32)
    page_request = jnp.sum(page_match * request_ids[:, None, None], axis=(0, 1))
    page_slot = jnp.sum(page_match * slot_ids[None, :, None], axis=(0, 1))
    page_used = jnp.sum(page_match, axis=(0, 1)) > 0
    token_pos = (page_slot[:, None] * PAGE + jnp.arange(PAGE, dtype=jnp.int32)[None, :]).reshape(-1)
    token_request = jnp.repeat(page_request, PAGE)
    token_used = jnp.repeat(page_used, PAGE)
    prefix_live = (
        token_used[None, :]
        & (token_request[None, :] == beam_request[:, None])
        & (token_pos[None, :] < beam_prompt[:, None])
    )
    page_keys = prefix_keys.reshape(pages_here * PAGE, heads_here, HEAD_DIM)
    page_values = prefix_values.reshape(pages_here * PAGE, heads_here, HEAD_DIM)
    flat_queries = queries.reshape(rows, heads_here, HEAD_DIM)
    prompt_scores = (
        jnp.einsum("rhd,thd->rht", flat_queries, page_keys, preferred_element_type=jnp.float32)
        * score_scale
    ).reshape(steps, batch, heads_here, -1)
    prompt_live = prefix_live[None, :, None, :]
    prompt_top = jnp.max(jnp.where(prompt_live, prompt_scores, MASKED), axis=3)

    group_queries = lax.dynamic_slice_in_dim(queries, first_beam, BEAMS, axis=1)
    group_origin = lax.dynamic_slice_in_dim(origin, first_beam, BEAMS, axis=1)
    own_keys = suffix_keys[0].reshape(GEN, heads_here, HEAD_DIM)
    own_values = suffix_values[0].reshape(GEN, heads_here, HEAD_DIM)
    cache_scores = (
        jnp.einsum("sbhd,jhd->sbhj", group_queries, own_keys, preferred_element_type=jnp.float32)
        * score_scale
    )
    gen_rows = jnp.arange(GEN, dtype=jnp.int32)
    cache_live = (group_origin == me)[:, :, None, None] & (gen_rows < my_gen)[None, None, None, :]
    cache_top = jnp.max(jnp.where(cache_live, cache_scores, MASKED), axis=3)

    own_beam = me
    own_queries = lax.dynamic_index_in_dim(queries, own_beam, axis=1, keepdims=False)
    new_src = jnp.stack(
        [jnp.stack([anc[(t, s)][own_beam] if t <= s else own_beam for t in range(steps)]) for s in range(steps)]
    )
    step_ids = jnp.arange(steps, dtype=jnp.int32)
    new_keys_here = key_new[step_ids[None, :], new_src].reshape(steps, steps, heads_here, HEAD_DIM)
    new_values_here = value_new[step_ids[None, :], new_src].reshape(steps, steps, heads_here, HEAD_DIM)
    new_scores = (
        jnp.einsum("shd,sthd->sht", own_queries, new_keys_here, preferred_element_type=jnp.float32)
        * score_scale
    )
    new_live = (step_ids[None, :] <= step_ids[:, None])[:, None, :]
    new_top = jnp.max(jnp.where(new_live, new_scores, MASKED), axis=2)

    local_top = prompt_top
    group_top = jnp.maximum(
        lax.dynamic_slice_in_dim(local_top, first_beam, BEAMS, axis=1), cache_top
    )
    local_top = lax.dynamic_update_slice_in_dim(local_top, group_top, first_beam, axis=1)
    own_top = jnp.maximum(lax.dynamic_index_in_dim(local_top, own_beam, axis=1, keepdims=True), new_top[:, None])
    local_top = lax.dynamic_update_slice_in_dim(local_top, own_top, own_beam, axis=1)
    top = all_combine(local_top, BLK_PARTS, jnp.max)

    prompt_weights = jnp.where(
        prompt_live, jnp.exp(prompt_scores - top[:, :, :, None]), 0.0
    ).astype(jnp.bfloat16)
    weighted = jnp.einsum(
        "rht,thd->rhd",
        prompt_weights.reshape(rows, heads_here, -1),
        page_values,
        preferred_element_type=jnp.float32,
    ).reshape(steps, batch, heads_here, HEAD_DIM)
    totals = jnp.sum(prompt_weights.astype(jnp.float32), axis=3)

    group_top_all = lax.dynamic_slice_in_dim(top, first_beam, BEAMS, axis=1)
    cache_weights = jnp.where(
        cache_live, jnp.exp(cache_scores - group_top_all[:, :, :, None]), 0.0
    ).astype(jnp.bfloat16)
    cache_weighted = jnp.einsum(
        "sbhj,jhd->sbhd", cache_weights, own_values, preferred_element_type=jnp.float32
    )
    cache_totals = jnp.sum(cache_weights.astype(jnp.float32), axis=3)

    own_top_all = lax.dynamic_index_in_dim(top, own_beam, axis=1, keepdims=False)
    new_weights = jnp.where(
        new_live, jnp.exp(new_scores - own_top_all[:, :, None]), 0.0
    ).astype(jnp.bfloat16)
    new_weighted = jnp.einsum(
        "sht,sthd->shd", new_weights, new_values_here, preferred_element_type=jnp.float32
    )
    new_totals = jnp.sum(new_weights.astype(jnp.float32), axis=2)

    group_weighted = lax.dynamic_slice_in_dim(weighted, first_beam, BEAMS, axis=1) + cache_weighted
    weighted = lax.dynamic_update_slice_in_dim(weighted, group_weighted, first_beam, axis=1)
    group_totals = lax.dynamic_slice_in_dim(totals, first_beam, BEAMS, axis=1) + cache_totals
    totals = lax.dynamic_update_slice_in_dim(totals, group_totals, first_beam, axis=1)
    own_weighted = lax.dynamic_index_in_dim(weighted, own_beam, axis=1, keepdims=True) + new_weighted[:, None]
    weighted = lax.dynamic_update_slice_in_dim(weighted, own_weighted, own_beam, axis=1)
    own_totals = lax.dynamic_index_in_dim(totals, own_beam, axis=1, keepdims=True) + new_totals[:, None]
    totals = lax.dynamic_update_slice_in_dim(totals, own_totals, own_beam, axis=1)

    lanes = 128
    packed = jnp.concatenate(
        [
            weighted.reshape(rows, feat_here),
            jnp.pad(totals.reshape(rows, heads_here), ((0, 0), (0, lanes - heads_here))),
        ],
        axis=1,
    )
    packed = scatter_sum(packed, blk_stages)
    part_rows = packed.shape[0]
    weighted = packed[:, :feat_here].reshape(part_rows, heads_here, HEAD_DIM)
    totals = packed[:, feat_here : feat_here + heads_here]
    attention = (weighted / totals[:, :, None]).reshape(part_rows, feat_here).astype(jnp.bfloat16)
    attention = gather_rows(attention, blk_stages)
    head_terms = jnp.dot(attention, w_out, preferred_element_type=jnp.float32)
    head_stages = ("head",)
    head_total = gather_rows(scatter_sum(head_terms, head_stages), head_stages)
    hidden = (head_total + b_out.astype(jnp.float32)[None, :]).astype(jnp.bfloat16)
    hidden = hidden.reshape(steps, batch, -1)

    final_origin = origin[steps - 1]
    pick = lax.dynamic_slice_in_dim(final_origin, first_beam, BEAMS) - first_beam
    my_final_src = [anc[(t, steps - 1)][own_beam] for t in range(steps)]
    write_rows = my_gen + step_ids

    def reorder(cache, fresh):
        chunks = cache[0].reshape(BEAMS, GEN // BEAMS, feat_here)
        spread = lax.all_to_all(chunks, GROUP, 0, 0, tiled=True)
        picked = jnp.take(spread, pick, axis=0)
        back = lax.all_to_all(picked, GROUP, 0, 0, tiled=True).reshape(GEN, feat_here)
        new_rows = jnp.stack([fresh[t, my_final_src[t]] for t in range(steps)])
        hit = gen_rows[:, None] == write_rows[None, :]
        chosen = jnp.argmax(hit, axis=1)
        out = jnp.where(jnp.any(hit, axis=1)[:, None], jnp.take(new_rows, chosen, axis=0), back)
        return out[None]

    final_keys = reorder(suffix_keys, key_new)
    final_values = reorder(suffix_values, value_new)
    return hidden, final_keys, final_values


def solution(mesh):
    heads = mesh.shape["head"]
    blocks = mesh.shape["blk"]
    cores = 2
    group_chips = BEAMS // cores
    devices = np.asarray(mesh.devices).reshape(heads, blocks // BEAMS, group_chips, cores)
    fine = Mesh(devices, ("head",) + BLK_PARTS)
    blk = BLK_PARTS
    in_specs = (
        P(None, None, blk),
        P(blk),
        P(blk),
        P(blk, "head"),
        P(blk, "head"),
        P(blk, "head"),
        P("head"),
        P("head"),
        P("head"),
        P("head", blk),
        P(blk),
        P(blk, None, "head"),
        P(blk, None, "head"),
        P(blk, None, "head"),
        P(blk, None, "head"),
        P(),
        P(),
        P(),
        P(),
    )
    out_specs = (P(None, None, blk), P(blk, None, "head"), P(blk, None, "head"))
    return jax.shard_map(body, mesh=fine, in_specs=in_specs, out_specs=out_specs, check_vma=False)
```

```python
import math

import jax
import jax.numpy as jnp
import numpy as np
from jax import lax
from jax.sharding import Mesh
from jax.sharding import PartitionSpec as P

D = 7168
HEAD_DIM = 128
BEAMS = 8
PAGE = 16
GEN = 256
STEPS = 4

MASKED = -1e30
NORM_EPSILON = 1e-05

BLK_PARTS = ("z", "x", "core")
GROUP = ("x", "core")


def nested(reduce, value):
    for axis in reversed(BLK_PARTS):
        value = reduce(value, axis)
    return value


def axes_size(axes):
    size = 1
    for axis in axes:
        size *= lax.axis_size(axis)
    return size


def scatter_sum(value, axes):
    n = axes_size(axes)
    got = lax.all_to_all(value, axes, 0, 0, tiled=True)
    return jnp.sum(got.reshape((n, value.shape[0] // n) + value.shape[1:]), axis=0)


def gather_rows(value, axes):
    n = axes_size(axes)
    copies = jnp.broadcast_to(value[None], (n,) + value.shape).reshape((n * value.shape[0],) + value.shape[1:])
    return lax.all_to_all(copies, axes, 0, 0, tiled=True)


def all_combine(value, axes, combine):
    n = axes_size(axes)
    got = gather_rows(value[None], axes)
    return combine(got.reshape((n,) + value.shape), axis=0)


def blk_index():
    index = lax.axis_index("z")
    for axis in BLK_PARTS[1:]:
        index = index * lax.axis_size(axis) + lax.axis_index(axis)
    return index


def body(
    inputs,
    ln_gain,
    ln_bias,
    w_query,
    w_key,
    w_value,
    b_query,
    b_key,
    b_value,
    w_out,
    b_out,
    prefix_keys,
    prefix_values,
    suffix_keys,
    suffix_values,
    page_table,
    prompt_len,
    gen_len,
    parents,
):
    me = blk_index()
    group = axes_size(GROUP)
    member = lax.axis_index("x") * lax.axis_size("core") + lax.axis_index("core")
    steps = inputs.shape[0]
    batch = inputs.shape[1]
    feat_local = inputs.shape[2]
    feat_here = w_query.shape[1]
    heads_here = feat_here // HEAD_DIM
    pages_here = prefix_keys.shape[0]
    requests = page_table.shape[0]
    slot_count = page_table.shape[1]
    rows = steps * batch
    score_scale = 1.0 / math.sqrt(HEAD_DIM)
    my_request = me // BEAMS
    first_beam = my_request * BEAMS
    my_gen = gen_len[my_request]
    cols_all = 3 * feat_here
    col_block = cols_all // group
    chunk_rows = GEN // group

    beam_ids = jnp.arange(batch, dtype=jnp.int32)
    anc = {}
    for s in range(steps):
        x = beam_ids
        anc[(s, s)] = x
        for t in range(s, -1, -1):
            x = jnp.take(parents[t], x)
            anc[(t - 1, s)] = x
    origin = jnp.stack([anc[(-1, s)] for s in range(steps)])

    rows_local = inputs.astype(jnp.float32).reshape(rows, feat_local)
    stats = jnp.stack([jnp.sum(rows_local, axis=1), jnp.sum(rows_local * rows_local, axis=1)], axis=1)
    stats = all_combine(stats, BLK_PARTS, jnp.sum)
    row_mean = stats[:, 0] / D
    variance = stats[:, 1] / D - row_mean * row_mean

    weights_all = jnp.concatenate([w_query, w_key, w_value], axis=1)
    weight_chunks = weights_all.reshape(feat_local, group, col_block).transpose(1, 0, 2).reshape(group, -1)
    row_block = jnp.concatenate(
        [inputs.reshape(-1), ln_gain, ln_bias]
    )
    cache_chunks = jnp.concatenate(
        [suffix_keys[0].reshape(group, -1), suffix_values[0].reshape(group, -1)], axis=1
    )
    sent = jnp.concatenate(
        [weight_chunks, jnp.broadcast_to(row_block[None], (group, row_block.shape[0])), cache_chunks], axis=1
    )
    got = lax.all_to_all(sent, GROUP, 0, 0, tiled=True)
    n_w = feat_local * col_block
    n_in = rows * feat_local
    w_group = got[:, :n_w].reshape(group * feat_local, col_block)
    in_group = got[:, n_w : n_w + n_in].reshape(group, rows, feat_local).transpose(1, 0, 2).reshape(rows, -1)
    gain_group = got[:, n_w + n_in : n_w + n_in + feat_local].reshape(-1)
    shift_group = got[:, n_w + n_in + feat_local : n_w + n_in + 2 * feat_local].reshape(-1)
    spread = got[:, n_w + n_in + 2 * feat_local :].reshape(group, 2, chunk_rows, feat_here)

    normed = (
        (in_group.astype(jnp.float32) - row_mean[:, None]) * lax.rsqrt(variance + NORM_EPSILON)[:, None]
        * gain_group.astype(jnp.float32)
        + shift_group.astype(jnp.float32)
    ).astype(jnp.bfloat16)
    partial = jnp.dot(normed, w_group, preferred_element_type=jnp.float32)
    partial = partial.reshape(steps, requests, BEAMS, col_block).transpose(1, 0, 2, 3)
    summed = jnp.sum(lax.all_to_all(partial, "z", 0, 0, tiled=True).reshape(
        (lax.axis_size("z"), steps, BEAMS, col_block)), axis=0)
    bias_all = jnp.concatenate([b_query, b_key, b_value]).astype(jnp.float32)
    bias_block = lax.dynamic_slice_in_dim(bias_all, member * col_block, col_block)
    mine = (summed + bias_block).astype(jnp.bfloat16)

    final_origin = origin[steps - 1]
    pick = lax.dynamic_slice_in_dim(final_origin, first_beam, BEAMS) - first_beam
    picked = jnp.take(spread, pick, axis=0).reshape(group, -1)

    n_mine = steps * BEAMS * col_block
    sent2 = jnp.concatenate(
        [jnp.broadcast_to(mine.reshape(1, -1), (group, n_mine)), picked], axis=1
    )
    got2 = lax.all_to_all(sent2, GROUP, 0, 0, tiled=True)
    projected = got2[:, :n_mine].reshape(group, steps, BEAMS, col_block).transpose(1, 2, 0, 3).reshape(
        steps, BEAMS, cols_all)
    back = got2[:, n_mine:].reshape(group, 2, chunk_rows, feat_here).transpose(1, 0, 2, 3).reshape(2, GEN, feat_here)
    group_queries = projected[:, :, :feat_here].reshape(steps, BEAMS, heads_here, HEAD_DIM)
    key_new = projected[:, :, feat_here : 2 * feat_here]
    value_new = projected[:, :, 2 * feat_here :]

    q_all = gather_rows(projected[None, :, :, :feat_here], ("z",))
    queries = q_all.transpose(1, 0, 2, 3).reshape(steps, batch, heads_here, HEAD_DIM)

    beam_request = beam_ids // BEAMS
    beam_prompt = jnp.take(prompt_len, beam_request)
    page_ids = me * pages_here + jnp.arange(pages_here, dtype=jnp.int32)
    slot_ids = jnp.arange(slot_count, dtype=jnp.int32)
    slot_live = slot_ids[None, :] * PAGE < prompt_len[:, None]
    page_match = (
        (page_table[:, :, None] == page_ids[None, None, :]) & slot_live[:, :, None]
    ).astype(jnp.int32)
    request_ids = jnp.arange(requests, dtype=jnp.int32)
    page_request = jnp.sum(page_match * request_ids[:, None, None], axis=(0, 1))
    page_slot = jnp.sum(page_match * slot_ids[None, :, None], axis=(0, 1))
    page_used = jnp.sum(page_match, axis=(0, 1)) > 0
    token_pos = (page_slot[:, None] * PAGE + jnp.arange(PAGE, dtype=jnp.int32)[None, :]).reshape(-1)
    token_request = jnp.repeat(page_request, PAGE)
    token_used = jnp.repeat(page_used, PAGE)
    prefix_live = (
        token_used[None, :]
        & (token_request[None, :] == beam_request[:, None])
        & (token_pos[None, :] < beam_prompt[:, None])
    )
    page_keys = prefix_keys.reshape(pages_here * PAGE, heads_here, HEAD_DIM)
    page_values = prefix_values.reshape(pages_here * PAGE, heads_here, HEAD_DIM)
    flat_queries = queries.reshape(rows, heads_here, HEAD_DIM)
    prompt_scores = (
        jnp.einsum("rhd,thd->rht", flat_queries, page_keys, preferred_element_type=jnp.float32)
        * score_scale
    ).reshape(steps, batch, heads_here, -1)
    prompt_live = prefix_live[None, :, None, :]
    prompt_top = jnp.max(jnp.where(prompt_live, prompt_scores, MASKED), axis=3)

    group_origin = lax.dynamic_slice_in_dim(origin, first_beam, BEAMS, axis=1)
    own_keys = suffix_keys[0].reshape(GEN, heads_here, HEAD_DIM)
    own_values = suffix_values[0].reshape(GEN, heads_here, HEAD_DIM)
    cache_scores = (
        jnp.einsum("sbhd,jhd->sbhj", group_queries, own_keys, preferred_element_type=jnp.float32)
        * score_scale
    )
    gen_rows = jnp.arange(GEN, dtype=jnp.int32)
    cache_live = (group_origin == me)[:, :, None, None] & (gen_rows < my_gen)[None, None, None, :]
    cache_top = jnp.max(jnp.where(cache_live, cache_scores, MASKED), axis=3)

    own_beam = me
    own_queries = lax.dynamic_index_in_dim(group_queries, member, axis=1, keepdims=False)
    new_src = jnp.stack(
        [jnp.stack([anc[(t, s)][own_beam] if t <= s else own_beam for t in range(steps)]) for s in range(steps)]
    ) - first_beam
    step_ids = jnp.arange(steps, dtype=jnp.int32)
    new_keys_here = key_new[step_ids[None, :], new_src].reshape(steps, steps, heads_here, HEAD_DIM)
    new_values_here = value_new[step_ids[None, :], new_src].reshape(steps, steps, heads_here, HEAD_DIM)
    new_scores = (
        jnp.einsum("shd,sthd->sht", own_queries, new_keys_here, preferred_element_type=jnp.float32)
        * score_scale
    )
    new_live = (step_ids[None, :] <= step_ids[:, None])[:, None, :]
    new_top = jnp.max(jnp.where(new_live, new_scores, MASKED), axis=2)

    local_top = prompt_top
    group_top = jnp.maximum(
        lax.dynamic_slice_in_dim(local_top, first_beam, BEAMS, axis=1), cache_top
    )
    local_top = lax.dynamic_update_slice_in_dim(local_top, group_top, first_beam, axis=1)
    own_top = jnp.maximum(lax.dynamic_index_in_dim(local_top, own_beam, axis=1, keepdims=True), new_top[:, None])
    local_top = lax.dynamic_update_slice_in_dim(local_top, own_top, own_beam, axis=1)
    top = all_combine(local_top, BLK_PARTS, jnp.max)

    prompt_weights = jnp.where(
        prompt_live, jnp.exp(prompt_scores - top[:, :, :, None]), 0.0
    ).astype(jnp.bfloat16)
    weighted = jnp.einsum(
        "rht,thd->rhd",
        prompt_weights.reshape(rows, heads_here, -1),
        page_values,
        preferred_element_type=jnp.float32,
    ).reshape(steps, batch, heads_here, HEAD_DIM)
    totals = jnp.sum(prompt_weights.astype(jnp.float32), axis=3)

    group_top_all = lax.dynamic_slice_in_dim(top, first_beam, BEAMS, axis=1)
    cache_weights = jnp.where(
        cache_live, jnp.exp(cache_scores - group_top_all[:, :, :, None]), 0.0
    ).astype(jnp.bfloat16)
    cache_weighted = jnp.einsum(
        "sbhj,jhd->sbhd", cache_weights, own_values, preferred_element_type=jnp.float32
    )
    cache_totals = jnp.sum(cache_weights.astype(jnp.float32), axis=3)

    own_top_all = lax.dynamic_index_in_dim(top, own_beam, axis=1, keepdims=False)
    new_weights = jnp.where(
        new_live, jnp.exp(new_scores - own_top_all[:, :, None]), 0.0
    ).astype(jnp.bfloat16)
    new_weighted = jnp.einsum(
        "sht,sthd->shd", new_weights, new_values_here, preferred_element_type=jnp.float32
    )
    new_totals = jnp.sum(new_weights.astype(jnp.float32), axis=2)

    group_weighted = lax.dynamic_slice_in_dim(weighted, first_beam, BEAMS, axis=1) + cache_weighted
    weighted = lax.dynamic_update_slice_in_dim(weighted, group_weighted, first_beam, axis=1)
    group_totals = lax.dynamic_slice_in_dim(totals, first_beam, BEAMS, axis=1) + cache_totals
    totals = lax.dynamic_update_slice_in_dim(totals, group_totals, first_beam, axis=1)
    own_weighted = lax.dynamic_index_in_dim(weighted, own_beam, axis=1, keepdims=True) + new_weighted[:, None]
    weighted = lax.dynamic_update_slice_in_dim(weighted, own_weighted, own_beam, axis=1)
    own_totals = lax.dynamic_index_in_dim(totals, own_beam, axis=1, keepdims=True) + new_totals[:, None]
    totals = lax.dynamic_update_slice_in_dim(totals, own_totals, own_beam, axis=1)

    lanes = 128
    packed = jnp.concatenate(
        [
            weighted.reshape(rows, feat_here),
            jnp.pad(totals.reshape(rows, heads_here), ((0, 0), (0, lanes - heads_here))),
        ],
        axis=1,
    )
    blk_stages = BLK_PARTS
    packed = scatter_sum(packed, blk_stages)
    part_rows = packed.shape[0]
    weighted = packed[:, :feat_here].reshape(part_rows, heads_here, HEAD_DIM)
    totals = packed[:, feat_here : feat_here + heads_here]
    attention = (weighted / totals[:, :, None]).reshape(part_rows, feat_here).astype(jnp.bfloat16)
    attention = gather_rows(attention, blk_stages)
    head_terms = jnp.dot(attention, w_out, preferred_element_type=jnp.float32)
    head_stages = ("head",)
    head_total = gather_rows(scatter_sum(head_terms, head_stages), head_stages)
    hidden = (head_total + b_out.astype(jnp.float32)[None, :]).astype(jnp.bfloat16)
    hidden = hidden.reshape(steps, batch, -1)

    my_final_src = [anc[(t, steps - 1)][own_beam] - first_beam for t in range(steps)]
    write_rows = my_gen + step_ids
    hit = gen_rows[:, None] == write_rows[None, :]
    chosen = jnp.argmax(hit, axis=1)
    written = jnp.any(hit, axis=1)[:, None]

    def finish(cache, fresh):
        new_rows = jnp.stack([fresh[t, my_final_src[t]] for t in range(steps)])
        return jnp.where(written, jnp.take(new_rows, chosen, axis=0), cache)[None]

    final_keys = finish(back[0], key_new)
    final_values = finish(back[1], value_new)
    return hidden, final_keys, final_values


def solution(mesh):
    heads = mesh.shape["head"]
    blocks = mesh.shape["blk"]
    cores = 2
    group_chips = BEAMS // cores
    devices = np.asarray(mesh.devices).reshape(heads, blocks // BEAMS, group_chips, cores)
    fine = Mesh(devices, ("head",) + BLK_PARTS)
    blk = BLK_PARTS
    in_specs = (
        P(None, None, blk),
        P(blk),
        P(blk),
        P(blk, "head"),
        P(blk, "head"),
        P(blk, "head"),
        P("head"),
        P("head"),
        P("head"),
        P("head", blk),
        P(blk),
        P(blk, None, "head"),
        P(blk, None, "head"),
        P(blk, None, "head"),
        P(blk, None, "head"),
        P(),
        P(),
        P(),
        P(),
    )
    out_specs = (P(None, None, blk), P(blk, None, "head"), P(blk, None, "head"))
    return jax.shard_map(body, mesh=fine, in_specs=in_specs, out_specs=out_specs, check_vma=False)
```

```python
import math

import jax
import jax.numpy as jnp
import numpy as np
from jax import lax
from jax.sharding import Mesh
from jax.sharding import PartitionSpec as P

D = 7168
HEAD_DIM = 128
BEAMS = 8
PAGE = 16
GEN = 256
STEPS = 4

MASKED = -1e30
NORM_EPSILON = 1e-05

BLK_PARTS = ("z", "x", "core")
GROUP = ("x", "core")


def nested(reduce, value):
    for axis in reversed(BLK_PARTS):
        value = reduce(value, axis)
    return value


def axes_size(axes):
    size = 1
    for axis in axes:
        size *= lax.axis_size(axis)
    return size


def scatter_sum(value, axes):
    n = axes_size(axes)
    got = lax.all_to_all(value, axes, 0, 0, tiled=True)
    return jnp.sum(got.reshape((n, value.shape[0] // n) + value.shape[1:]), axis=0)


def gather_rows(value, axes):
    n = axes_size(axes)
    copies = jnp.broadcast_to(value[None], (n,) + value.shape).reshape((n * value.shape[0],) + value.shape[1:])
    return lax.all_to_all(copies, axes, 0, 0, tiled=True)


def all_combine(value, axes, combine):
    n = axes_size(axes)
    got = gather_rows(value[None], axes)
    return combine(got.reshape((n,) + value.shape), axis=0)


def blk_index():
    index = lax.axis_index("z")
    for axis in BLK_PARTS[1:]:
        index = index * lax.axis_size(axis) + lax.axis_index(axis)
    return index


def body(
    inputs,
    ln_gain,
    ln_bias,
    w_query,
    w_key,
    w_value,
    b_query,
    b_key,
    b_value,
    w_out,
    b_out,
    prefix_keys,
    prefix_values,
    suffix_keys,
    suffix_values,
    page_table,
    prompt_len,
    gen_len,
    parents,
):
    me = blk_index()
    group = axes_size(GROUP)
    member = lax.axis_index("x") * lax.axis_size("core") + lax.axis_index("core")
    steps = inputs.shape[0]
    batch = inputs.shape[1]
    feat_local = inputs.shape[2]
    feat_here = w_query.shape[1]
    heads_here = feat_here // HEAD_DIM
    pages_here = prefix_keys.shape[0]
    requests = page_table.shape[0]
    slot_count = page_table.shape[1]
    rows = steps * batch
    score_scale = 1.0 / math.sqrt(HEAD_DIM)
    my_request = me // BEAMS
    first_beam = my_request * BEAMS
    my_gen = gen_len[my_request]
    cols_all = 3 * feat_here
    col_block = cols_all // group
    chunk_rows = GEN // group

    beam_ids = jnp.arange(batch, dtype=jnp.int32)
    anc = {}
    for s in range(steps):
        x = beam_ids
        anc[(s, s)] = x
        for t in range(s, -1, -1):
            x = jnp.take(parents[t], x)
            anc[(t - 1, s)] = x
    origin = jnp.stack([anc[(-1, s)] for s in range(steps)])

    cw = feat_here // group
    weight_chunks = jnp.stack([w_query, w_key, w_value], axis=1).reshape(feat_local, 3, group, cw)
    weight_chunks = weight_chunks.transpose(2, 0, 1, 3).reshape(group, -1)
    row_block = jnp.concatenate([inputs.reshape(-1), ln_gain, ln_bias])
    cache_chunks = jnp.concatenate(
        [suffix_keys[0].reshape(group, -1), suffix_values[0].reshape(group, -1)], axis=1
    )
    sent = jnp.concatenate(
        [weight_chunks, jnp.broadcast_to(row_block[None], (group, row_block.shape[0])), cache_chunks], axis=1
    )
    got = lax.all_to_all(sent, GROUP, 0, 0, tiled=True)
    n_w = feat_local * 3 * cw
    n_in = rows * feat_local
    w_group = got[:, :n_w].reshape(group, feat_local, 3, cw)
    in_group = got[:, n_w : n_w + n_in].reshape(group, rows, feat_local).astype(jnp.float32)
    gain_group = got[:, n_w + n_in : n_w + n_in + feat_local].astype(jnp.float32)
    shift_group = got[:, n_w + n_in + feat_local : n_w + n_in + 2 * feat_local].astype(jnp.float32)
    spread = got[:, n_w + n_in + 2 * feat_local :].reshape(group, 2, chunk_rows, feat_here)

    stats = jnp.stack([jnp.sum(in_group, axis=(0, 2)), jnp.sum(in_group * in_group, axis=(0, 2))], axis=1)
    stats = all_combine(stats, ("z",), jnp.sum)
    row_mean = stats[:, 0] / D
    variance = stats[:, 1] / D - row_mean * row_mean
    normed = (
        (in_group - row_mean[None, :, None]) * lax.rsqrt(variance + NORM_EPSILON)[None, :, None]
        * gain_group[:, None, :]
        + shift_group[:, None, :]
    ).astype(jnp.bfloat16)
    partial = jnp.einsum("grf,gfwc->rwc", normed, w_group, preferred_element_type=jnp.float32)
    partial = partial.reshape(steps, requests, BEAMS, 3, cw).transpose(1, 0, 2, 3, 4)
    summed = jnp.sum(lax.all_to_all(partial, "z", 0, 0, tiled=True).reshape(
        (lax.axis_size("z"), steps, BEAMS, 3, cw)), axis=0)
    bias_all = jnp.stack([b_query, b_key, b_value]).astype(jnp.float32).reshape(3, group, cw)
    bias_block = lax.dynamic_index_in_dim(bias_all, member, axis=1, keepdims=False)
    mine = (summed + bias_block).astype(jnp.bfloat16)

    q_blocks = gather_rows(mine[None, :, :, 0, :], BLK_PARTS)
    queries = q_blocks.reshape(requests, group, steps, BEAMS, cw).transpose(2, 0, 3, 1, 4).reshape(
        steps, batch, heads_here, HEAD_DIM)
    group_queries = lax.dynamic_slice_in_dim(queries, first_beam, BEAMS, axis=1)

    final_origin = origin[steps - 1]
    pick = lax.dynamic_slice_in_dim(final_origin, first_beam, BEAMS) - first_beam
    picked = jnp.take(spread, pick, axis=0).reshape(group, -1)

    kv_mine = mine[:, :, 1:, :]
    n_mine = steps * BEAMS * 2 * cw
    sent2 = jnp.concatenate(
        [jnp.broadcast_to(kv_mine.reshape(1, -1), (group, n_mine)), picked], axis=1
    )
    got2 = lax.all_to_all(sent2, GROUP, 0, 0, tiled=True)
    kv = got2[:, :n_mine].reshape(group, steps, BEAMS, 2, cw).transpose(1, 2, 3, 0, 4).reshape(
        steps, BEAMS, 2, feat_here)
    back = got2[:, n_mine:].reshape(group, 2, chunk_rows, feat_here).transpose(1, 0, 2, 3).reshape(2, GEN, feat_here)
    key_new = kv[:, :, 0]
    value_new = kv[:, :, 1]

    beam_request = beam_ids // BEAMS
    beam_prompt = jnp.take(prompt_len, beam_request)
    page_ids = me * pages_here + jnp.arange(pages_here, dtype=jnp.int32)
    slot_ids = jnp.arange(slot_count, dtype=jnp.int32)
    slot_live = slot_ids[None, :] * PAGE < prompt_len[:, None]
    page_match = (
        (page_table[:, :, None] == page_ids[None, None, :]) & slot_live[:, :, None]
    ).astype(jnp.int32)
    request_ids = jnp.arange(requests, dtype=jnp.int32)
    page_request = jnp.sum(page_match * request_ids[:, None, None], axis=(0, 1))
    page_slot = jnp.sum(page_match * slot_ids[None, :, None], axis=(0, 1))
    page_used = jnp.sum(page_match, axis=(0, 1)) > 0
    token_pos = (page_slot[:, None] * PAGE + jnp.arange(PAGE, dtype=jnp.int32)[None, :]).reshape(-1)
    token_request = jnp.repeat(page_request, PAGE)
    token_used = jnp.repeat(page_used, PAGE)
    prefix_live = (
        token_used[None, :]
        & (token_request[None, :] == beam_request[:, None])
        & (token_pos[None, :] < beam_prompt[:, None])
    )
    page_keys = prefix_keys.reshape(pages_here * PAGE, heads_here, HEAD_DIM)
    page_values = prefix_values.reshape(pages_here * PAGE, heads_here, HEAD_DIM)
    flat_queries = queries.reshape(rows, heads_here, HEAD_DIM)
    prompt_scores = (
        jnp.einsum("rhd,thd->rht", flat_queries, page_keys, preferred_element_type=jnp.float32)
        * score_scale
    ).reshape(steps, batch, heads_here, -1)
    prompt_live = prefix_live[None, :, None, :]
    prompt_top = jnp.max(jnp.where(prompt_live, prompt_scores, MASKED), axis=3)

    group_origin = lax.dynamic_slice_in_dim(origin, first_beam, BEAMS, axis=1)
    own_keys = suffix_keys[0].reshape(GEN, heads_here, HEAD_DIM)
    own_values = suffix_values[0].reshape(GEN, heads_here, HEAD_DIM)
    cache_scores = (
        jnp.einsum("sbhd,jhd->sbhj", group_queries, own_keys, preferred_element_type=jnp.float32)
        * score_scale
    )
    gen_rows = jnp.arange(GEN, dtype=jnp.int32)
    cache_live = (group_origin == me)[:, :, None, None] & (gen_rows < my_gen)[None, None, None, :]
    cache_top = jnp.max(jnp.where(cache_live, cache_scores, MASKED), axis=3)

    own_beam = me
    own_queries = lax.dynamic_index_in_dim(group_queries, member, axis=1, keepdims=False)
    new_src = jnp.stack(
        [jnp.stack([anc[(t, s)][own_beam] if t <= s else own_beam for t in range(steps)]) for s in range(steps)]
    ) - first_beam
    step_ids = jnp.arange(steps, dtype=jnp.int32)
    new_keys_here = key_new[step_ids[None, :], new_src].reshape(steps, steps, heads_here, HEAD_DIM)
    new_values_here = value_new[step_ids[None, :], new_src].reshape(steps, steps, heads_here, HEAD_DIM)
    new_scores = (
        jnp.einsum("shd,sthd->sht", own_queries, new_keys_here, preferred_element_type=jnp.float32)
        * score_scale
    )
    new_live = (step_ids[None, :] <= step_ids[:, None])[:, None, :]
    new_top = jnp.max(jnp.where(new_live, new_scores, MASKED), axis=2)

    local_top = prompt_top
    group_top = jnp.maximum(
        lax.dynamic_slice_in_dim(local_top, first_beam, BEAMS, axis=1), cache_top
    )
    local_top = lax.dynamic_update_slice_in_dim(local_top, group_top, first_beam, axis=1)
    own_top = jnp.maximum(lax.dynamic_index_in_dim(local_top, own_beam, axis=1, keepdims=True), new_top[:, None])
    local_top = lax.dynamic_update_slice_in_dim(local_top, own_top, own_beam, axis=1)
    top = all_combine(local_top, BLK_PARTS, jnp.max)

    prompt_weights = jnp.where(
        prompt_live, jnp.exp(prompt_scores - top[:, :, :, None]), 0.0
    ).astype(jnp.bfloat16)
    weighted = jnp.einsum(
        "rht,thd->rhd",
        prompt_weights.reshape(rows, heads_here, -1),
        page_values,
        preferred_element_type=jnp.float32,
    ).reshape(steps, batch, heads_here, HEAD_DIM)
    totals = jnp.sum(prompt_weights.astype(jnp.float32), axis=3)

    group_top_all = lax.dynamic_slice_in_dim(top, first_beam, BEAMS, axis=1)
    cache_weights = jnp.where(
        cache_live, jnp.exp(cache_scores - group_top_all[:, :, :, None]), 0.0
    ).astype(jnp.bfloat16)
    cache_weighted = jnp.einsum(
        "sbhj,jhd->sbhd", cache_weights, own_values, preferred_element_type=jnp.float32
    )
    cache_totals = jnp.sum(cache_weights.astype(jnp.float32), axis=3)

    own_top_all = lax.dynamic_index_in_dim(top, own_beam, axis=1, keepdims=False)
    new_weights = jnp.where(
        new_live, jnp.exp(new_scores - own_top_all[:, :, None]), 0.0
    ).astype(jnp.bfloat16)
    new_weighted = jnp.einsum(
        "sht,sthd->shd", new_weights, new_values_here, preferred_element_type=jnp.float32
    )
    new_totals = jnp.sum(new_weights.astype(jnp.float32), axis=2)

    group_weighted = lax.dynamic_slice_in_dim(weighted, first_beam, BEAMS, axis=1) + cache_weighted
    weighted = lax.dynamic_update_slice_in_dim(weighted, group_weighted, first_beam, axis=1)
    group_totals = lax.dynamic_slice_in_dim(totals, first_beam, BEAMS, axis=1) + cache_totals
    totals = lax.dynamic_update_slice_in_dim(totals, group_totals, first_beam, axis=1)
    own_weighted = lax.dynamic_index_in_dim(weighted, own_beam, axis=1, keepdims=True) + new_weighted[:, None]
    weighted = lax.dynamic_update_slice_in_dim(weighted, own_weighted, own_beam, axis=1)
    own_totals = lax.dynamic_index_in_dim(totals, own_beam, axis=1, keepdims=True) + new_totals[:, None]
    totals = lax.dynamic_update_slice_in_dim(totals, own_totals, own_beam, axis=1)

    lanes = 128
    packed = jnp.concatenate(
        [
            weighted.reshape(rows, feat_here),
            jnp.pad(totals.reshape(rows, heads_here), ((0, 0), (0, lanes - heads_here))),
        ],
        axis=1,
    )
    blk_stages = BLK_PARTS
    packed = scatter_sum(packed, blk_stages)
    part_rows = packed.shape[0]
    weighted = packed[:, :feat_here].reshape(part_rows, heads_here, HEAD_DIM)
    totals = packed[:, feat_here : feat_here + heads_here]
    attention = (weighted / totals[:, :, None]).reshape(part_rows, feat_here).astype(jnp.bfloat16)
    attention = gather_rows(attention, blk_stages)
    head_terms = jnp.dot(attention, w_out, preferred_element_type=jnp.float32)
    head_stages = ("head",)
    head_part = scatter_sum(head_terms, head_stages)
    hidden = gather_rows((head_part + b_out.astype(jnp.float32)[None, :]).astype(jnp.bfloat16), head_stages)
    hidden = hidden.reshape(steps, batch, -1)

    my_final_src = [anc[(t, steps - 1)][own_beam] - first_beam for t in range(steps)]
    write_rows = my_gen + step_ids
    hit = gen_rows[:, None] == write_rows[None, :]
    chosen = jnp.argmax(hit, axis=1)
    written = jnp.any(hit, axis=1)[:, None]

    def finish(cache, fresh):
        new_rows = jnp.stack([fresh[t, my_final_src[t]] for t in range(steps)])
        return jnp.where(written, jnp.take(new_rows, chosen, axis=0), cache)[None]

    final_keys = finish(back[0], key_new)
    final_values = finish(back[1], value_new)
    return hidden, final_keys, final_values


def solution(mesh):
    heads = mesh.shape["head"]
    blocks = mesh.shape["blk"]
    cores = 2
    group_chips = BEAMS // cores
    devices = np.asarray(mesh.devices).reshape(heads, blocks // BEAMS, group_chips, cores)
    fine = Mesh(devices, ("head",) + BLK_PARTS)
    blk = BLK_PARTS
    in_specs = (
        P(None, None, blk),
        P(blk),
        P(blk),
        P(blk, "head"),
        P(blk, "head"),
        P(blk, "head"),
        P("head"),
        P("head"),
        P("head"),
        P("head", blk),
        P(blk),
        P(blk, None, "head"),
        P(blk, None, "head"),
        P(blk, None, "head"),
        P(blk, None, "head"),
        P(),
        P(),
        P(),
        P(),
    )
    out_specs = (P(None, None, blk), P(blk, None, "head"), P(blk, None, "head"))
    return jax.shard_map(body, mesh=fine, in_specs=in_specs, out_specs=out_specs, check_vma=False)
```

```python
import math

import jax
import jax.numpy as jnp
import numpy as np
from jax import lax
from jax.sharding import Mesh
from jax.sharding import PartitionSpec as P

D = 7168
HEAD_DIM = 128
BEAMS = 8
PAGE = 16
GEN = 256
STEPS = 4

MASKED = -1e30
NORM_EPSILON = 1e-05

BLK_PARTS = ("z", "x", "core")
GROUP = ("x", "core")


def nested(reduce, value):
    for axis in reversed(BLK_PARTS):
        value = reduce(value, axis)
    return value


def axes_size(axes):
    size = 1
    for axis in axes:
        size *= lax.axis_size(axis)
    return size


def scatter_sum(value, axes):
    n = axes_size(axes)
    got = lax.all_to_all(value, axes, 0, 0, tiled=True)
    return jnp.sum(got.reshape((n, value.shape[0] // n) + value.shape[1:]), axis=0)


def gather_rows(value, axes):
    n = axes_size(axes)
    copies = jnp.broadcast_to(value[None], (n,) + value.shape).reshape((n * value.shape[0],) + value.shape[1:])
    return lax.all_to_all(copies, axes, 0, 0, tiled=True)


def all_combine(value, axes, combine):
    n = axes_size(axes)
    got = gather_rows(value[None], axes)
    return combine(got.reshape((n,) + value.shape), axis=0)


def blk_index():
    index = lax.axis_index("z")
    for axis in BLK_PARTS[1:]:
        index = index * lax.axis_size(axis) + lax.axis_index(axis)
    return index


def body(
    inputs,
    ln_gain,
    ln_bias,
    w_query,
    w_key,
    w_value,
    b_query,
    b_key,
    b_value,
    w_out,
    b_out,
    prefix_keys,
    prefix_values,
    suffix_keys,
    suffix_values,
    page_table,
    prompt_len,
    gen_len,
    parents,
):
    me = blk_index()
    group = axes_size(GROUP)
    member = lax.axis_index("x") * lax.axis_size("core") + lax.axis_index("core")
    steps = inputs.shape[0]
    batch = inputs.shape[1]
    feat_local = inputs.shape[2]
    feat_here = w_query.shape[1]
    heads_here = feat_here // HEAD_DIM
    pages_here = prefix_keys.shape[0]
    requests = page_table.shape[0]
    slot_count = page_table.shape[1]
    rows = steps * batch
    score_scale = 1.0 / math.sqrt(HEAD_DIM)
    my_request = me // BEAMS
    first_beam = my_request * BEAMS
    my_gen = gen_len[my_request]
    cols_all = 3 * feat_here
    col_block = cols_all // group
    chunk_rows = GEN // group

    beam_ids = jnp.arange(batch, dtype=jnp.int32)
    anc = {}
    for s in range(steps):
        x = beam_ids
        anc[(s, s)] = x
        for t in range(s, -1, -1):
            x = jnp.take(parents[t], x)
            anc[(t - 1, s)] = x
    origin = jnp.stack([anc[(-1, s)] for s in range(steps)])

    rows_local = inputs.astype(jnp.float32).reshape(rows, feat_local)
    stats = jnp.stack([jnp.sum(rows_local, axis=1), jnp.sum(rows_local * rows_local, axis=1)], axis=1)
    stats = all_combine(stats, BLK_PARTS, jnp.sum)
    row_mean = stats[:, 0] / D
    variance = stats[:, 1] / D - row_mean * row_mean

    lanes = 128
    cw = feat_here // group
    weight_chunks = jnp.stack([w_query, w_key, w_value], axis=1).reshape(feat_local, 3, group, cw)
    weight_chunks = weight_chunks.transpose(2, 0, 1, 3).reshape(group, -1)
    norm_params = jnp.concatenate([ln_gain, ln_bias])
    pad = -(inputs.size + norm_params.shape[0]) % lanes
    row_block = jnp.concatenate([inputs.reshape(-1), norm_params, jnp.zeros((pad,), inputs.dtype)])
    cache_chunks = jnp.concatenate(
        [suffix_keys[0].reshape(group, -1), suffix_values[0].reshape(group, -1)], axis=1
    )
    sent = jnp.concatenate(
        [weight_chunks, jnp.broadcast_to(row_block[None], (group, row_block.shape[0])), cache_chunks], axis=1
    )
    sent = sent.reshape(group, -1, lanes)
    got = lax.all_to_all(sent, GROUP, 0, 0, tiled=True).reshape(group, -1)
    n_w = feat_local * 3 * cw
    n_in = rows * feat_local
    n_row = row_block.shape[0]
    w_group = got[:, :n_w].reshape(group, feat_local, 3, cw)
    in_group = got[:, n_w : n_w + n_in].reshape(group, rows, feat_local).astype(jnp.float32)
    gain_group = got[:, n_w + n_in : n_w + n_in + feat_local].astype(jnp.float32)
    shift_group = got[:, n_w + n_in + feat_local : n_w + n_in + 2 * feat_local].astype(jnp.float32)
    spread = got[:, n_w + n_row :].reshape(group, 2, chunk_rows, feat_here)

    normed = (
        (in_group - row_mean[None, :, None]) * lax.rsqrt(variance + NORM_EPSILON)[None, :, None]
        * gain_group[:, None, :]
        + shift_group[:, None, :]
    ).astype(jnp.bfloat16)
    partial = jnp.einsum("grf,gfwc->rwc", normed, w_group, preferred_element_type=jnp.float32)
    partial = partial.reshape(steps, requests, BEAMS, 3, cw).transpose(1, 0, 2, 3, 4)
    summed = jnp.sum(lax.all_to_all(partial, "z", 0, 0, tiled=True).reshape(
        (lax.axis_size("z"), steps, BEAMS, 3, cw)), axis=0)
    bias_all = jnp.stack([b_query, b_key, b_value]).astype(jnp.float32).reshape(3, group, cw)
    bias_block = lax.dynamic_index_in_dim(bias_all, member, axis=1, keepdims=False)
    mine = (summed + bias_block).astype(jnp.bfloat16)

    q_blocks = gather_rows(mine[None, :, :, 0, :], BLK_PARTS)
    queries = q_blocks.reshape(requests, group, steps, BEAMS, cw).transpose(2, 0, 3, 1, 4).reshape(
        steps, batch, heads_here, HEAD_DIM)
    group_queries = lax.dynamic_slice_in_dim(queries, first_beam, BEAMS, axis=1)

    final_origin = origin[steps - 1]
    pick = lax.dynamic_slice_in_dim(final_origin, first_beam, BEAMS) - first_beam
    picked = jnp.take(spread, pick, axis=0).reshape(group, -1)

    kv_mine = mine[:, :, 1:, :]
    n_mine = steps * BEAMS * 2 * cw
    sent2 = jnp.concatenate(
        [jnp.broadcast_to(kv_mine.reshape(1, -1), (group, n_mine)), picked], axis=1
    )
    got2 = lax.all_to_all(sent2, GROUP, 0, 0, tiled=True)
    kv = got2[:, :n_mine].reshape(group, steps, BEAMS, 2, cw).transpose(1, 2, 3, 0, 4).reshape(
        steps, BEAMS, 2, feat_here)
    back = got2[:, n_mine:].reshape(group, 2, chunk_rows, feat_here).transpose(1, 0, 2, 3).reshape(2, GEN, feat_here)
    key_new = kv[:, :, 0]
    value_new = kv[:, :, 1]

    beam_request = beam_ids // BEAMS
    beam_prompt = jnp.take(prompt_len, beam_request)
    page_ids = me * pages_here + jnp.arange(pages_here, dtype=jnp.int32)
    slot_ids = jnp.arange(slot_count, dtype=jnp.int32)
    slot_live = slot_ids[None, :] * PAGE < prompt_len[:, None]
    page_match = (
        (page_table[:, :, None] == page_ids[None, None, :]) & slot_live[:, :, None]
    ).astype(jnp.int32)
    request_ids = jnp.arange(requests, dtype=jnp.int32)
    page_request = jnp.sum(page_match * request_ids[:, None, None], axis=(0, 1))
    page_slot = jnp.sum(page_match * slot_ids[None, :, None], axis=(0, 1))
    page_used = jnp.sum(page_match, axis=(0, 1)) > 0
    token_pos = (page_slot[:, None] * PAGE + jnp.arange(PAGE, dtype=jnp.int32)[None, :]).reshape(-1)
    token_request = jnp.repeat(page_request, PAGE)
    token_used = jnp.repeat(page_used, PAGE)
    prefix_live = (
        token_used[None, :]
        & (token_request[None, :] == beam_request[:, None])
        & (token_pos[None, :] < beam_prompt[:, None])
    )
    page_keys = prefix_keys.reshape(pages_here * PAGE, heads_here, HEAD_DIM)
    page_values = prefix_values.reshape(pages_here * PAGE, heads_here, HEAD_DIM)
    flat_queries = queries.reshape(rows, heads_here, HEAD_DIM)
    prompt_scores = (
        jnp.einsum("rhd,thd->rht", flat_queries, page_keys, preferred_element_type=jnp.float32)
        * score_scale
    ).reshape(steps, batch, heads_here, -1)
    prompt_live = prefix_live[None, :, None, :]
    prompt_top = jnp.max(jnp.where(prompt_live, prompt_scores, MASKED), axis=3)

    group_origin = lax.dynamic_slice_in_dim(origin, first_beam, BEAMS, axis=1)
    own_keys = suffix_keys[0].reshape(GEN, heads_here, HEAD_DIM)
    own_values = suffix_values[0].reshape(GEN, heads_here, HEAD_DIM)
    cache_scores = (
        jnp.einsum("sbhd,jhd->sbhj", group_queries, own_keys, preferred_element_type=jnp.float32)
        * score_scale
    )
    gen_rows = jnp.arange(GEN, dtype=jnp.int32)
    cache_live = (group_origin == me)[:, :, None, None] & (gen_rows < my_gen)[None, None, None, :]
    cache_top = jnp.max(jnp.where(cache_live, cache_scores, MASKED), axis=3)

    own_beam = me
    own_queries = lax.dynamic_index_in_dim(group_queries, member, axis=1, keepdims=False)
    new_src = jnp.stack(
        [jnp.stack([anc[(t, s)][own_beam] if t <= s else own_beam for t in range(steps)]) for s in range(steps)]
    ) - first_beam
    step_ids = jnp.arange(steps, dtype=jnp.int32)
    new_keys_here = key_new[step_ids[None, :], new_src].reshape(steps, steps, heads_here, HEAD_DIM)
    new_values_here = value_new[step_ids[None, :], new_src].reshape(steps, steps, heads_here, HEAD_DIM)
    new_scores = (
        jnp.einsum("shd,sthd->sht", own_queries, new_keys_here, preferred_element_type=jnp.float32)
        * score_scale
    )
    new_live = (step_ids[None, :] <= step_ids[:, None])[:, None, :]
    new_top = jnp.max(jnp.where(new_live, new_scores, MASKED), axis=2)

    local_top = prompt_top
    group_top = jnp.maximum(
        lax.dynamic_slice_in_dim(local_top, first_beam, BEAMS, axis=1), cache_top
    )
    local_top = lax.dynamic_update_slice_in_dim(local_top, group_top, first_beam, axis=1)
    own_top = jnp.maximum(lax.dynamic_index_in_dim(local_top, own_beam, axis=1, keepdims=True), new_top[:, None])
    local_top = lax.dynamic_update_slice_in_dim(local_top, own_top, own_beam, axis=1)
    top = all_combine(local_top, BLK_PARTS, jnp.max)

    prompt_weights = jnp.where(
        prompt_live, jnp.exp(prompt_scores - top[:, :, :, None]), 0.0
    ).astype(jnp.bfloat16)
    weighted = jnp.einsum(
        "rht,thd->rhd",
        prompt_weights.reshape(rows, heads_here, -1),
        page_values,
        preferred_element_type=jnp.float32,
    ).reshape(steps, batch, heads_here, HEAD_DIM)
    totals = jnp.sum(prompt_weights.astype(jnp.float32), axis=3)

    group_top_all = lax.dynamic_slice_in_dim(top, first_beam, BEAMS, axis=1)
    cache_weights = jnp.where(
        cache_live, jnp.exp(cache_scores - group_top_all[:, :, :, None]), 0.0
    ).astype(jnp.bfloat16)
    cache_weighted = jnp.einsum(
        "sbhj,jhd->sbhd", cache_weights, own_values, preferred_element_type=jnp.float32
    )
    cache_totals = jnp.sum(cache_weights.astype(jnp.float32), axis=3)

    own_top_all = lax.dynamic_index_in_dim(top, own_beam, axis=1, keepdims=False)
    new_weights = jnp.where(
        new_live, jnp.exp(new_scores - own_top_all[:, :, None]), 0.0
    ).astype(jnp.bfloat16)
    new_weighted = jnp.einsum(
        "sht,sthd->shd", new_weights, new_values_here, preferred_element_type=jnp.float32
    )
    new_totals = jnp.sum(new_weights.astype(jnp.float32), axis=2)

    group_weighted = lax.dynamic_slice_in_dim(weighted, first_beam, BEAMS, axis=1) + cache_weighted
    weighted = lax.dynamic_update_slice_in_dim(weighted, group_weighted, first_beam, axis=1)
    group_totals = lax.dynamic_slice_in_dim(totals, first_beam, BEAMS, axis=1) + cache_totals
    totals = lax.dynamic_update_slice_in_dim(totals, group_totals, first_beam, axis=1)
    own_weighted = lax.dynamic_index_in_dim(weighted, own_beam, axis=1, keepdims=True) + new_weighted[:, None]
    weighted = lax.dynamic_update_slice_in_dim(weighted, own_weighted, own_beam, axis=1)
    own_totals = lax.dynamic_index_in_dim(totals, own_beam, axis=1, keepdims=True) + new_totals[:, None]
    totals = lax.dynamic_update_slice_in_dim(totals, own_totals, own_beam, axis=1)

    packed = jnp.concatenate(
        [
            weighted.reshape(rows, feat_here),
            jnp.pad(totals.reshape(rows, heads_here), ((0, 0), (0, lanes - heads_here))),
        ],
        axis=1,
    )
    blk_stages = BLK_PARTS
    packed = scatter_sum(packed, blk_stages)
    part_rows = packed.shape[0]
    weighted = packed[:, :feat_here].reshape(part_rows, heads_here, HEAD_DIM)
    totals = packed[:, feat_here : feat_here + heads_here]
    attention = (weighted / totals[:, :, None]).reshape(part_rows, feat_here).astype(jnp.bfloat16)
    attention = gather_rows(attention, blk_stages)
    head_terms = jnp.dot(attention, w_out, preferred_element_type=jnp.float32)
    head_stages = ("head",)
    head_total = all_combine(head_terms, head_stages, jnp.sum)
    hidden = (head_total + b_out.astype(jnp.float32)[None, :]).astype(jnp.bfloat16)
    hidden = hidden.reshape(steps, batch, -1)

    my_final_src = [anc[(t, steps - 1)][own_beam] - first_beam for t in range(steps)]
    write_rows = my_gen + step_ids
    hit = gen_rows[:, None] == write_rows[None, :]
    chosen = jnp.argmax(hit, axis=1)
    written = jnp.any(hit, axis=1)[:, None]

    def finish(cache, fresh):
        new_rows = jnp.stack([fresh[t, my_final_src[t]] for t in range(steps)])
        return jnp.where(written, jnp.take(new_rows, chosen, axis=0), cache)[None]

    final_keys = finish(back[0], key_new)
    final_values = finish(back[1], value_new)
    return hidden, final_keys, final_values


def solution(mesh):
    heads = mesh.shape["head"]
    blocks = mesh.shape["blk"]
    cores = 2
    group_chips = BEAMS // cores
    devices = np.asarray(mesh.devices).reshape(heads, blocks // BEAMS, group_chips, cores)
    fine = Mesh(devices, ("head",) + BLK_PARTS)
    blk = BLK_PARTS
    in_specs = (
        P(None, None, blk),
        P(blk),
        P(blk),
        P(blk, "head"),
        P(blk, "head"),
        P(blk, "head"),
        P("head"),
        P("head"),
        P("head"),
        P("head", blk),
        P(blk),
        P(blk, None, "head"),
        P(blk, None, "head"),
        P(blk, None, "head"),
        P(blk, None, "head"),
        P(),
        P(),
        P(),
        P(),
    )
    out_specs = (P(None, None, blk), P(blk, None, "head"), P(blk, None, "head"))
    return jax.shard_map(body, mesh=fine, in_specs=in_specs, out_specs=out_specs, check_vma=False)
```

```python
import math

import jax
import jax.numpy as jnp
import numpy as np
from jax import lax
from jax.sharding import Mesh
from jax.sharding import PartitionSpec as P

D = 7168
HEAD_DIM = 128
BEAMS = 8
PAGE = 16
GEN = 256
STEPS = 4

MASKED = -1e30
NORM_EPSILON = 1e-05

BLK_PARTS = ("z", "x", "core")
GROUP = ("x", "core")


def nested(reduce, value):
    for axis in reversed(BLK_PARTS):
        value = reduce(value, axis)
    return value


def axes_size(axes):
    size = 1
    for axis in axes:
        size *= lax.axis_size(axis)
    return size


def scatter_sum(value, axes):
    n = axes_size(axes)
    got = lax.all_to_all(value, axes, 0, 0, tiled=True)
    return jnp.sum(got.reshape((n, value.shape[0] // n) + value.shape[1:]), axis=0)


def gather_rows(value, axes):
    n = axes_size(axes)
    copies = jnp.broadcast_to(value[None], (n,) + value.shape).reshape((n * value.shape[0],) + value.shape[1:])
    return lax.all_to_all(copies, axes, 0, 0, tiled=True)


def all_combine(value, axes, combine):
    n = axes_size(axes)
    got = gather_rows(value[None], axes)
    return combine(got.reshape((n,) + value.shape), axis=0)


def butterfly_sum(value, axis):
    bit = 1
    while bit < lax.axis_size(axis):
        value = value + lax.ppermute(value, axis, [(i, i ^ bit) for i in range(lax.axis_size(axis))])
        bit *= 2
    return value


def blk_index():
    index = lax.axis_index("z")
    for axis in BLK_PARTS[1:]:
        index = index * lax.axis_size(axis) + lax.axis_index(axis)
    return index


def body(
    inputs,
    ln_gain,
    ln_bias,
    w_query,
    w_key,
    w_value,
    b_query,
    b_key,
    b_value,
    w_out,
    b_out,
    prefix_keys,
    prefix_values,
    suffix_keys,
    suffix_values,
    page_table,
    prompt_len,
    gen_len,
    parents,
):
    me = blk_index()
    group = axes_size(GROUP)
    member = lax.axis_index("x") * lax.axis_size("core") + lax.axis_index("core")
    steps = inputs.shape[0]
    batch = inputs.shape[1]
    feat_local = inputs.shape[2]
    feat_here = w_query.shape[1]
    heads_here = feat_here // HEAD_DIM
    pages_here = prefix_keys.shape[0]
    requests = page_table.shape[0]
    slot_count = page_table.shape[1]
    rows = steps * batch
    score_scale = 1.0 / math.sqrt(HEAD_DIM)
    my_request = me // BEAMS
    first_beam = my_request * BEAMS
    my_gen = gen_len[my_request]
    cols_all = 3 * feat_here
    col_block = cols_all // group
    chunk_rows = GEN // group

    beam_ids = jnp.arange(batch, dtype=jnp.int32)
    anc = {}
    for s in range(steps):
        x = beam_ids
        anc[(s, s)] = x
        for t in range(s, -1, -1):
            x = jnp.take(parents[t], x)
            anc[(t - 1, s)] = x
    origin = jnp.stack([anc[(-1, s)] for s in range(steps)])

    rows_local = inputs.astype(jnp.float32).reshape(rows, feat_local)
    stats = jnp.stack([jnp.sum(rows_local, axis=1), jnp.sum(rows_local * rows_local, axis=1)], axis=1)
    stats = all_combine(stats, BLK_PARTS, jnp.sum)
    row_mean = stats[:, 0] / D
    variance = stats[:, 1] / D - row_mean * row_mean

    lanes = 128
    cw = feat_here // group
    weight_chunks = jnp.stack([w_query, w_key, w_value], axis=1).reshape(feat_local, 3, group, cw)
    weight_chunks = weight_chunks.transpose(2, 0, 1, 3).reshape(group, -1)
    norm_params = jnp.concatenate([ln_gain, ln_bias])
    pad = -(inputs.size + norm_params.shape[0]) % lanes
    row_block = jnp.concatenate([inputs.reshape(-1), norm_params, jnp.zeros((pad,), inputs.dtype)])
    cache_chunks = jnp.concatenate(
        [suffix_keys[0].reshape(group, -1), suffix_values[0].reshape(group, -1)], axis=1
    )
    sent = jnp.concatenate(
        [weight_chunks, jnp.broadcast_to(row_block[None], (group, row_block.shape[0])), cache_chunks], axis=1
    )
    sent = sent.reshape(group, -1, lanes)
    got = lax.all_to_all(sent, GROUP, 0, 0, tiled=True).reshape(group, -1)
    n_w = feat_local * 3 * cw
    n_in = rows * feat_local
    n_row = row_block.shape[0]
    w_group = got[:, :n_w].reshape(group, feat_local, 3, cw)
    in_group = got[:, n_w : n_w + n_in].reshape(group, rows, feat_local).astype(jnp.float32)
    gain_group = got[:, n_w + n_in : n_w + n_in + feat_local].astype(jnp.float32)
    shift_group = got[:, n_w + n_in + feat_local : n_w + n_in + 2 * feat_local].astype(jnp.float32)
    spread = got[:, n_w + n_row :].reshape(group, 2, chunk_rows, feat_here)

    normed = (
        (in_group - row_mean[None, :, None]) * lax.rsqrt(variance + NORM_EPSILON)[None, :, None]
        * gain_group[:, None, :]
        + shift_group[:, None, :]
    ).astype(jnp.bfloat16)
    partial = jnp.einsum("grf,gfwc->rwc", normed, w_group, preferred_element_type=jnp.float32)
    partial = partial.reshape(steps, requests, BEAMS, 3, cw).transpose(1, 0, 2, 3, 4)
    summed = jnp.sum(lax.all_to_all(partial, "z", 0, 0, tiled=True).reshape(
        (lax.axis_size("z"), steps, BEAMS, 3, cw)), axis=0)
    bias_all = jnp.stack([b_query, b_key, b_value]).astype(jnp.float32).reshape(3, group, cw)
    bias_block = lax.dynamic_index_in_dim(bias_all, member, axis=1, keepdims=False)
    mine = (summed + bias_block).astype(jnp.bfloat16)

    q_blocks = gather_rows(mine[None, :, :, 0, :], BLK_PARTS)
    queries = q_blocks.reshape(requests, group, steps, BEAMS, cw).transpose(2, 0, 3, 1, 4).reshape(
        steps, batch, heads_here, HEAD_DIM)
    group_queries = lax.dynamic_slice_in_dim(queries, first_beam, BEAMS, axis=1)

    final_origin = origin[steps - 1]
    pick = lax.dynamic_slice_in_dim(final_origin, first_beam, BEAMS) - first_beam
    picked = jnp.take(spread, pick, axis=0).reshape(group, -1)

    kv_mine = mine[:, :, 1:, :]
    n_mine = steps * BEAMS * 2 * cw
    sent2 = jnp.concatenate(
        [jnp.broadcast_to(kv_mine.reshape(1, -1), (group, n_mine)), picked], axis=1
    )
    got2 = lax.all_to_all(sent2, GROUP, 0, 0, tiled=True)
    kv = got2[:, :n_mine].reshape(group, steps, BEAMS, 2, cw).transpose(1, 2, 3, 0, 4).reshape(
        steps, BEAMS, 2, feat_here)
    back = got2[:, n_mine:].reshape(group, 2, chunk_rows, feat_here).transpose(1, 0, 2, 3).reshape(2, GEN, feat_here)
    key_new = kv[:, :, 0]
    value_new = kv[:, :, 1]

    beam_request = beam_ids // BEAMS
    beam_prompt = jnp.take(prompt_len, beam_request)
    page_ids = me * pages_here + jnp.arange(pages_here, dtype=jnp.int32)
    slot_ids = jnp.arange(slot_count, dtype=jnp.int32)
    slot_live = slot_ids[None, :] * PAGE < prompt_len[:, None]
    page_match = (
        (page_table[:, :, None] == page_ids[None, None, :]) & slot_live[:, :, None]
    ).astype(jnp.int32)
    request_ids = jnp.arange(requests, dtype=jnp.int32)
    page_request = jnp.sum(page_match * request_ids[:, None, None], axis=(0, 1))
    page_slot = jnp.sum(page_match * slot_ids[None, :, None], axis=(0, 1))
    page_used = jnp.sum(page_match, axis=(0, 1)) > 0
    token_pos = (page_slot[:, None] * PAGE + jnp.arange(PAGE, dtype=jnp.int32)[None, :]).reshape(-1)
    token_request = jnp.repeat(page_request, PAGE)
    token_used = jnp.repeat(page_used, PAGE)
    prefix_live = (
        token_used[None, :]
        & (token_request[None, :] == beam_request[:, None])
        & (token_pos[None, :] < beam_prompt[:, None])
    )
    page_keys = prefix_keys.reshape(pages_here * PAGE, heads_here, HEAD_DIM)
    page_values = prefix_values.reshape(pages_here * PAGE, heads_here, HEAD_DIM)
    flat_queries = queries.reshape(rows, heads_here, HEAD_DIM)
    prompt_scores = (
        jnp.einsum("rhd,thd->rht", flat_queries, page_keys, preferred_element_type=jnp.float32)
        * score_scale
    ).reshape(steps, batch, heads_here, -1)
    prompt_live = prefix_live[None, :, None, :]
    prompt_top = jnp.max(jnp.where(prompt_live, prompt_scores, MASKED), axis=3)

    group_origin = lax.dynamic_slice_in_dim(origin, first_beam, BEAMS, axis=1)
    own_keys = suffix_keys[0].reshape(GEN, heads_here, HEAD_DIM)
    own_values = suffix_values[0].reshape(GEN, heads_here, HEAD_DIM)
    cache_scores = (
        jnp.einsum("sbhd,jhd->sbhj", group_queries, own_keys, preferred_element_type=jnp.float32)
        * score_scale
    )
    gen_rows = jnp.arange(GEN, dtype=jnp.int32)
    cache_live = (group_origin == me)[:, :, None, None] & (gen_rows < my_gen)[None, None, None, :]
    cache_top = jnp.max(jnp.where(cache_live, cache_scores, MASKED), axis=3)

    own_beam = me
    own_queries = lax.dynamic_index_in_dim(group_queries, member, axis=1, keepdims=False)
    new_src = jnp.stack(
        [jnp.stack([anc[(t, s)][own_beam] if t <= s else own_beam for t in range(steps)]) for s in range(steps)]
    ) - first_beam
    step_ids = jnp.arange(steps, dtype=jnp.int32)
    new_keys_here = key_new[step_ids[None, :], new_src].reshape(steps, steps, heads_here, HEAD_DIM)
    new_values_here = value_new[step_ids[None, :], new_src].reshape(steps, steps, heads_here, HEAD_DIM)
    new_scores = (
        jnp.einsum("shd,sthd->sht", own_queries, new_keys_here, preferred_element_type=jnp.float32)
        * score_scale
    )
    new_live = (step_ids[None, :] <= step_ids[:, None])[:, None, :]
    new_top = jnp.max(jnp.where(new_live, new_scores, MASKED), axis=2)

    local_top = prompt_top
    group_top = jnp.maximum(
        lax.dynamic_slice_in_dim(local_top, first_beam, BEAMS, axis=1), cache_top
    )
    local_top = lax.dynamic_update_slice_in_dim(local_top, group_top, first_beam, axis=1)
    own_top = jnp.maximum(lax.dynamic_index_in_dim(local_top, own_beam, axis=1, keepdims=True), new_top[:, None])
    local_top = lax.dynamic_update_slice_in_dim(local_top, own_top, own_beam, axis=1)
    top = all_combine(local_top, BLK_PARTS, jnp.max)

    prompt_weights = jnp.where(
        prompt_live, jnp.exp(prompt_scores - top[:, :, :, None]), 0.0
    ).astype(jnp.bfloat16)
    weighted = jnp.einsum(
        "rht,thd->rhd",
        prompt_weights.reshape(rows, heads_here, -1),
        page_values,
        preferred_element_type=jnp.float32,
    ).reshape(steps, batch, heads_here, HEAD_DIM)
    totals = jnp.sum(prompt_weights.astype(jnp.float32), axis=3)

    group_top_all = lax.dynamic_slice_in_dim(top, first_beam, BEAMS, axis=1)
    cache_weights = jnp.where(
        cache_live, jnp.exp(cache_scores - group_top_all[:, :, :, None]), 0.0
    ).astype(jnp.bfloat16)
    cache_weighted = jnp.einsum(
        "sbhj,jhd->sbhd", cache_weights, own_values, preferred_element_type=jnp.float32
    )
    cache_totals = jnp.sum(cache_weights.astype(jnp.float32), axis=3)

    own_top_all = lax.dynamic_index_in_dim(top, own_beam, axis=1, keepdims=False)
    new_weights = jnp.where(
        new_live, jnp.exp(new_scores - own_top_all[:, :, None]), 0.0
    ).astype(jnp.bfloat16)
    new_weighted = jnp.einsum(
        "sht,sthd->shd", new_weights, new_values_here, preferred_element_type=jnp.float32
    )
    new_totals = jnp.sum(new_weights.astype(jnp.float32), axis=2)

    group_weighted = lax.dynamic_slice_in_dim(weighted, first_beam, BEAMS, axis=1) + cache_weighted
    weighted = lax.dynamic_update_slice_in_dim(weighted, group_weighted, first_beam, axis=1)
    group_totals = lax.dynamic_slice_in_dim(totals, first_beam, BEAMS, axis=1) + cache_totals
    totals = lax.dynamic_update_slice_in_dim(totals, group_totals, first_beam, axis=1)
    own_weighted = lax.dynamic_index_in_dim(weighted, own_beam, axis=1, keepdims=True) + new_weighted[:, None]
    weighted = lax.dynamic_update_slice_in_dim(weighted, own_weighted, own_beam, axis=1)
    own_totals = lax.dynamic_index_in_dim(totals, own_beam, axis=1, keepdims=True) + new_totals[:, None]
    totals = lax.dynamic_update_slice_in_dim(totals, own_totals, own_beam, axis=1)

    packed = jnp.concatenate(
        [
            weighted.reshape(rows, feat_here),
            jnp.pad(totals.reshape(rows, heads_here), ((0, 0), (0, lanes - heads_here))),
        ],
        axis=1,
    )
    blk_stages = BLK_PARTS
    packed = scatter_sum(packed, blk_stages)
    part_rows = packed.shape[0]
    weighted = packed[:, :feat_here].reshape(part_rows, heads_here, HEAD_DIM)
    totals = packed[:, feat_here : feat_here + heads_here]
    attention = (weighted / totals[:, :, None]).reshape(part_rows, feat_here).astype(jnp.bfloat16)
    attention = gather_rows(attention, blk_stages)
    head_terms = jnp.dot(attention, w_out, preferred_element_type=jnp.float32)
    head_stages = ("head",)
    head_total = butterfly_sum(head_terms, "head")
    hidden = (head_total + b_out.astype(jnp.float32)[None, :]).astype(jnp.bfloat16)
    hidden = hidden.reshape(steps, batch, -1)

    my_final_src = [anc[(t, steps - 1)][own_beam] - first_beam for t in range(steps)]
    write_rows = my_gen + step_ids
    hit = gen_rows[:, None] == write_rows[None, :]
    chosen = jnp.argmax(hit, axis=1)
    written = jnp.any(hit, axis=1)[:, None]

    def finish(cache, fresh):
        new_rows = jnp.stack([fresh[t, my_final_src[t]] for t in range(steps)])
        return jnp.where(written, jnp.take(new_rows, chosen, axis=0), cache)[None]

    final_keys = finish(back[0], key_new)
    final_values = finish(back[1], value_new)
    return hidden, final_keys, final_values


def solution(mesh):
    heads = mesh.shape["head"]
    blocks = mesh.shape["blk"]
    cores = 2
    group_chips = BEAMS // cores
    devices = np.asarray(mesh.devices).reshape(heads, blocks // BEAMS, group_chips, cores)
    fine = Mesh(devices, ("head",) + BLK_PARTS)
    blk = BLK_PARTS
    in_specs = (
        P(None, None, blk),
        P(blk),
        P(blk),
        P(blk, "head"),
        P(blk, "head"),
        P(blk, "head"),
        P("head"),
        P("head"),
        P("head"),
        P("head", blk),
        P(blk),
        P(blk, None, "head"),
        P(blk, None, "head"),
        P(blk, None, "head"),
        P(blk, None, "head"),
        P(),
        P(),
        P(),
        P(),
    )
    out_specs = (P(None, None, blk), P(blk, None, "head"), P(blk, None, "head"))
    return jax.shard_map(body, mesh=fine, in_specs=in_specs, out_specs=out_specs, check_vma=False)
```

```python
import math

import jax
import jax.numpy as jnp
import numpy as np
from jax import lax
from jax.sharding import Mesh
from jax.sharding import PartitionSpec as P

D = 7168
HEAD_DIM = 128
BEAMS = 8
PAGE = 16
GEN = 256
STEPS = 4

MASKED = -1e30
NORM_EPSILON = 1e-05

BLK_PARTS = ("z", "x", "core")
GROUP = ("x", "core")


def nested(reduce, value):
    for axis in reversed(BLK_PARTS):
        value = reduce(value, axis)
    return value


def axes_size(axes):
    size = 1
    for axis in axes:
        size *= lax.axis_size(axis)
    return size


def scatter_sum(value, axes):
    n = axes_size(axes)
    got = lax.all_to_all(value, axes, 0, 0, tiled=True)
    return jnp.sum(got.reshape((n, value.shape[0] // n) + value.shape[1:]), axis=0)


def gather_rows(value, axes):
    n = axes_size(axes)
    copies = jnp.broadcast_to(value[None], (n,) + value.shape).reshape((n * value.shape[0],) + value.shape[1:])
    return lax.all_to_all(copies, axes, 0, 0, tiled=True)


def all_combine(value, axes, combine):
    n = axes_size(axes)
    got = gather_rows(value[None], axes)
    return combine(got.reshape((n,) + value.shape), axis=0)


def butterfly_sum(value, axis):
    bit = 1
    while bit < lax.axis_size(axis):
        value = value + lax.ppermute(value, axis, [(i, i ^ bit) for i in range(lax.axis_size(axis))])
        bit *= 2
    return value


def blk_index():
    index = lax.axis_index("z")
    for axis in BLK_PARTS[1:]:
        index = index * lax.axis_size(axis) + lax.axis_index(axis)
    return index


def body(
    inputs,
    ln_gain,
    ln_bias,
    w_query,
    w_key,
    w_value,
    b_query,
    b_key,
    b_value,
    w_out,
    b_out,
    prefix_keys,
    prefix_values,
    suffix_keys,
    suffix_values,
    page_table,
    prompt_len,
    gen_len,
    parents,
):
    me = blk_index()
    group = axes_size(GROUP)
    member = lax.axis_index("x") * lax.axis_size("core") + lax.axis_index("core")
    steps = inputs.shape[0]
    batch = inputs.shape[1]
    feat_local = inputs.shape[2]
    feat_here = w_query.shape[1]
    heads_here = feat_here // HEAD_DIM
    pages_here = prefix_keys.shape[0]
    requests = page_table.shape[0]
    slot_count = page_table.shape[1]
    rows = steps * batch
    score_scale = 1.0 / math.sqrt(HEAD_DIM)
    my_request = me // BEAMS
    first_beam = my_request * BEAMS
    my_gen = gen_len[my_request]
    cols_all = 3 * feat_here
    col_block = cols_all // group
    chunk_rows = GEN // group

    beam_ids = jnp.arange(batch, dtype=jnp.int32)
    anc = {}
    for s in range(steps):
        x = beam_ids
        anc[(s, s)] = x
        for t in range(s, -1, -1):
            x = jnp.take(parents[t], x)
            anc[(t - 1, s)] = x
    origin = jnp.stack([anc[(-1, s)] for s in range(steps)])

    rows_local = inputs.astype(jnp.float32).reshape(rows, feat_local)
    stats = jnp.stack([jnp.sum(rows_local, axis=1), jnp.sum(rows_local * rows_local, axis=1)], axis=1)
    stats = all_combine(stats, BLK_PARTS, jnp.sum)
    row_mean = stats[:, 0] / D
    variance = stats[:, 1] / D - row_mean * row_mean

    lanes = 128
    cw = feat_here // group
    weight_chunks = jnp.stack([w_query, w_key, w_value], axis=1).reshape(feat_local, 3, group, cw)
    weight_chunks = weight_chunks.transpose(2, 0, 1, 3).reshape(group, -1)
    norm_params = jnp.concatenate([ln_gain, ln_bias])
    pad = -(inputs.size + norm_params.shape[0]) % lanes
    row_block = jnp.concatenate([inputs.reshape(-1), norm_params, jnp.zeros((pad,), inputs.dtype)])
    cache_chunks = jnp.concatenate(
        [suffix_keys[0].reshape(group, -1), suffix_values[0].reshape(group, -1)], axis=1
    )
    sent = jnp.concatenate(
        [weight_chunks, jnp.broadcast_to(row_block[None], (group, row_block.shape[0])), cache_chunks], axis=1
    )
    sent = sent.reshape(group, -1, lanes)
    got = lax.all_to_all(sent, GROUP, 0, 0, tiled=True).reshape(group, -1)
    n_w = feat_local * 3 * cw
    n_in = rows * feat_local
    n_row = row_block.shape[0]
    w_group = got[:, :n_w].reshape(group, feat_local, 3, cw)
    in_group = got[:, n_w : n_w + n_in].reshape(group, rows, feat_local).astype(jnp.float32)
    gain_group = got[:, n_w + n_in : n_w + n_in + feat_local].astype(jnp.float32)
    shift_group = got[:, n_w + n_in + feat_local : n_w + n_in + 2 * feat_local].astype(jnp.float32)
    spread = got[:, n_w + n_row :].reshape(group, 2, chunk_rows, feat_here)

    normed = (
        (in_group - row_mean[None, :, None]) * lax.rsqrt(variance + NORM_EPSILON)[None, :, None]
        * gain_group[:, None, :]
        + shift_group[:, None, :]
    ).astype(jnp.bfloat16)
    partial = jnp.einsum("grf,gfwc->rwc", normed, w_group, preferred_element_type=jnp.float32)
    summed = butterfly_sum(partial, "z")
    bias_all = jnp.stack([b_query, b_key, b_value]).astype(jnp.float32).reshape(3, group, cw)
    bias_block = lax.dynamic_index_in_dim(bias_all, member, axis=1, keepdims=False)
    mine = (summed + bias_block).astype(jnp.bfloat16)
    q_block = mine[:, 0, :]
    kv_mine = lax.dynamic_index_in_dim(
        mine.reshape(steps, requests, BEAMS, 3, cw), my_request, axis=1, keepdims=False)[:, :, 1:, :]

    final_origin = origin[steps - 1]
    pick = lax.dynamic_slice_in_dim(final_origin, first_beam, BEAMS) - first_beam
    picked = jnp.take(spread, pick, axis=0).reshape(group, -1)

    n_q = rows * cw
    n_kv = steps * BEAMS * 2 * cw
    copies = jnp.concatenate([q_block.reshape(-1), kv_mine.reshape(-1)])
    sent2 = jnp.concatenate([jnp.broadcast_to(copies[None], (group, n_q + n_kv)), picked], axis=1)
    sent2 = sent2.reshape(group, -1, lanes)
    got2 = lax.all_to_all(sent2, GROUP, 0, 0, tiled=True).reshape(group, -1)
    queries = got2[:, :n_q].reshape(group, steps, batch, cw).transpose(1, 2, 0, 3).reshape(
        steps, batch, heads_here, HEAD_DIM)
    group_queries = lax.dynamic_slice_in_dim(queries, first_beam, BEAMS, axis=1)
    kv = got2[:, n_q : n_q + n_kv].reshape(group, steps, BEAMS, 2, cw).transpose(1, 2, 3, 0, 4).reshape(
        steps, BEAMS, 2, feat_here)
    back = got2[:, n_q + n_kv :].reshape(group, 2, chunk_rows, feat_here).transpose(1, 0, 2, 3).reshape(
        2, GEN, feat_here)
    key_new = kv[:, :, 0]
    value_new = kv[:, :, 1]

    beam_request = beam_ids // BEAMS
    beam_prompt = jnp.take(prompt_len, beam_request)
    page_ids = me * pages_here + jnp.arange(pages_here, dtype=jnp.int32)
    slot_ids = jnp.arange(slot_count, dtype=jnp.int32)
    slot_live = slot_ids[None, :] * PAGE < prompt_len[:, None]
    page_match = (
        (page_table[:, :, None] == page_ids[None, None, :]) & slot_live[:, :, None]
    ).astype(jnp.int32)
    request_ids = jnp.arange(requests, dtype=jnp.int32)
    page_request = jnp.sum(page_match * request_ids[:, None, None], axis=(0, 1))
    page_slot = jnp.sum(page_match * slot_ids[None, :, None], axis=(0, 1))
    page_used = jnp.sum(page_match, axis=(0, 1)) > 0
    token_pos = (page_slot[:, None] * PAGE + jnp.arange(PAGE, dtype=jnp.int32)[None, :]).reshape(-1)
    token_request = jnp.repeat(page_request, PAGE)
    token_used = jnp.repeat(page_used, PAGE)
    prefix_live = (
        token_used[None, :]
        & (token_request[None, :] == beam_request[:, None])
        & (token_pos[None, :] < beam_prompt[:, None])
    )
    page_keys = prefix_keys.reshape(pages_here * PAGE, heads_here, HEAD_DIM)
    page_values = prefix_values.reshape(pages_here * PAGE, heads_here, HEAD_DIM)
    flat_queries = queries.reshape(rows, heads_here, HEAD_DIM)
    prompt_scores = (
        jnp.einsum("rhd,thd->rht", flat_queries, page_keys, preferred_element_type=jnp.float32)
        * score_scale
    ).reshape(steps, batch, heads_here, -1)
    prompt_live = prefix_live[None, :, None, :]
    prompt_top = jnp.max(jnp.where(prompt_live, prompt_scores, MASKED), axis=3)

    group_origin = lax.dynamic_slice_in_dim(origin, first_beam, BEAMS, axis=1)
    own_keys = suffix_keys[0].reshape(GEN, heads_here, HEAD_DIM)
    own_values = suffix_values[0].reshape(GEN, heads_here, HEAD_DIM)
    cache_scores = (
        jnp.einsum("sbhd,jhd->sbhj", group_queries, own_keys, preferred_element_type=jnp.float32)
        * score_scale
    )
    gen_rows = jnp.arange(GEN, dtype=jnp.int32)
    cache_live = (group_origin == me)[:, :, None, None] & (gen_rows < my_gen)[None, None, None, :]
    cache_top = jnp.max(jnp.where(cache_live, cache_scores, MASKED), axis=3)

    own_beam = me
    own_queries = lax.dynamic_index_in_dim(group_queries, member, axis=1, keepdims=False)
    new_src = jnp.stack(
        [jnp.stack([anc[(t, s)][own_beam] if t <= s else own_beam for t in range(steps)]) for s in range(steps)]
    ) - first_beam
    step_ids = jnp.arange(steps, dtype=jnp.int32)
    new_keys_here = key_new[step_ids[None, :], new_src].reshape(steps, steps, heads_here, HEAD_DIM)
    new_values_here = value_new[step_ids[None, :], new_src].reshape(steps, steps, heads_here, HEAD_DIM)
    new_scores = (
        jnp.einsum("shd,sthd->sht", own_queries, new_keys_here, preferred_element_type=jnp.float32)
        * score_scale
    )
    new_live = (step_ids[None, :] <= step_ids[:, None])[:, None, :]
    new_top = jnp.max(jnp.where(new_live, new_scores, MASKED), axis=2)

    local_top = prompt_top
    group_top = jnp.maximum(
        lax.dynamic_slice_in_dim(local_top, first_beam, BEAMS, axis=1), cache_top
    )
    local_top = lax.dynamic_update_slice_in_dim(local_top, group_top, first_beam, axis=1)
    own_top = jnp.maximum(lax.dynamic_index_in_dim(local_top, own_beam, axis=1, keepdims=True), new_top[:, None])
    local_top = lax.dynamic_update_slice_in_dim(local_top, own_top, own_beam, axis=1)
    top = all_combine(local_top, BLK_PARTS, jnp.max)

    prompt_weights = jnp.where(
        prompt_live, jnp.exp(prompt_scores - top[:, :, :, None]), 0.0
    ).astype(jnp.bfloat16)
    weighted = jnp.einsum(
        "rht,thd->rhd",
        prompt_weights.reshape(rows, heads_here, -1),
        page_values,
        preferred_element_type=jnp.float32,
    ).reshape(steps, batch, heads_here, HEAD_DIM)
    totals = jnp.sum(prompt_weights.astype(jnp.float32), axis=3)

    group_top_all = lax.dynamic_slice_in_dim(top, first_beam, BEAMS, axis=1)
    cache_weights = jnp.where(
        cache_live, jnp.exp(cache_scores - group_top_all[:, :, :, None]), 0.0
    ).astype(jnp.bfloat16)
    cache_weighted = jnp.einsum(
        "sbhj,jhd->sbhd", cache_weights, own_values, preferred_element_type=jnp.float32
    )
    cache_totals = jnp.sum(cache_weights.astype(jnp.float32), axis=3)

    own_top_all = lax.dynamic_index_in_dim(top, own_beam, axis=1, keepdims=False)
    new_weights = jnp.where(
        new_live, jnp.exp(new_scores - own_top_all[:, :, None]), 0.0
    ).astype(jnp.bfloat16)
    new_weighted = jnp.einsum(
        "sht,sthd->shd", new_weights, new_values_here, preferred_element_type=jnp.float32
    )
    new_totals = jnp.sum(new_weights.astype(jnp.float32), axis=2)

    group_weighted = lax.dynamic_slice_in_dim(weighted, first_beam, BEAMS, axis=1) + cache_weighted
    weighted = lax.dynamic_update_slice_in_dim(weighted, group_weighted, first_beam, axis=1)
    group_totals = lax.dynamic_slice_in_dim(totals, first_beam, BEAMS, axis=1) + cache_totals
    totals = lax.dynamic_update_slice_in_dim(totals, group_totals, first_beam, axis=1)
    own_weighted = lax.dynamic_index_in_dim(weighted, own_beam, axis=1, keepdims=True) + new_weighted[:, None]
    weighted = lax.dynamic_update_slice_in_dim(weighted, own_weighted, own_beam, axis=1)
    own_totals = lax.dynamic_index_in_dim(totals, own_beam, axis=1, keepdims=True) + new_totals[:, None]
    totals = lax.dynamic_update_slice_in_dim(totals, own_totals, own_beam, axis=1)

    packed = jnp.concatenate(
        [
            weighted.reshape(rows, feat_here),
            jnp.pad(totals.reshape(rows, heads_here), ((0, 0), (0, lanes - heads_here))),
        ],
        axis=1,
    )
    blk_stages = BLK_PARTS
    packed = scatter_sum(packed, blk_stages)
    part_rows = packed.shape[0]
    weighted = packed[:, :feat_here].reshape(part_rows, heads_here, HEAD_DIM)
    totals = packed[:, feat_here : feat_here + heads_here]
    attention = (weighted / totals[:, :, None]).reshape(part_rows, feat_here).astype(jnp.bfloat16)
    attention = gather_rows(attention, blk_stages)
    head_terms = jnp.dot(attention, w_out, preferred_element_type=jnp.float32)
    head_stages = ("head",)
    head_total = butterfly_sum(head_terms, "head")
    hidden = (head_total + b_out.astype(jnp.float32)[None, :]).astype(jnp.bfloat16)
    hidden = hidden.reshape(steps, batch, -1)

    my_final_src = [anc[(t, steps - 1)][own_beam] - first_beam for t in range(steps)]
    write_rows = my_gen + step_ids
    hit = gen_rows[:, None] == write_rows[None, :]
    chosen = jnp.argmax(hit, axis=1)
    written = jnp.any(hit, axis=1)[:, None]

    def finish(cache, fresh):
        new_rows = jnp.stack([fresh[t, my_final_src[t]] for t in range(steps)])
        return jnp.where(written, jnp.take(new_rows, chosen, axis=0), cache)[None]

    final_keys = finish(back[0], key_new)
    final_values = finish(back[1], value_new)
    return hidden, final_keys, final_values


def solution(mesh):
    heads = mesh.shape["head"]
    blocks = mesh.shape["blk"]
    cores = 2
    group_chips = BEAMS // cores
    devices = np.asarray(mesh.devices).reshape(heads, blocks // BEAMS, group_chips, cores)
    fine = Mesh(devices, ("head",) + BLK_PARTS)
    blk = BLK_PARTS
    in_specs = (
        P(None, None, blk),
        P(blk),
        P(blk),
        P(blk, "head"),
        P(blk, "head"),
        P(blk, "head"),
        P("head"),
        P("head"),
        P("head"),
        P("head", blk),
        P(blk),
        P(blk, None, "head"),
        P(blk, None, "head"),
        P(blk, None, "head"),
        P(blk, None, "head"),
        P(),
        P(),
        P(),
        P(),
    )
    out_specs = (P(None, None, blk), P(blk, None, "head"), P(blk, None, "head"))
    return jax.shard_map(body, mesh=fine, in_specs=in_specs, out_specs=out_specs, check_vma=False)
```

```python
import math

import jax
import jax.numpy as jnp
import numpy as np
from jax import lax
from jax.sharding import Mesh
from jax.sharding import PartitionSpec as P

D = 7168
HEAD_DIM = 128
BEAMS = 8
PAGE = 16
GEN = 256
STEPS = 4

MASKED = -1e30
NORM_EPSILON = 1e-05

BLK_PARTS = ("z", "x", "core")
GROUP = ("x", "core")


def nested(reduce, value):
    for axis in reversed(BLK_PARTS):
        value = reduce(value, axis)
    return value


def axes_size(axes):
    size = 1
    for axis in axes:
        size *= lax.axis_size(axis)
    return size


def scatter_sum(value, axes):
    n = axes_size(axes)
    got = lax.all_to_all(value, axes, 0, 0, tiled=True)
    return jnp.sum(got.reshape((n, value.shape[0] // n) + value.shape[1:]), axis=0)


def gather_rows(value, axes):
    n = axes_size(axes)
    copies = jnp.broadcast_to(value[None], (n,) + value.shape).reshape((n * value.shape[0],) + value.shape[1:])
    return lax.all_to_all(copies, axes, 0, 0, tiled=True)


def all_combine(value, axes, combine):
    n = axes_size(axes)
    got = gather_rows(value[None], axes)
    return combine(got.reshape((n,) + value.shape), axis=0)


def butterfly_sum(value, axis):
    bit = 1
    while bit < lax.axis_size(axis):
        value = value + lax.ppermute(value, axis, [(i, i ^ bit) for i in range(lax.axis_size(axis))])
        bit *= 2
    return value


def blk_index():
    index = lax.axis_index("z")
    for axis in BLK_PARTS[1:]:
        index = index * lax.axis_size(axis) + lax.axis_index(axis)
    return index


def body(
    inputs,
    ln_gain,
    ln_bias,
    w_query,
    w_key,
    w_value,
    b_query,
    b_key,
    b_value,
    w_out,
    b_out,
    prefix_keys,
    prefix_values,
    suffix_keys,
    suffix_values,
    page_table,
    prompt_len,
    gen_len,
    parents,
):
    me = blk_index()
    group = axes_size(GROUP)
    member = lax.axis_index("x") * lax.axis_size("core") + lax.axis_index("core")
    steps = inputs.shape[0]
    batch = inputs.shape[1]
    feat_local = inputs.shape[2]
    feat_here = w_query.shape[1]
    heads_here = feat_here // HEAD_DIM
    pages_here = prefix_keys.shape[0]
    requests = page_table.shape[0]
    slot_count = page_table.shape[1]
    rows = steps * batch
    score_scale = 1.0 / math.sqrt(HEAD_DIM)
    my_request = me // BEAMS
    first_beam = my_request * BEAMS
    my_gen = gen_len[my_request]
    cols_all = 3 * feat_here
    col_block = cols_all // group
    chunk_rows = GEN // group

    beam_ids = jnp.arange(batch, dtype=jnp.int32)
    anc = {}
    for s in range(steps):
        x = beam_ids
        anc[(s, s)] = x
        for t in range(s, -1, -1):
            x = jnp.take(parents[t], x)
            anc[(t - 1, s)] = x
    origin = jnp.stack([anc[(-1, s)] for s in range(steps)])

    beam_request = beam_ids // BEAMS
    beam_prompt = jnp.take(prompt_len, beam_request)
    page_ids = me * pages_here + jnp.arange(pages_here, dtype=jnp.int32)
    slot_ids = jnp.arange(slot_count, dtype=jnp.int32)
    slot_live = slot_ids[None, :] * PAGE < prompt_len[:, None]
    page_match = (
        (page_table[:, :, None] == page_ids[None, None, :]) & slot_live[:, :, None]
    ).astype(jnp.int32)
    request_ids = jnp.arange(requests, dtype=jnp.int32)
    page_request = jnp.sum(page_match * request_ids[:, None, None], axis=(0, 1))
    page_slot = jnp.sum(page_match * slot_ids[None, :, None], axis=(0, 1))
    page_used = jnp.sum(page_match, axis=(0, 1)) > 0
    token_pos = (page_slot[:, None] * PAGE + jnp.arange(PAGE, dtype=jnp.int32)[None, :]).reshape(-1)
    token_request = jnp.repeat(page_request, PAGE)
    token_used = jnp.repeat(page_used, PAGE)
    prefix_live = (
        token_used[None, :]
        & (token_request[None, :] == beam_request[:, None])
        & (token_pos[None, :] < beam_prompt[:, None])
    )
    own_beam = me
    new_src = jnp.stack(
        [jnp.stack([anc[(t, s)][own_beam] if t <= s else own_beam for t in range(steps)]) for s in range(steps)]
    ) - first_beam
    final_origin = origin[steps - 1]
    pick = lax.dynamic_slice_in_dim(final_origin, first_beam, BEAMS) - first_beam


    rows_local = inputs.astype(jnp.float32).reshape(rows, feat_local)
    stats = jnp.stack([jnp.sum(rows_local, axis=1), jnp.sum(rows_local * rows_local, axis=1)], axis=1)
    stats = all_combine(stats, BLK_PARTS, jnp.sum)
    row_mean = stats[:, 0] / D
    variance = stats[:, 1] / D - row_mean * row_mean

    lanes = 128
    cw = feat_here // group
    weight_chunks = jnp.stack([w_query, w_key, w_value], axis=1).reshape(feat_local, 3, group, cw)
    weight_chunks = weight_chunks.transpose(2, 0, 1, 3).reshape(group, -1)
    norm_params = jnp.concatenate([ln_gain, ln_bias])
    pad = -(inputs.size + norm_params.shape[0]) % lanes
    row_block = jnp.concatenate([inputs.reshape(-1), norm_params, jnp.zeros((pad,), inputs.dtype)])
    cache_chunks = jnp.concatenate(
        [suffix_keys[0].reshape(group, -1), suffix_values[0].reshape(group, -1)], axis=1
    )
    sent = jnp.concatenate(
        [weight_chunks, jnp.broadcast_to(row_block[None], (group, row_block.shape[0])), cache_chunks], axis=1
    )
    sent = sent.reshape(group, -1, lanes)
    got = lax.all_to_all(sent, GROUP, 0, 0, tiled=True).reshape(group, -1)
    got, origin, prefix_live, new_src, pick = lax.optimization_barrier((got, origin, prefix_live, new_src, pick))
    n_w = feat_local * 3 * cw
    n_in = rows * feat_local
    n_row = row_block.shape[0]
    w_group = got[:, :n_w].reshape(group, feat_local, 3, cw)
    in_group = got[:, n_w : n_w + n_in].reshape(group, rows, feat_local).astype(jnp.float32)
    gain_group = got[:, n_w + n_in : n_w + n_in + feat_local].astype(jnp.float32)
    shift_group = got[:, n_w + n_in + feat_local : n_w + n_in + 2 * feat_local].astype(jnp.float32)
    spread = got[:, n_w + n_row :].reshape(group, 2, chunk_rows, feat_here)

    normed = (
        (in_group - row_mean[None, :, None]) * lax.rsqrt(variance + NORM_EPSILON)[None, :, None]
        * gain_group[:, None, :]
        + shift_group[:, None, :]
    ).astype(jnp.bfloat16)
    partial = jnp.einsum("grf,gfwc->rwc", normed, w_group, preferred_element_type=jnp.float32)
    partial = partial.reshape(steps, requests, BEAMS, 3, cw).transpose(1, 0, 2, 3, 4)
    summed = jnp.sum(lax.all_to_all(partial, "z", 0, 0, tiled=True).reshape(
        (lax.axis_size("z"), steps, BEAMS, 3, cw)), axis=0)
    bias_all = jnp.stack([b_query, b_key, b_value]).astype(jnp.float32).reshape(3, group, cw)
    bias_block = lax.dynamic_index_in_dim(bias_all, member, axis=1, keepdims=False)
    mine = (summed + bias_block).astype(jnp.bfloat16)

    q_blocks = gather_rows(mine[None, :, :, 0, :], BLK_PARTS)
    queries = q_blocks.reshape(requests, group, steps, BEAMS, cw).transpose(2, 0, 3, 1, 4).reshape(
        steps, batch, heads_here, HEAD_DIM)
    group_queries = lax.dynamic_slice_in_dim(queries, first_beam, BEAMS, axis=1)

    picked = jnp.take(spread, pick, axis=0).reshape(group, -1)

    kv_mine = mine[:, :, 1:, :]
    n_mine = steps * BEAMS * 2 * cw
    sent2 = jnp.concatenate(
        [jnp.broadcast_to(kv_mine.reshape(1, -1), (group, n_mine)), picked], axis=1
    )
    got2 = lax.all_to_all(sent2, GROUP, 0, 0, tiled=True)
    kv = got2[:, :n_mine].reshape(group, steps, BEAMS, 2, cw).transpose(1, 2, 3, 0, 4).reshape(
        steps, BEAMS, 2, feat_here)
    back = got2[:, n_mine:].reshape(group, 2, chunk_rows, feat_here).transpose(1, 0, 2, 3).reshape(2, GEN, feat_here)
    key_new = kv[:, :, 0]
    value_new = kv[:, :, 1]

    page_keys = prefix_keys.reshape(pages_here * PAGE, heads_here, HEAD_DIM)
    page_values = prefix_values.reshape(pages_here * PAGE, heads_here, HEAD_DIM)
    flat_queries = queries.reshape(rows, heads_here, HEAD_DIM)
    prompt_scores = (
        jnp.einsum("rhd,thd->rht", flat_queries, page_keys, preferred_element_type=jnp.float32)
        * score_scale
    ).reshape(steps, batch, heads_here, -1)
    prompt_live = prefix_live[None, :, None, :]
    prompt_top = jnp.max(jnp.where(prompt_live, prompt_scores, MASKED), axis=3)

    group_origin = lax.dynamic_slice_in_dim(origin, first_beam, BEAMS, axis=1)
    own_keys = suffix_keys[0].reshape(GEN, heads_here, HEAD_DIM)
    own_values = suffix_values[0].reshape(GEN, heads_here, HEAD_DIM)
    cache_scores = (
        jnp.einsum("sbhd,jhd->sbhj", group_queries, own_keys, preferred_element_type=jnp.float32)
        * score_scale
    )
    gen_rows = jnp.arange(GEN, dtype=jnp.int32)
    cache_live = (group_origin == me)[:, :, None, None] & (gen_rows < my_gen)[None, None, None, :]
    cache_top = jnp.max(jnp.where(cache_live, cache_scores, MASKED), axis=3)

    own_queries = lax.dynamic_index_in_dim(group_queries, member, axis=1, keepdims=False)
    step_ids = jnp.arange(steps, dtype=jnp.int32)
    new_keys_here = key_new[step_ids[None, :], new_src].reshape(steps, steps, heads_here, HEAD_DIM)
    new_values_here = value_new[step_ids[None, :], new_src].reshape(steps, steps, heads_here, HEAD_DIM)
    new_scores = (
        jnp.einsum("shd,sthd->sht", own_queries, new_keys_here, preferred_element_type=jnp.float32)
        * score_scale
    )
    new_live = (step_ids[None, :] <= step_ids[:, None])[:, None, :]
    new_top = jnp.max(jnp.where(new_live, new_scores, MASKED), axis=2)

    local_top = prompt_top
    group_top = jnp.maximum(
        lax.dynamic_slice_in_dim(local_top, first_beam, BEAMS, axis=1), cache_top
    )
    local_top = lax.dynamic_update_slice_in_dim(local_top, group_top, first_beam, axis=1)
    own_top = jnp.maximum(lax.dynamic_index_in_dim(local_top, own_beam, axis=1, keepdims=True), new_top[:, None])
    local_top = lax.dynamic_update_slice_in_dim(local_top, own_top, own_beam, axis=1)
    top = all_combine(local_top, BLK_PARTS, jnp.max)

    prompt_weights = jnp.where(
        prompt_live, jnp.exp(prompt_scores - top[:, :, :, None]), 0.0
    ).astype(jnp.bfloat16)
    weighted = jnp.einsum(
        "rht,thd->rhd",
        prompt_weights.reshape(rows, heads_here, -1),
        page_values,
        preferred_element_type=jnp.float32,
    ).reshape(steps, batch, heads_here, HEAD_DIM)
    totals = jnp.sum(prompt_weights.astype(jnp.float32), axis=3)

    group_top_all = lax.dynamic_slice_in_dim(top, first_beam, BEAMS, axis=1)
    cache_weights = jnp.where(
        cache_live, jnp.exp(cache_scores - group_top_all[:, :, :, None]), 0.0
    ).astype(jnp.bfloat16)
    cache_weighted = jnp.einsum(
        "sbhj,jhd->sbhd", cache_weights, own_values, preferred_element_type=jnp.float32
    )
    cache_totals = jnp.sum(cache_weights.astype(jnp.float32), axis=3)

    own_top_all = lax.dynamic_index_in_dim(top, own_beam, axis=1, keepdims=False)
    new_weights = jnp.where(
        new_live, jnp.exp(new_scores - own_top_all[:, :, None]), 0.0
    ).astype(jnp.bfloat16)
    new_weighted = jnp.einsum(
        "sht,sthd->shd", new_weights, new_values_here, preferred_element_type=jnp.float32
    )
    new_totals = jnp.sum(new_weights.astype(jnp.float32), axis=2)

    group_weighted = lax.dynamic_slice_in_dim(weighted, first_beam, BEAMS, axis=1) + cache_weighted
    weighted = lax.dynamic_update_slice_in_dim(weighted, group_weighted, first_beam, axis=1)
    group_totals = lax.dynamic_slice_in_dim(totals, first_beam, BEAMS, axis=1) + cache_totals
    totals = lax.dynamic_update_slice_in_dim(totals, group_totals, first_beam, axis=1)
    own_weighted = lax.dynamic_index_in_dim(weighted, own_beam, axis=1, keepdims=True) + new_weighted[:, None]
    weighted = lax.dynamic_update_slice_in_dim(weighted, own_weighted, own_beam, axis=1)
    own_totals = lax.dynamic_index_in_dim(totals, own_beam, axis=1, keepdims=True) + new_totals[:, None]
    totals = lax.dynamic_update_slice_in_dim(totals, own_totals, own_beam, axis=1)

    packed = jnp.concatenate(
        [
            weighted.reshape(rows, feat_here),
            jnp.pad(totals.reshape(rows, heads_here), ((0, 0), (0, lanes - heads_here))),
        ],
        axis=1,
    )
    blk_stages = BLK_PARTS
    packed = scatter_sum(packed, blk_stages)
    part_rows = packed.shape[0]
    weighted = packed[:, :feat_here].reshape(part_rows, heads_here, HEAD_DIM)
    totals = packed[:, feat_here : feat_here + heads_here]
    attention = (weighted / totals[:, :, None]).reshape(part_rows, feat_here).astype(jnp.bfloat16)
    attention = gather_rows(attention, blk_stages)
    head_terms = jnp.dot(attention, w_out, preferred_element_type=jnp.float32)
    head_stages = ("head",)
    head_total = butterfly_sum(head_terms, "head")
    hidden = (head_total + b_out.astype(jnp.float32)[None, :]).astype(jnp.bfloat16)
    hidden = hidden.reshape(steps, batch, -1)

    my_final_src = [anc[(t, steps - 1)][own_beam] - first_beam for t in range(steps)]
    write_rows = my_gen + step_ids
    hit = gen_rows[:, None] == write_rows[None, :]
    chosen = jnp.argmax(hit, axis=1)
    written = jnp.any(hit, axis=1)[:, None]

    def finish(cache, fresh):
        new_rows = jnp.stack([fresh[t, my_final_src[t]] for t in range(steps)])
        return jnp.where(written, jnp.take(new_rows, chosen, axis=0), cache)[None]

    final_keys = finish(back[0], key_new)
    final_values = finish(back[1], value_new)
    return hidden, final_keys, final_values


def solution(mesh):
    heads = mesh.shape["head"]
    blocks = mesh.shape["blk"]
    cores = 2
    group_chips = BEAMS // cores
    devices = np.asarray(mesh.devices).reshape(heads, blocks // BEAMS, group_chips, cores)
    fine = Mesh(devices, ("head",) + BLK_PARTS)
    blk = BLK_PARTS
    in_specs = (
        P(None, None, blk),
        P(blk),
        P(blk),
        P(blk, "head"),
        P(blk, "head"),
        P(blk, "head"),
        P("head"),
        P("head"),
        P("head"),
        P("head", blk),
        P(blk),
        P(blk, None, "head"),
        P(blk, None, "head"),
        P(blk, None, "head"),
        P(blk, None, "head"),
        P(),
        P(),
        P(),
        P(),
    )
    out_specs = (P(None, None, blk), P(blk, None, "head"), P(blk, None, "head"))
    return jax.shard_map(body, mesh=fine, in_specs=in_specs, out_specs=out_specs, check_vma=False)
```

```python
import math

import jax
import jax.numpy as jnp
import numpy as np
from jax import lax
from jax.sharding import Mesh
from jax.sharding import PartitionSpec as P

D = 7168
HEAD_DIM = 128
BEAMS = 8
PAGE = 16
GEN = 256
STEPS = 4

MASKED = -1e30
NORM_EPSILON = 1e-05

BLK_PARTS = ("z", "x", "core")
GROUP = ("x", "core")


def nested(reduce, value):
    for axis in reversed(BLK_PARTS):
        value = reduce(value, axis)
    return value


def axes_size(axes):
    size = 1
    for axis in axes:
        size *= lax.axis_size(axis)
    return size


def scatter_sum(value, axes):
    n = axes_size(axes)
    got = lax.all_to_all(value, axes, 0, 0, tiled=True)
    return jnp.sum(got.reshape((n, value.shape[0] // n) + value.shape[1:]), axis=0)


def gather_rows(value, axes):
    n = axes_size(axes)
    copies = jnp.broadcast_to(value[None], (n,) + value.shape).reshape((n * value.shape[0],) + value.shape[1:])
    return lax.all_to_all(copies, axes, 0, 0, tiled=True)


def all_combine(value, axes, combine):
    n = axes_size(axes)
    got = gather_rows(value[None], axes)
    return combine(got.reshape((n,) + value.shape), axis=0)


def butterfly_sum(value, axis):
    bit = 1
    while bit < lax.axis_size(axis):
        value = value + lax.ppermute(value, axis, [(i, i ^ bit) for i in range(lax.axis_size(axis))])
        bit *= 2
    return value


def blk_index():
    index = lax.axis_index("z")
    for axis in BLK_PARTS[1:]:
        index = index * lax.axis_size(axis) + lax.axis_index(axis)
    return index


def body(
    inputs,
    ln_gain,
    ln_bias,
    w_query,
    w_key,
    w_value,
    b_query,
    b_key,
    b_value,
    w_out,
    b_out,
    prefix_keys,
    prefix_values,
    suffix_keys,
    suffix_values,
    page_table,
    prompt_len,
    gen_len,
    parents,
):
    me = blk_index()
    group = axes_size(GROUP)
    member = lax.axis_index("x") * lax.axis_size("core") + lax.axis_index("core")
    steps = inputs.shape[0]
    batch = inputs.shape[1]
    feat_local = inputs.shape[2]
    feat_here = w_query.shape[1]
    heads_here = feat_here // HEAD_DIM
    pages_here = prefix_keys.shape[0]
    requests = page_table.shape[0]
    slot_count = page_table.shape[1]
    rows = steps * batch
    score_scale = 1.0 / math.sqrt(HEAD_DIM)
    my_request = me // BEAMS
    first_beam = my_request * BEAMS
    my_gen = gen_len[my_request]
    cols_all = 3 * feat_here
    col_block = cols_all // group
    chunk_rows = GEN // group

    beam_ids = jnp.arange(batch, dtype=jnp.int32)
    anc = {}
    for s in range(steps):
        x = beam_ids
        anc[(s, s)] = x
        for t in range(s, -1, -1):
            x = jnp.take(parents[t], x)
            anc[(t - 1, s)] = x
    origin = jnp.stack([anc[(-1, s)] for s in range(steps)])

    beam_request = beam_ids // BEAMS
    beam_prompt = jnp.take(prompt_len, beam_request)
    page_ids = me * pages_here + jnp.arange(pages_here, dtype=jnp.int32)
    slot_ids = jnp.arange(slot_count, dtype=jnp.int32)
    slot_live = slot_ids[None, :] * PAGE < prompt_len[:, None]
    page_match = (
        (page_table[:, :, None] == page_ids[None, None, :]) & slot_live[:, :, None]
    ).astype(jnp.int32)
    request_ids = jnp.arange(requests, dtype=jnp.int32)
    page_request = jnp.sum(page_match * request_ids[:, None, None], axis=(0, 1))
    page_slot = jnp.sum(page_match * slot_ids[None, :, None], axis=(0, 1))
    page_used = jnp.sum(page_match, axis=(0, 1)) > 0
    token_pos = (page_slot[:, None] * PAGE + jnp.arange(PAGE, dtype=jnp.int32)[None, :]).reshape(-1)
    token_request = jnp.repeat(page_request, PAGE)
    token_used = jnp.repeat(page_used, PAGE)
    prefix_live = (
        token_used[None, :]
        & (token_request[None, :] == beam_request[:, None])
        & (token_pos[None, :] < beam_prompt[:, None])
    )
    own_beam = me
    new_src = jnp.stack(
        [jnp.stack([anc[(t, s)][own_beam] if t <= s else own_beam for t in range(steps)]) for s in range(steps)]
    ) - first_beam
    final_origin = origin[steps - 1]
    pick = lax.dynamic_slice_in_dim(final_origin, first_beam, BEAMS) - first_beam


    rows_local = inputs.astype(jnp.float32).reshape(rows, feat_local)
    stats = jnp.stack([jnp.sum(rows_local, axis=1), jnp.sum(rows_local * rows_local, axis=1)], axis=1)
    stats = all_combine(stats, BLK_PARTS, jnp.sum)
    row_mean = stats[:, 0] / D
    variance = stats[:, 1] / D - row_mean * row_mean

    lanes = 128
    cw = feat_here // group
    weight_chunks = jnp.stack([w_query, w_key, w_value], axis=1).reshape(feat_local, 3, group, cw)
    weight_chunks = weight_chunks.transpose(2, 0, 1, 3).reshape(group, -1)
    norm_params = jnp.concatenate([ln_gain, ln_bias])
    pad = -(inputs.size + norm_params.shape[0]) % lanes
    row_block = jnp.concatenate([inputs.reshape(-1), norm_params, jnp.zeros((pad,), inputs.dtype)])
    cache_chunks = jnp.concatenate(
        [suffix_keys[0].reshape(group, -1), suffix_values[0].reshape(group, -1)], axis=1
    )
    sent = jnp.concatenate(
        [weight_chunks, jnp.broadcast_to(row_block[None], (group, row_block.shape[0])), cache_chunks], axis=1
    )
    sent = sent.reshape(group, -1, lanes)
    got = lax.all_to_all(sent, GROUP, 0, 0, tiled=True).reshape(group, -1)
    got, origin, prefix_live, new_src, pick = lax.optimization_barrier((got, origin, prefix_live, new_src, pick))
    n_w = feat_local * 3 * cw
    n_in = rows * feat_local
    n_row = row_block.shape[0]
    w_group = got[:, :n_w].reshape(group, feat_local, 3, cw)
    in_group = got[:, n_w : n_w + n_in].reshape(group, rows, feat_local).astype(jnp.float32)
    gain_group = got[:, n_w + n_in : n_w + n_in + feat_local].astype(jnp.float32)
    shift_group = got[:, n_w + n_in + feat_local : n_w + n_in + 2 * feat_local].astype(jnp.float32)
    spread = got[:, n_w + n_row :].reshape(group, 2, chunk_rows, feat_here)

    normed = (
        (in_group - row_mean[None, :, None]) * lax.rsqrt(variance + NORM_EPSILON)[None, :, None]
        * gain_group[:, None, :]
        + shift_group[:, None, :]
    ).astype(jnp.bfloat16)
    partial = jnp.einsum("grf,gfwc->rwc", normed, w_group, preferred_element_type=jnp.float32)
    partial = partial.reshape(steps, requests, BEAMS, 3, cw).transpose(1, 0, 2, 3, 4)
    summed = jnp.sum(lax.all_to_all(partial, "z", 0, 0, tiled=True).reshape(
        (lax.axis_size("z"), steps, BEAMS, 3, cw)), axis=0)
    bias_all = jnp.stack([b_query, b_key, b_value]).astype(jnp.float32).reshape(3, group, cw)
    bias_block = lax.dynamic_index_in_dim(bias_all, member, axis=1, keepdims=False)
    mine = (summed + bias_block).astype(jnp.bfloat16)

    q_blocks = gather_rows(mine[None, :, :, 0, :], BLK_PARTS)
    queries = q_blocks.reshape(requests, group, steps, BEAMS, cw).transpose(2, 0, 3, 1, 4).reshape(
        steps, batch, heads_here, HEAD_DIM)
    group_queries = lax.dynamic_slice_in_dim(queries, first_beam, BEAMS, axis=1)

    picked = jnp.take(spread, pick, axis=0).reshape(group, -1)

    kv_mine = mine[:, :, 1:, :]
    n_mine = steps * BEAMS * 2 * cw
    sent2 = jnp.concatenate(
        [jnp.broadcast_to(kv_mine.reshape(1, -1), (group, n_mine)), picked], axis=1
    )
    got2 = lax.all_to_all(sent2, GROUP, 0, 0, tiled=True)
    kv = got2[:, :n_mine].reshape(group, steps, BEAMS, 2, cw).transpose(1, 2, 3, 0, 4).reshape(
        steps, BEAMS, 2, feat_here)
    back = got2[:, n_mine:].reshape(group, 2, chunk_rows, feat_here).transpose(1, 0, 2, 3).reshape(2, GEN, feat_here)
    key_new = kv[:, :, 0]
    value_new = kv[:, :, 1]

    page_keys = prefix_keys.reshape(pages_here * PAGE, heads_here, HEAD_DIM)
    page_values = prefix_values.reshape(pages_here * PAGE, heads_here, HEAD_DIM)
    flat_queries = queries.reshape(rows, heads_here, HEAD_DIM)
    prompt_scores = (
        jnp.einsum("rhd,thd->rht", flat_queries, page_keys, preferred_element_type=jnp.float32)
        * score_scale
    ).reshape(steps, batch, heads_here, -1)
    prompt_live = prefix_live[None, :, None, :]
    prompt_top = jnp.max(jnp.where(prompt_live, prompt_scores, MASKED), axis=3)

    group_origin = lax.dynamic_slice_in_dim(origin, first_beam, BEAMS, axis=1)
    own_keys = suffix_keys[0].reshape(GEN, heads_here, HEAD_DIM)
    own_values = suffix_values[0].reshape(GEN, heads_here, HEAD_DIM)
    cache_scores = (
        jnp.einsum("sbhd,jhd->sbhj", group_queries, own_keys, preferred_element_type=jnp.float32)
        * score_scale
    )
    gen_rows = jnp.arange(GEN, dtype=jnp.int32)
    cache_live = (group_origin == me)[:, :, None, None] & (gen_rows < my_gen)[None, None, None, :]
    cache_top = jnp.max(jnp.where(cache_live, cache_scores, MASKED), axis=3)

    own_queries = lax.dynamic_index_in_dim(group_queries, member, axis=1, keepdims=False)
    step_ids = jnp.arange(steps, dtype=jnp.int32)
    new_keys_here = key_new[step_ids[None, :], new_src].reshape(steps, steps, heads_here, HEAD_DIM)
    new_values_here = value_new[step_ids[None, :], new_src].reshape(steps, steps, heads_here, HEAD_DIM)
    new_scores = (
        jnp.einsum("shd,sthd->sht", own_queries, new_keys_here, preferred_element_type=jnp.float32)
        * score_scale
    )
    new_live = (step_ids[None, :] <= step_ids[:, None])[:, None, :]
    new_top = jnp.max(jnp.where(new_live, new_scores, MASKED), axis=2)

    local_top = prompt_top
    group_top = jnp.maximum(
        lax.dynamic_slice_in_dim(local_top, first_beam, BEAMS, axis=1), cache_top
    )
    local_top = lax.dynamic_update_slice_in_dim(local_top, group_top, first_beam, axis=1)
    own_top = jnp.maximum(lax.dynamic_index_in_dim(local_top, own_beam, axis=1, keepdims=True), new_top[:, None])
    local_top = lax.dynamic_update_slice_in_dim(local_top, own_top, own_beam, axis=1)
    top = all_combine(local_top, BLK_PARTS, jnp.max)

    prompt_weights = jnp.where(
        prompt_live, jnp.exp(prompt_scores - top[:, :, :, None]), 0.0
    ).astype(jnp.bfloat16)
    weighted = jnp.einsum(
        "rht,thd->rhd",
        prompt_weights.reshape(rows, heads_here, -1),
        page_values,
        preferred_element_type=jnp.float32,
    ).reshape(steps, batch, heads_here, HEAD_DIM)
    totals = jnp.sum(prompt_weights.astype(jnp.float32), axis=3)

    group_top_all = lax.dynamic_slice_in_dim(top, first_beam, BEAMS, axis=1)
    cache_weights = jnp.where(
        cache_live, jnp.exp(cache_scores - group_top_all[:, :, :, None]), 0.0
    ).astype(jnp.bfloat16)
    cache_weighted = jnp.einsum(
        "sbhj,jhd->sbhd", cache_weights, own_values, preferred_element_type=jnp.float32
    )
    cache_totals = jnp.sum(cache_weights.astype(jnp.float32), axis=3)

    own_top_all = lax.dynamic_index_in_dim(top, own_beam, axis=1, keepdims=False)
    new_weights = jnp.where(
        new_live, jnp.exp(new_scores - own_top_all[:, :, None]), 0.0
    ).astype(jnp.bfloat16)
    new_weighted = jnp.einsum(
        "sht,sthd->shd", new_weights, new_values_here, preferred_element_type=jnp.float32
    )
    new_totals = jnp.sum(new_weights.astype(jnp.float32), axis=2)

    group_weighted = lax.dynamic_slice_in_dim(weighted, first_beam, BEAMS, axis=1) + cache_weighted
    weighted = lax.dynamic_update_slice_in_dim(weighted, group_weighted, first_beam, axis=1)
    group_totals = lax.dynamic_slice_in_dim(totals, first_beam, BEAMS, axis=1) + cache_totals
    totals = lax.dynamic_update_slice_in_dim(totals, group_totals, first_beam, axis=1)
    own_weighted = lax.dynamic_index_in_dim(weighted, own_beam, axis=1, keepdims=True) + new_weighted[:, None]
    weighted = lax.dynamic_update_slice_in_dim(weighted, own_weighted, own_beam, axis=1)
    own_totals = lax.dynamic_index_in_dim(totals, own_beam, axis=1, keepdims=True) + new_totals[:, None]
    totals = lax.dynamic_update_slice_in_dim(totals, own_totals, own_beam, axis=1)

    packed = jnp.concatenate(
        [
            weighted.reshape(rows, feat_here),
            jnp.pad(totals.reshape(rows, heads_here), ((0, 0), (0, lanes - heads_here))),
        ],
        axis=1,
    )
    blk_stages = BLK_PARTS
    packed = scatter_sum(packed, blk_stages)
    part_rows = packed.shape[0]
    weighted = packed[:, :feat_here].reshape(part_rows, heads_here, HEAD_DIM)
    totals = packed[:, feat_here : feat_here + heads_here]
    attention = (weighted / totals[:, :, None]).reshape(part_rows, feat_here).astype(jnp.bfloat16)
    attention = gather_rows(attention, blk_stages)
    head_terms = jnp.dot(attention, w_out, preferred_element_type=jnp.float32)
    head_stages = ("head",)
    head_part = scatter_sum(head_terms, head_stages)
    hidden = gather_rows((head_part + b_out.astype(jnp.float32)[None, :]).astype(jnp.bfloat16), head_stages)
    hidden = hidden.reshape(steps, batch, -1)

    my_final_src = [anc[(t, steps - 1)][own_beam] - first_beam for t in range(steps)]
    write_rows = my_gen + step_ids
    hit = gen_rows[:, None] == write_rows[None, :]
    chosen = jnp.argmax(hit, axis=1)
    written = jnp.any(hit, axis=1)[:, None]

    def finish(cache, fresh):
        new_rows = jnp.stack([fresh[t, my_final_src[t]] for t in range(steps)])
        return jnp.where(written, jnp.take(new_rows, chosen, axis=0), cache)[None]

    final_keys = finish(back[0], key_new)
    final_values = finish(back[1], value_new)
    return hidden, final_keys, final_values


def solution(mesh):
    heads = mesh.shape["head"]
    blocks = mesh.shape["blk"]
    cores = 2
    group_chips = BEAMS // cores
    devices = np.asarray(mesh.devices).reshape(heads, blocks // BEAMS, group_chips, cores)
    fine = Mesh(devices, ("head",) + BLK_PARTS)
    blk = BLK_PARTS
    in_specs = (
        P(None, None, blk),
        P(blk),
        P(blk),
        P(blk, "head"),
        P(blk, "head"),
        P(blk, "head"),
        P("head"),
        P("head"),
        P("head"),
        P("head", blk),
        P(blk),
        P(blk, None, "head"),
        P(blk, None, "head"),
        P(blk, None, "head"),
        P(blk, None, "head"),
        P(),
        P(),
        P(),
        P(),
    )
    out_specs = (P(None, None, blk), P(blk, None, "head"), P(blk, None, "head"))
    return jax.shard_map(body, mesh=fine, in_specs=in_specs, out_specs=out_specs, check_vma=False)
```

```python
import math

import jax
import jax.numpy as jnp
import numpy as np
from jax import lax
from jax.sharding import Mesh
from jax.sharding import PartitionSpec as P

D = 7168
HEAD_DIM = 128
BEAMS = 8
PAGE = 16
GEN = 256
STEPS = 4

MASKED = -1e30
NORM_EPSILON = 1e-05

BLK_PARTS = ("z", "x", "core")
GROUP = ("x", "core")


def nested(reduce, value):
    for axis in reversed(BLK_PARTS):
        value = reduce(value, axis)
    return value


def axes_size(axes):
    size = 1
    for axis in axes:
        size *= lax.axis_size(axis)
    return size


def scatter_sum(value, axes):
    n = axes_size(axes)
    got = lax.all_to_all(value, axes, 0, 0, tiled=True)
    return jnp.sum(got.reshape((n, value.shape[0] // n) + value.shape[1:]), axis=0)


def gather_rows(value, axes):
    n = axes_size(axes)
    copies = jnp.broadcast_to(value[None], (n,) + value.shape).reshape((n * value.shape[0],) + value.shape[1:])
    return lax.all_to_all(copies, axes, 0, 0, tiled=True)


def all_combine(value, axes, combine):
    n = axes_size(axes)
    got = gather_rows(value[None], axes)
    return combine(got.reshape((n,) + value.shape), axis=0)


def butterfly_sum(value, axis):
    bit = 1
    while bit < lax.axis_size(axis):
        value = value + lax.ppermute(value, axis, [(i, i ^ bit) for i in range(lax.axis_size(axis))])
        bit *= 2
    return value


def blk_index():
    index = lax.axis_index("z")
    for axis in BLK_PARTS[1:]:
        index = index * lax.axis_size(axis) + lax.axis_index(axis)
    return index


def body(
    inputs,
    ln_gain,
    ln_bias,
    w_query,
    w_key,
    w_value,
    b_query,
    b_key,
    b_value,
    w_out,
    b_out,
    prefix_keys,
    prefix_values,
    suffix_keys,
    suffix_values,
    page_table,
    prompt_len,
    gen_len,
    parents,
):
    me = blk_index()
    group = axes_size(GROUP)
    member = lax.axis_index("x") * lax.axis_size("core") + lax.axis_index("core")
    steps = inputs.shape[0]
    batch = inputs.shape[1]
    feat_local = inputs.shape[2]
    feat_here = w_query.shape[1]
    heads_here = feat_here // HEAD_DIM
    pages_here = prefix_keys.shape[0]
    requests = page_table.shape[0]
    slot_count = page_table.shape[1]
    rows = steps * batch
    score_scale = 1.0 / math.sqrt(HEAD_DIM)
    my_request = me // BEAMS
    first_beam = my_request * BEAMS
    my_gen = gen_len[my_request]
    cols_all = 3 * feat_here
    col_block = cols_all // group
    chunk_rows = GEN // group

    beam_ids = jnp.arange(batch, dtype=jnp.int32)
    anc = {}
    for s in range(steps):
        x = beam_ids
        anc[(s, s)] = x
        for t in range(s, -1, -1):
            x = jnp.take(parents[t], x)
            anc[(t - 1, s)] = x
    origin = jnp.stack([anc[(-1, s)] for s in range(steps)])

    beam_request = beam_ids // BEAMS
    beam_prompt = jnp.take(prompt_len, beam_request)
    page_ids = me * pages_here + jnp.arange(pages_here, dtype=jnp.int32)
    slot_ids = jnp.arange(slot_count, dtype=jnp.int32)
    slot_live = slot_ids[None, :] * PAGE < prompt_len[:, None]
    page_match = (
        (page_table[:, :, None] == page_ids[None, None, :]) & slot_live[:, :, None]
    ).astype(jnp.int32)
    request_ids = jnp.arange(requests, dtype=jnp.int32)
    page_request = jnp.sum(page_match * request_ids[:, None, None], axis=(0, 1))
    page_slot = jnp.sum(page_match * slot_ids[None, :, None], axis=(0, 1))
    page_used = jnp.sum(page_match, axis=(0, 1)) > 0
    token_pos = (page_slot[:, None] * PAGE + jnp.arange(PAGE, dtype=jnp.int32)[None, :]).reshape(-1)
    token_request = jnp.repeat(page_request, PAGE)
    token_used = jnp.repeat(page_used, PAGE)
    prefix_live = (
        token_used[None, :]
        & (token_request[None, :] == beam_request[:, None])
        & (token_pos[None, :] < beam_prompt[:, None])
    )
    own_beam = me
    new_src = jnp.stack(
        [jnp.stack([anc[(t, s)][own_beam] if t <= s else own_beam for t in range(steps)]) for s in range(steps)]
    ) - first_beam
    final_origin = origin[steps - 1]
    pick = lax.dynamic_slice_in_dim(final_origin, first_beam, BEAMS) - first_beam


    rows_local = inputs.astype(jnp.float32).reshape(rows, feat_local)
    stats = jnp.stack([jnp.sum(rows_local, axis=1), jnp.sum(rows_local * rows_local, axis=1)], axis=1)
    stats = all_combine(stats, BLK_PARTS, jnp.sum)
    row_mean = stats[:, 0] / D
    variance = stats[:, 1] / D - row_mean * row_mean

    lanes = 128
    cw = feat_here // group
    weight_chunks = jnp.stack([w_query, w_key, w_value], axis=1).reshape(feat_local, 3, group, cw)
    weight_chunks = weight_chunks.transpose(2, 0, 1, 3).reshape(group, -1)
    norm_params = jnp.concatenate([ln_gain, ln_bias])
    pad = -(inputs.size + norm_params.shape[0]) % lanes
    row_block = jnp.concatenate([inputs.reshape(-1), norm_params, jnp.zeros((pad,), inputs.dtype)])
    cache_chunks = jnp.concatenate(
        [suffix_keys[0].reshape(group, -1), suffix_values[0].reshape(group, -1)], axis=1
    )
    sent = jnp.concatenate(
        [weight_chunks, jnp.broadcast_to(row_block[None], (group, row_block.shape[0])), cache_chunks], axis=1
    )
    sent = sent.reshape(group, -1, lanes)
    got = lax.all_to_all(sent, GROUP, 0, 0, tiled=True).reshape(group, -1)
    got, origin, prefix_live, new_src, pick = lax.optimization_barrier((got, origin, prefix_live, new_src, pick))
    n_w = feat_local * 3 * cw
    n_in = rows * feat_local
    n_row = row_block.shape[0]
    w_group = got[:, :n_w].reshape(group, feat_local, 3, cw)
    in_group = got[:, n_w : n_w + n_in].reshape(group, rows, feat_local).astype(jnp.float32)
    gain_group = got[:, n_w + n_in : n_w + n_in + feat_local].astype(jnp.float32)
    shift_group = got[:, n_w + n_in + feat_local : n_w + n_in + 2 * feat_local].astype(jnp.float32)
    spread = got[:, n_w + n_row :].reshape(group, 2, chunk_rows, feat_here)

    normed = (
        (in_group - row_mean[None, :, None]) * lax.rsqrt(variance + NORM_EPSILON)[None, :, None]
        * gain_group[:, None, :]
        + shift_group[:, None, :]
    ).astype(jnp.bfloat16)
    partial = jnp.einsum("grf,gfwc->rwc", normed, w_group, preferred_element_type=jnp.float32)
    partial = partial.reshape(steps, requests, BEAMS, 3, cw).transpose(1, 0, 2, 3, 4)
    summed = jnp.sum(lax.all_to_all(partial, "z", 0, 0, tiled=True).reshape(
        (lax.axis_size("z"), steps, BEAMS, 3, cw)), axis=0)
    bias_all = jnp.stack([b_query, b_key, b_value]).astype(jnp.float32).reshape(3, group, cw)
    bias_block = lax.dynamic_index_in_dim(bias_all, member, axis=1, keepdims=False)
    mine = (summed + bias_block).astype(jnp.bfloat16)

    q_blocks = gather_rows(mine[None, :, :, 0, :], BLK_PARTS)
    queries = q_blocks.reshape(requests, group, steps, BEAMS, cw).transpose(2, 0, 3, 1, 4).reshape(
        steps, batch, heads_here, HEAD_DIM)
    group_queries = lax.dynamic_slice_in_dim(queries, first_beam, BEAMS, axis=1)

    picked = jnp.take(spread, pick, axis=0).reshape(group, -1)

    kv_mine = mine[:, :, 1:, :]
    n_mine = steps * BEAMS * 2 * cw
    sent2 = jnp.concatenate(
        [jnp.broadcast_to(kv_mine.reshape(1, -1), (group, n_mine)), picked], axis=1
    )
    got2 = lax.all_to_all(sent2, GROUP, 0, 0, tiled=True)
    kv = got2[:, :n_mine].reshape(group, steps, BEAMS, 2, cw).transpose(1, 2, 3, 0, 4).reshape(
        steps, BEAMS, 2, feat_here)
    back = got2[:, n_mine:].reshape(group, 2, chunk_rows, feat_here).transpose(1, 0, 2, 3).reshape(2, GEN, feat_here)
    key_new = kv[:, :, 0]
    value_new = kv[:, :, 1]

    page_keys = prefix_keys.reshape(pages_here * PAGE, heads_here, HEAD_DIM)
    page_values = prefix_values.reshape(pages_here * PAGE, heads_here, HEAD_DIM)
    flat_queries = queries.reshape(rows, heads_here, HEAD_DIM)
    prompt_scores = (
        jnp.einsum("rhd,thd->rht", flat_queries, page_keys, preferred_element_type=jnp.float32)
        * score_scale
    ).reshape(steps, batch, heads_here, -1)
    prompt_live = prefix_live[None, :, None, :]
    prompt_top = jnp.max(jnp.where(prompt_live, prompt_scores, MASKED), axis=3)

    group_origin = lax.dynamic_slice_in_dim(origin, first_beam, BEAMS, axis=1)
    own_keys = suffix_keys[0].reshape(GEN, heads_here, HEAD_DIM)
    own_values = suffix_values[0].reshape(GEN, heads_here, HEAD_DIM)
    cache_scores = (
        jnp.einsum("sbhd,jhd->sbhj", group_queries, own_keys, preferred_element_type=jnp.float32)
        * score_scale
    )
    gen_rows = jnp.arange(GEN, dtype=jnp.int32)
    cache_live = (group_origin == me)[:, :, None, None] & (gen_rows < my_gen)[None, None, None, :]
    cache_top = jnp.max(jnp.where(cache_live, cache_scores, MASKED), axis=3)

    own_queries = lax.dynamic_index_in_dim(group_queries, member, axis=1, keepdims=False)
    step_ids = jnp.arange(steps, dtype=jnp.int32)
    new_keys_here = key_new[step_ids[None, :], new_src].reshape(steps, steps, heads_here, HEAD_DIM)
    new_values_here = value_new[step_ids[None, :], new_src].reshape(steps, steps, heads_here, HEAD_DIM)
    new_scores = (
        jnp.einsum("shd,sthd->sht", own_queries, new_keys_here, preferred_element_type=jnp.float32)
        * score_scale
    )
    new_live = (step_ids[None, :] <= step_ids[:, None])[:, None, :]
    new_top = jnp.max(jnp.where(new_live, new_scores, MASKED), axis=2)

    local_top = prompt_top
    group_top = jnp.maximum(
        lax.dynamic_slice_in_dim(local_top, first_beam, BEAMS, axis=1), cache_top
    )
    local_top = lax.dynamic_update_slice_in_dim(local_top, group_top, first_beam, axis=1)
    own_top = jnp.maximum(lax.dynamic_index_in_dim(local_top, own_beam, axis=1, keepdims=True), new_top[:, None])
    local_top = lax.dynamic_update_slice_in_dim(local_top, own_top, own_beam, axis=1)
    n_blk = axes_size(BLK_PARTS)
    top_rows = local_top.reshape(rows, heads_here)
    top_part = jnp.max(lax.all_to_all(top_rows, BLK_PARTS, 0, 0, tiled=True).reshape(
        n_blk, rows // n_blk, heads_here), axis=0)
    top = gather_rows(top_part, BLK_PARTS).reshape(steps, batch, heads_here)

    prompt_weights = jnp.where(
        prompt_live, jnp.exp(prompt_scores - top[:, :, :, None]), 0.0
    ).astype(jnp.bfloat16)
    weighted = jnp.einsum(
        "rht,thd->rhd",
        prompt_weights.reshape(rows, heads_here, -1),
        page_values,
        preferred_element_type=jnp.float32,
    ).reshape(steps, batch, heads_here, HEAD_DIM)
    totals = jnp.sum(prompt_weights.astype(jnp.float32), axis=3)

    group_top_all = lax.dynamic_slice_in_dim(top, first_beam, BEAMS, axis=1)
    cache_weights = jnp.where(
        cache_live, jnp.exp(cache_scores - group_top_all[:, :, :, None]), 0.0
    ).astype(jnp.bfloat16)
    cache_weighted = jnp.einsum(
        "sbhj,jhd->sbhd", cache_weights, own_values, preferred_element_type=jnp.float32
    )
    cache_totals = jnp.sum(cache_weights.astype(jnp.float32), axis=3)

    own_top_all = lax.dynamic_index_in_dim(top, own_beam, axis=1, keepdims=False)
    new_weights = jnp.where(
        new_live, jnp.exp(new_scores - own_top_all[:, :, None]), 0.0
    ).astype(jnp.bfloat16)
    new_weighted = jnp.einsum(
        "sht,sthd->shd", new_weights, new_values_here, preferred_element_type=jnp.float32
    )
    new_totals = jnp.sum(new_weights.astype(jnp.float32), axis=2)

    group_weighted = lax.dynamic_slice_in_dim(weighted, first_beam, BEAMS, axis=1) + cache_weighted
    weighted = lax.dynamic_update_slice_in_dim(weighted, group_weighted, first_beam, axis=1)
    group_totals = lax.dynamic_slice_in_dim(totals, first_beam, BEAMS, axis=1) + cache_totals
    totals = lax.dynamic_update_slice_in_dim(totals, group_totals, first_beam, axis=1)
    own_weighted = lax.dynamic_index_in_dim(weighted, own_beam, axis=1, keepdims=True) + new_weighted[:, None]
    weighted = lax.dynamic_update_slice_in_dim(weighted, own_weighted, own_beam, axis=1)
    own_totals = lax.dynamic_index_in_dim(totals, own_beam, axis=1, keepdims=True) + new_totals[:, None]
    totals = lax.dynamic_update_slice_in_dim(totals, own_totals, own_beam, axis=1)

    packed = jnp.concatenate(
        [
            weighted.reshape(rows, feat_here),
            jnp.pad(totals.reshape(rows, heads_here), ((0, 0), (0, lanes - heads_here))),
        ],
        axis=1,
    )
    blk_stages = BLK_PARTS
    packed = scatter_sum(packed, blk_stages)
    part_rows = packed.shape[0]
    weighted = packed[:, :feat_here].reshape(part_rows, heads_here, HEAD_DIM)
    totals = packed[:, feat_here : feat_here + heads_here]
    attention = (weighted / totals[:, :, None]).reshape(part_rows, feat_here).astype(jnp.bfloat16)
    attention = gather_rows(attention, blk_stages)
    head_terms = jnp.dot(attention, w_out, preferred_element_type=jnp.float32)
    head_stages = ("head",)
    head_part = scatter_sum(head_terms, head_stages)
    hidden = gather_rows((head_part + b_out.astype(jnp.float32)[None, :]).astype(jnp.bfloat16), head_stages)
    hidden = hidden.reshape(steps, batch, -1)

    my_final_src = [anc[(t, steps - 1)][own_beam] - first_beam for t in range(steps)]
    write_rows = my_gen + step_ids
    hit = gen_rows[:, None] == write_rows[None, :]
    chosen = jnp.argmax(hit, axis=1)
    written = jnp.any(hit, axis=1)[:, None]

    def finish(cache, fresh):
        new_rows = jnp.stack([fresh[t, my_final_src[t]] for t in range(steps)])
        return jnp.where(written, jnp.take(new_rows, chosen, axis=0), cache)[None]

    final_keys = finish(back[0], key_new)
    final_values = finish(back[1], value_new)
    return hidden, final_keys, final_values


def solution(mesh):
    heads = mesh.shape["head"]
    blocks = mesh.shape["blk"]
    cores = 2
    group_chips = BEAMS // cores
    devices = np.asarray(mesh.devices).reshape(heads, blocks // BEAMS, group_chips, cores)
    fine = Mesh(devices, ("head",) + BLK_PARTS)
    blk = BLK_PARTS
    in_specs = (
        P(None, None, blk),
        P(blk),
        P(blk),
        P(blk, "head"),
        P(blk, "head"),
        P(blk, "head"),
        P("head"),
        P("head"),
        P("head"),
        P("head", blk),
        P(blk),
        P(blk, None, "head"),
        P(blk, None, "head"),
        P(blk, None, "head"),
        P(blk, None, "head"),
        P(),
        P(),
        P(),
        P(),
    )
    out_specs = (P(None, None, blk), P(blk, None, "head"), P(blk, None, "head"))
    return jax.shard_map(body, mesh=fine, in_specs=in_specs, out_specs=out_specs, check_vma=False)
```

```python
import math

import jax
import jax.numpy as jnp
import numpy as np
from jax import lax
from jax.sharding import Mesh
from jax.sharding import PartitionSpec as P

D = 7168
HEAD_DIM = 128
BEAMS = 8
PAGE = 16
GEN = 256
STEPS = 4

MASKED = -1e30
NORM_EPSILON = 1e-05

BLK_PARTS = ("z", "x", "core")
GROUP = ("x", "core")


def nested(reduce, value):
    for axis in reversed(BLK_PARTS):
        value = reduce(value, axis)
    return value


def axes_size(axes):
    size = 1
    for axis in axes:
        size *= lax.axis_size(axis)
    return size


def scatter_sum(value, axes):
    n = axes_size(axes)
    got = lax.all_to_all(value, axes, 0, 0, tiled=True)
    return jnp.sum(got.reshape((n, value.shape[0] // n) + value.shape[1:]), axis=0)


def gather_rows(value, axes):
    n = axes_size(axes)
    copies = jnp.broadcast_to(value[None], (n,) + value.shape).reshape((n * value.shape[0],) + value.shape[1:])
    return lax.all_to_all(copies, axes, 0, 0, tiled=True)


def all_combine(value, axes, combine):
    n = axes_size(axes)
    got = gather_rows(value[None], axes)
    return combine(got.reshape((n,) + value.shape), axis=0)


def butterfly_sum(value, axis):
    bit = 1
    while bit < lax.axis_size(axis):
        value = value + lax.ppermute(value, axis, [(i, i ^ bit) for i in range(lax.axis_size(axis))])
        bit *= 2
    return value


def blk_index():
    index = lax.axis_index("z")
    for axis in BLK_PARTS[1:]:
        index = index * lax.axis_size(axis) + lax.axis_index(axis)
    return index


def body(
    inputs,
    ln_gain,
    ln_bias,
    w_query,
    w_key,
    w_value,
    b_query,
    b_key,
    b_value,
    w_out,
    b_out,
    prefix_keys,
    prefix_values,
    suffix_keys,
    suffix_values,
    page_table,
    prompt_len,
    gen_len,
    parents,
):
    me = blk_index()
    group = axes_size(GROUP)
    member = lax.axis_index("x") * lax.axis_size("core") + lax.axis_index("core")
    steps = inputs.shape[0]
    batch = inputs.shape[1]
    feat_local = inputs.shape[2]
    feat_here = w_query.shape[1]
    heads_here = feat_here // HEAD_DIM
    pages_here = prefix_keys.shape[0]
    requests = page_table.shape[0]
    slot_count = page_table.shape[1]
    rows = steps * batch
    score_scale = 1.0 / math.sqrt(HEAD_DIM)
    my_request = me // BEAMS
    first_beam = my_request * BEAMS
    my_gen = gen_len[my_request]
    cols_all = 3 * feat_here
    col_block = cols_all // group
    chunk_rows = GEN // group

    beam_ids = jnp.arange(batch, dtype=jnp.int32)
    anc = {}
    for s in range(steps):
        x = beam_ids
        anc[(s, s)] = x
        for t in range(s, -1, -1):
            x = jnp.take(parents[t], x)
            anc[(t - 1, s)] = x
    origin = jnp.stack([anc[(-1, s)] for s in range(steps)])

    beam_request = beam_ids // BEAMS
    beam_prompt = jnp.take(prompt_len, beam_request)
    page_ids = me * pages_here + jnp.arange(pages_here, dtype=jnp.int32)
    slot_ids = jnp.arange(slot_count, dtype=jnp.int32)
    slot_live = slot_ids[None, :] * PAGE < prompt_len[:, None]
    page_match = (
        (page_table[:, :, None] == page_ids[None, None, :]) & slot_live[:, :, None]
    ).astype(jnp.int32)
    request_ids = jnp.arange(requests, dtype=jnp.int32)
    page_request = jnp.sum(page_match * request_ids[:, None, None], axis=(0, 1))
    page_slot = jnp.sum(page_match * slot_ids[None, :, None], axis=(0, 1))
    page_used = jnp.sum(page_match, axis=(0, 1)) > 0
    token_pos = (page_slot[:, None] * PAGE + jnp.arange(PAGE, dtype=jnp.int32)[None, :]).reshape(-1)
    token_request = jnp.repeat(page_request, PAGE)
    token_used = jnp.repeat(page_used, PAGE)
    prefix_live = (
        token_used[None, :]
        & (token_request[None, :] == beam_request[:, None])
        & (token_pos[None, :] < beam_prompt[:, None])
    )
    own_beam = me
    new_src = jnp.stack(
        [jnp.stack([anc[(t, s)][own_beam] if t <= s else own_beam for t in range(steps)]) for s in range(steps)]
    ) - first_beam
    final_origin = origin[steps - 1]
    pick = lax.dynamic_slice_in_dim(final_origin, first_beam, BEAMS) - first_beam


    rows_local = inputs.astype(jnp.float32).reshape(rows, feat_local)
    stats = jnp.stack([jnp.sum(rows_local, axis=1), jnp.sum(rows_local * rows_local, axis=1)], axis=1)
    stats = all_combine(stats, BLK_PARTS, jnp.sum)
    row_mean = stats[:, 0] / D
    variance = stats[:, 1] / D - row_mean * row_mean

    lanes = 128
    cw = feat_here // group
    weight_chunks = jnp.stack([w_query, w_key, w_value], axis=1).reshape(feat_local, 3, group, cw)
    weight_chunks = weight_chunks.transpose(2, 0, 1, 3).reshape(group, -1)
    norm_params = jnp.concatenate([ln_gain, ln_bias])
    pad = -(inputs.size + norm_params.shape[0]) % feat_here
    row_block = jnp.concatenate([inputs.reshape(-1), norm_params, jnp.zeros((pad,), inputs.dtype)])
    cache_chunks = jnp.concatenate(
        [suffix_keys[0].reshape(group, -1), suffix_values[0].reshape(group, -1)], axis=1
    )
    sent = jnp.concatenate(
        [weight_chunks, jnp.broadcast_to(row_block[None], (group, row_block.shape[0])), cache_chunks], axis=1
    )
    sent = sent.reshape(group, -1, feat_here)
    got = lax.all_to_all(sent, GROUP, 0, 0, tiled=True).reshape(group, -1)
    got, origin, prefix_live, new_src, pick = lax.optimization_barrier((got, origin, prefix_live, new_src, pick))
    n_w = feat_local * 3 * cw
    n_in = rows * feat_local
    n_row = row_block.shape[0]
    w_group = got[:, :n_w].reshape(group, feat_local, 3, cw)
    in_group = got[:, n_w : n_w + n_in].reshape(group, rows, feat_local).astype(jnp.float32)
    gain_group = got[:, n_w + n_in : n_w + n_in + feat_local].astype(jnp.float32)
    shift_group = got[:, n_w + n_in + feat_local : n_w + n_in + 2 * feat_local].astype(jnp.float32)
    spread = got[:, n_w + n_row :].reshape(group, 2, chunk_rows, feat_here)

    normed = (
        (in_group - row_mean[None, :, None]) * lax.rsqrt(variance + NORM_EPSILON)[None, :, None]
        * gain_group[:, None, :]
        + shift_group[:, None, :]
    ).astype(jnp.bfloat16)
    partial = jnp.einsum("grf,gfwc->rwc", normed, w_group, preferred_element_type=jnp.float32)
    partial = partial.reshape(steps, requests, BEAMS, 3, cw).transpose(1, 0, 2, 3, 4)
    summed = jnp.sum(lax.all_to_all(partial, "z", 0, 0, tiled=True).reshape(
        (lax.axis_size("z"), steps, BEAMS, 3, cw)), axis=0)
    bias_all = jnp.stack([b_query, b_key, b_value]).astype(jnp.float32).reshape(3, group, cw)
    bias_block = lax.dynamic_index_in_dim(bias_all, member, axis=1, keepdims=False)
    mine = (summed + bias_block).astype(jnp.bfloat16)

    q_blocks = gather_rows(mine[None, :, :, 0, :], BLK_PARTS)
    queries = q_blocks.reshape(requests, group, steps, BEAMS, cw).transpose(2, 0, 3, 1, 4).reshape(
        steps, batch, heads_here, HEAD_DIM)
    group_queries = lax.dynamic_slice_in_dim(queries, first_beam, BEAMS, axis=1)

    picked = jnp.take(spread, pick, axis=0).reshape(group, -1)

    kv_mine = mine[:, :, 1:, :]
    n_mine = steps * BEAMS * 2 * cw
    sent2 = jnp.concatenate(
        [jnp.broadcast_to(kv_mine.reshape(1, -1), (group, n_mine)), picked], axis=1
    )
    got2 = lax.all_to_all(sent2, GROUP, 0, 0, tiled=True)
    kv = got2[:, :n_mine].reshape(group, steps, BEAMS, 2, cw).transpose(1, 2, 3, 0, 4).reshape(
        steps, BEAMS, 2, feat_here)
    back = got2[:, n_mine:].reshape(group, 2, chunk_rows, feat_here).transpose(1, 0, 2, 3).reshape(2, GEN, feat_here)
    key_new = kv[:, :, 0]
    value_new = kv[:, :, 1]

    page_keys = prefix_keys.reshape(pages_here * PAGE, heads_here, HEAD_DIM)
    page_values = prefix_values.reshape(pages_here * PAGE, heads_here, HEAD_DIM)
    flat_queries = queries.reshape(rows, heads_here, HEAD_DIM)
    prompt_scores = (
        jnp.einsum("rhd,thd->rht", flat_queries, page_keys, preferred_element_type=jnp.float32)
        * score_scale
    ).reshape(steps, batch, heads_here, -1)
    prompt_live = prefix_live[None, :, None, :]
    prompt_top = jnp.max(jnp.where(prompt_live, prompt_scores, MASKED), axis=3)

    group_origin = lax.dynamic_slice_in_dim(origin, first_beam, BEAMS, axis=1)
    own_keys = suffix_keys[0].reshape(GEN, heads_here, HEAD_DIM)
    own_values = suffix_values[0].reshape(GEN, heads_here, HEAD_DIM)
    cache_scores = (
        jnp.einsum("sbhd,jhd->sbhj", group_queries, own_keys, preferred_element_type=jnp.float32)
        * score_scale
    )
    gen_rows = jnp.arange(GEN, dtype=jnp.int32)
    cache_live = (group_origin == me)[:, :, None, None] & (gen_rows < my_gen)[None, None, None, :]
    cache_top = jnp.max(jnp.where(cache_live, cache_scores, MASKED), axis=3)

    own_queries = lax.dynamic_index_in_dim(group_queries, member, axis=1, keepdims=False)
    step_ids = jnp.arange(steps, dtype=jnp.int32)
    new_keys_here = key_new[step_ids[None, :], new_src].reshape(steps, steps, heads_here, HEAD_DIM)
    new_values_here = value_new[step_ids[None, :], new_src].reshape(steps, steps, heads_here, HEAD_DIM)
    new_scores = (
        jnp.einsum("shd,sthd->sht", own_queries, new_keys_here, preferred_element_type=jnp.float32)
        * score_scale
    )
    new_live = (step_ids[None, :] <= step_ids[:, None])[:, None, :]
    new_top = jnp.max(jnp.where(new_live, new_scores, MASKED), axis=2)

    local_top = prompt_top
    group_top = jnp.maximum(
        lax.dynamic_slice_in_dim(local_top, first_beam, BEAMS, axis=1), cache_top
    )
    local_top = lax.dynamic_update_slice_in_dim(local_top, group_top, first_beam, axis=1)
    own_top = jnp.maximum(lax.dynamic_index_in_dim(local_top, own_beam, axis=1, keepdims=True), new_top[:, None])
    local_top = lax.dynamic_update_slice_in_dim(local_top, own_top, own_beam, axis=1)
    top = all_combine(local_top, BLK_PARTS, jnp.max)

    prompt_weights = jnp.where(
        prompt_live, jnp.exp(prompt_scores - top[:, :, :, None]), 0.0
    ).astype(jnp.bfloat16)
    weighted = jnp.einsum(
        "rht,thd->rhd",
        prompt_weights.reshape(rows, heads_here, -1),
        page_values,
        preferred_element_type=jnp.float32,
    ).reshape(steps, batch, heads_here, HEAD_DIM)
    totals = jnp.sum(prompt_weights.astype(jnp.float32), axis=3)

    group_top_all = lax.dynamic_slice_in_dim(top, first_beam, BEAMS, axis=1)
    cache_weights = jnp.where(
        cache_live, jnp.exp(cache_scores - group_top_all[:, :, :, None]), 0.0
    ).astype(jnp.bfloat16)
    cache_weighted = jnp.einsum(
        "sbhj,jhd->sbhd", cache_weights, own_values, preferred_element_type=jnp.float32
    )
    cache_totals = jnp.sum(cache_weights.astype(jnp.float32), axis=3)

    own_top_all = lax.dynamic_index_in_dim(top, own_beam, axis=1, keepdims=False)
    new_weights = jnp.where(
        new_live, jnp.exp(new_scores - own_top_all[:, :, None]), 0.0
    ).astype(jnp.bfloat16)
    new_weighted = jnp.einsum(
        "sht,sthd->shd", new_weights, new_values_here, preferred_element_type=jnp.float32
    )
    new_totals = jnp.sum(new_weights.astype(jnp.float32), axis=2)

    group_weighted = lax.dynamic_slice_in_dim(weighted, first_beam, BEAMS, axis=1) + cache_weighted
    weighted = lax.dynamic_update_slice_in_dim(weighted, group_weighted, first_beam, axis=1)
    group_totals = lax.dynamic_slice_in_dim(totals, first_beam, BEAMS, axis=1) + cache_totals
    totals = lax.dynamic_update_slice_in_dim(totals, group_totals, first_beam, axis=1)
    own_weighted = lax.dynamic_index_in_dim(weighted, own_beam, axis=1, keepdims=True) + new_weighted[:, None]
    weighted = lax.dynamic_update_slice_in_dim(weighted, own_weighted, own_beam, axis=1)
    own_totals = lax.dynamic_index_in_dim(totals, own_beam, axis=1, keepdims=True) + new_totals[:, None]
    totals = lax.dynamic_update_slice_in_dim(totals, own_totals, own_beam, axis=1)

    packed = jnp.concatenate(
        [
            weighted.reshape(rows, feat_here),
            jnp.pad(totals.reshape(rows, heads_here), ((0, 0), (0, lanes - heads_here))),
        ],
        axis=1,
    )
    blk_stages = BLK_PARTS
    packed = scatter_sum(packed, blk_stages)
    part_rows = packed.shape[0]
    weighted = packed[:, :feat_here].reshape(part_rows, heads_here, HEAD_DIM)
    totals = packed[:, feat_here : feat_here + heads_here]
    attention = (weighted / totals[:, :, None]).reshape(part_rows, feat_here).astype(jnp.bfloat16)
    attention = gather_rows(attention, blk_stages)
    head_terms = jnp.dot(attention, w_out, preferred_element_type=jnp.float32)
    head_stages = ("head",)
    head_part = scatter_sum(head_terms, head_stages)
    hidden = gather_rows((head_part + b_out.astype(jnp.float32)[None, :]).astype(jnp.bfloat16), head_stages)
    hidden = hidden.reshape(steps, batch, -1)

    my_final_src = [anc[(t, steps - 1)][own_beam] - first_beam for t in range(steps)]
    write_rows = my_gen + step_ids
    hit = gen_rows[:, None] == write_rows[None, :]
    chosen = jnp.argmax(hit, axis=1)
    written = jnp.any(hit, axis=1)[:, None]

    def finish(cache, fresh):
        new_rows = jnp.stack([fresh[t, my_final_src[t]] for t in range(steps)])
        return jnp.where(written, jnp.take(new_rows, chosen, axis=0), cache)[None]

    final_keys = finish(back[0], key_new)
    final_values = finish(back[1], value_new)
    return hidden, final_keys, final_values


def solution(mesh):
    heads = mesh.shape["head"]
    blocks = mesh.shape["blk"]
    cores = 2
    group_chips = BEAMS // cores
    devices = np.asarray(mesh.devices).reshape(heads, blocks // BEAMS, group_chips, cores)
    fine = Mesh(devices, ("head",) + BLK_PARTS)
    blk = BLK_PARTS
    in_specs = (
        P(None, None, blk),
        P(blk),
        P(blk),
        P(blk, "head"),
        P(blk, "head"),
        P(blk, "head"),
        P("head"),
        P("head"),
        P("head"),
        P("head", blk),
        P(blk),
        P(blk, None, "head"),
        P(blk, None, "head"),
        P(blk, None, "head"),
        P(blk, None, "head"),
        P(),
        P(),
        P(),
        P(),
    )
    out_specs = (P(None, None, blk), P(blk, None, "head"), P(blk, None, "head"))
    return jax.shard_map(body, mesh=fine, in_specs=in_specs, out_specs=out_specs, check_vma=False)
```

```python
import math

import jax
import jax.numpy as jnp
import numpy as np
from jax import lax
from jax.sharding import Mesh
from jax.sharding import PartitionSpec as P

D = 7168
HEAD_DIM = 128
BEAMS = 8
PAGE = 16
GEN = 256
STEPS = 4

MASKED = -1e30
NORM_EPSILON = 1e-05

BLK_PARTS = ("z", "x", "core")
GROUP = ("x", "core")


def nested(reduce, value):
    for axis in reversed(BLK_PARTS):
        value = reduce(value, axis)
    return value


def axes_size(axes):
    size = 1
    for axis in axes:
        size *= lax.axis_size(axis)
    return size


def scatter_sum(value, axes):
    n = axes_size(axes)
    got = lax.all_to_all(value, axes, 0, 0, tiled=True)
    return jnp.sum(got.reshape((n, value.shape[0] // n) + value.shape[1:]), axis=0)


def gather_rows(value, axes):
    n = axes_size(axes)
    copies = jnp.broadcast_to(value[None], (n,) + value.shape).reshape((n * value.shape[0],) + value.shape[1:])
    return lax.all_to_all(copies, axes, 0, 0, tiled=True)


def all_combine(value, axes, combine):
    n = axes_size(axes)
    got = gather_rows(value[None], axes)
    return combine(got.reshape((n,) + value.shape), axis=0)


def butterfly_sum(value, axis):
    bit = 1
    while bit < lax.axis_size(axis):
        value = value + lax.ppermute(value, axis, [(i, i ^ bit) for i in range(lax.axis_size(axis))])
        bit *= 2
    return value


def blk_index():
    index = lax.axis_index("z")
    for axis in BLK_PARTS[1:]:
        index = index * lax.axis_size(axis) + lax.axis_index(axis)
    return index


def body(
    inputs,
    ln_gain,
    ln_bias,
    w_query,
    w_key,
    w_value,
    b_query,
    b_key,
    b_value,
    w_out,
    b_out,
    prefix_keys,
    prefix_values,
    suffix_keys,
    suffix_values,
    page_table,
    prompt_len,
    gen_len,
    parents,
):
    me = blk_index()
    group = axes_size(GROUP)
    member = lax.axis_index("x") * lax.axis_size("core") + lax.axis_index("core")
    steps = inputs.shape[0]
    batch = inputs.shape[1]
    feat_local = inputs.shape[2]
    feat_here = w_query.shape[1]
    heads_here = feat_here // HEAD_DIM
    pages_here = prefix_keys.shape[0]
    requests = page_table.shape[0]
    slot_count = page_table.shape[1]
    rows = steps * batch
    score_scale = 1.0 / math.sqrt(HEAD_DIM)
    my_request = me // BEAMS
    first_beam = my_request * BEAMS
    my_gen = gen_len[my_request]
    cols_all = 3 * feat_here
    col_block = cols_all // group
    chunk_rows = GEN // group

    beam_ids = jnp.arange(batch, dtype=jnp.int32)
    anc = {}
    for s in range(steps):
        x = beam_ids
        anc[(s, s)] = x
        for t in range(s, -1, -1):
            x = jnp.take(parents[t], x)
            anc[(t - 1, s)] = x
    origin = jnp.stack([anc[(-1, s)] for s in range(steps)])

    beam_request = beam_ids // BEAMS
    beam_prompt = jnp.take(prompt_len, beam_request)
    page_ids = me * pages_here + jnp.arange(pages_here, dtype=jnp.int32)
    slot_ids = jnp.arange(slot_count, dtype=jnp.int32)
    slot_live = slot_ids[None, :] * PAGE < prompt_len[:, None]
    page_match = (
        (page_table[:, :, None] == page_ids[None, None, :]) & slot_live[:, :, None]
    ).astype(jnp.int32)
    request_ids = jnp.arange(requests, dtype=jnp.int32)
    page_request = jnp.sum(page_match * request_ids[:, None, None], axis=(0, 1))
    page_slot = jnp.sum(page_match * slot_ids[None, :, None], axis=(0, 1))
    page_used = jnp.sum(page_match, axis=(0, 1)) > 0
    token_pos = (page_slot[:, None] * PAGE + jnp.arange(PAGE, dtype=jnp.int32)[None, :]).reshape(-1)
    token_request = jnp.repeat(page_request, PAGE)
    token_used = jnp.repeat(page_used, PAGE)
    prefix_live = (
        token_used[None, :]
        & (token_request[None, :] == beam_request[:, None])
        & (token_pos[None, :] < beam_prompt[:, None])
    )
    own_beam = me
    new_src = jnp.stack(
        [jnp.stack([anc[(t, s)][own_beam] if t <= s else own_beam for t in range(steps)]) for s in range(steps)]
    ) - first_beam
    final_origin = origin[steps - 1]
    pick = lax.dynamic_slice_in_dim(final_origin, first_beam, BEAMS) - first_beam


    rows_local = inputs.astype(jnp.float32).reshape(rows, feat_local)
    stats = jnp.stack([jnp.sum(rows_local, axis=1), jnp.sum(rows_local * rows_local, axis=1)], axis=1)
    stats = all_combine(stats, BLK_PARTS, jnp.sum)
    row_mean = stats[:, 0] / D
    variance = stats[:, 1] / D - row_mean * row_mean

    lanes = 128
    cw = feat_here // group
    weight_chunks = jnp.stack([w_query, w_key, w_value], axis=1).reshape(feat_local, 3, group, cw)
    weight_chunks = weight_chunks.transpose(2, 0, 1, 3).reshape(group, -1)
    norm_params = jnp.concatenate([ln_gain, ln_bias])
    pad = -(inputs.size + norm_params.shape[0]) % lanes
    row_block = jnp.concatenate([inputs.reshape(-1), norm_params, jnp.zeros((pad,), inputs.dtype)])
    cache_chunks = jnp.concatenate(
        [suffix_keys[0].reshape(group, -1), suffix_values[0].reshape(group, -1)], axis=1
    )
    sent = jnp.concatenate(
        [weight_chunks, jnp.broadcast_to(row_block[None], (group, row_block.shape[0])), cache_chunks], axis=1
    )
    sent = sent.reshape(group, -1, lanes)
    got = lax.all_to_all(sent, GROUP, 0, 0, tiled=True).reshape(group, -1)
    got, origin, prefix_live, new_src, pick = lax.optimization_barrier((got, origin, prefix_live, new_src, pick))
    n_w = feat_local * 3 * cw
    n_in = rows * feat_local
    n_row = row_block.shape[0]
    w_group = got[:, :n_w].reshape(group, feat_local, 3, cw)
    in_group = got[:, n_w : n_w + n_in].reshape(group, rows, feat_local).astype(jnp.float32)
    gain_group = got[:, n_w + n_in : n_w + n_in + feat_local].astype(jnp.float32)
    shift_group = got[:, n_w + n_in + feat_local : n_w + n_in + 2 * feat_local].astype(jnp.float32)
    spread = got[:, n_w + n_row :].reshape(group, 2, chunk_rows, feat_here)

    normed = (
        (in_group - row_mean[None, :, None]) * lax.rsqrt(variance + NORM_EPSILON)[None, :, None]
        * gain_group[:, None, :]
        + shift_group[:, None, :]
    ).astype(jnp.bfloat16)
    partial = jnp.einsum("grf,gfwc->rwc", normed, w_group, preferred_element_type=jnp.float32)
    partial = partial.reshape(steps, requests, BEAMS, 3, cw).transpose(1, 0, 2, 3, 4)
    summed = jnp.sum(lax.all_to_all(partial, "z", 0, 0, tiled=True).reshape(
        (lax.axis_size("z"), steps, BEAMS, 3, cw)), axis=0)
    bias_all = jnp.stack([b_query, b_key, b_value]).astype(jnp.float32).reshape(3, group, cw)
    bias_block = lax.dynamic_index_in_dim(bias_all, member, axis=1, keepdims=False)
    mine = (summed + bias_block).astype(jnp.bfloat16)

    q_blocks = gather_rows(mine[:, :, 0, :].reshape(1, -1, 128), BLK_PARTS)
    queries = q_blocks.reshape(requests, group, steps, BEAMS, cw).transpose(2, 0, 3, 1, 4).reshape(
        steps, batch, heads_here, HEAD_DIM)
    group_queries = lax.dynamic_slice_in_dim(queries, first_beam, BEAMS, axis=1)

    picked = jnp.take(spread, pick, axis=0).reshape(group, -1)

    kv_mine = mine[:, :, 1:, :]
    n_mine = steps * BEAMS * 2 * cw
    sent2 = jnp.concatenate(
        [jnp.broadcast_to(kv_mine.reshape(1, -1), (group, n_mine)), picked], axis=1
    )
    got2 = lax.all_to_all(sent2, GROUP, 0, 0, tiled=True)
    kv = got2[:, :n_mine].reshape(group, steps, BEAMS, 2, cw).transpose(1, 2, 3, 0, 4).reshape(
        steps, BEAMS, 2, feat_here)
    back = got2[:, n_mine:].reshape(group, 2, chunk_rows, feat_here).transpose(1, 0, 2, 3).reshape(2, GEN, feat_here)
    key_new = kv[:, :, 0]
    value_new = kv[:, :, 1]

    page_keys = prefix_keys.reshape(pages_here * PAGE, heads_here, HEAD_DIM)
    page_values = prefix_values.reshape(pages_here * PAGE, heads_here, HEAD_DIM)
    flat_queries = queries.reshape(rows, heads_here, HEAD_DIM)
    prompt_scores = (
        jnp.einsum("rhd,thd->rht", flat_queries, page_keys, preferred_element_type=jnp.float32)
        * score_scale
    ).reshape(steps, batch, heads_here, -1)
    prompt_live = prefix_live[None, :, None, :]
    prompt_top = jnp.max(jnp.where(prompt_live, prompt_scores, MASKED), axis=3)

    group_origin = lax.dynamic_slice_in_dim(origin, first_beam, BEAMS, axis=1)
    own_keys = suffix_keys[0].reshape(GEN, heads_here, HEAD_DIM)
    own_values = suffix_values[0].reshape(GEN, heads_here, HEAD_DIM)
    cache_scores = (
        jnp.einsum("sbhd,jhd->sbhj", group_queries, own_keys, preferred_element_type=jnp.float32)
        * score_scale
    )
    gen_rows = jnp.arange(GEN, dtype=jnp.int32)
    cache_live = (group_origin == me)[:, :, None, None] & (gen_rows < my_gen)[None, None, None, :]
    cache_top = jnp.max(jnp.where(cache_live, cache_scores, MASKED), axis=3)

    own_queries = lax.dynamic_index_in_dim(group_queries, member, axis=1, keepdims=False)
    step_ids = jnp.arange(steps, dtype=jnp.int32)
    new_keys_here = key_new[step_ids[None, :], new_src].reshape(steps, steps, heads_here, HEAD_DIM)
    new_values_here = value_new[step_ids[None, :], new_src].reshape(steps, steps, heads_here, HEAD_DIM)
    new_scores = (
        jnp.einsum("shd,sthd->sht", own_queries, new_keys_here, preferred_element_type=jnp.float32)
        * score_scale
    )
    new_live = (step_ids[None, :] <= step_ids[:, None])[:, None, :]
    new_top = jnp.max(jnp.where(new_live, new_scores, MASKED), axis=2)

    local_top = prompt_top
    group_top = jnp.maximum(
        lax.dynamic_slice_in_dim(local_top, first_beam, BEAMS, axis=1), cache_top
    )
    local_top = lax.dynamic_update_slice_in_dim(local_top, group_top, first_beam, axis=1)
    own_top = jnp.maximum(lax.dynamic_index_in_dim(local_top, own_beam, axis=1, keepdims=True), new_top[:, None])
    local_top = lax.dynamic_update_slice_in_dim(local_top, own_top, own_beam, axis=1)
    top = all_combine(local_top, BLK_PARTS, jnp.max)

    prompt_weights = jnp.where(
        prompt_live, jnp.exp(prompt_scores - top[:, :, :, None]), 0.0
    ).astype(jnp.bfloat16)
    weighted = jnp.einsum(
        "rht,thd->rhd",
        prompt_weights.reshape(rows, heads_here, -1),
        page_values,
        preferred_element_type=jnp.float32,
    ).reshape(steps, batch, heads_here, HEAD_DIM)
    totals = jnp.sum(prompt_weights.astype(jnp.float32), axis=3)

    group_top_all = lax.dynamic_slice_in_dim(top, first_beam, BEAMS, axis=1)
    cache_weights = jnp.where(
        cache_live, jnp.exp(cache_scores - group_top_all[:, :, :, None]), 0.0
    ).astype(jnp.bfloat16)
    cache_weighted = jnp.einsum(
        "sbhj,jhd->sbhd", cache_weights, own_values, preferred_element_type=jnp.float32
    )
    cache_totals = jnp.sum(cache_weights.astype(jnp.float32), axis=3)

    own_top_all = lax.dynamic_index_in_dim(top, own_beam, axis=1, keepdims=False)
    new_weights = jnp.where(
        new_live, jnp.exp(new_scores - own_top_all[:, :, None]), 0.0
    ).astype(jnp.bfloat16)
    new_weighted = jnp.einsum(
        "sht,sthd->shd", new_weights, new_values_here, preferred_element_type=jnp.float32
    )
    new_totals = jnp.sum(new_weights.astype(jnp.float32), axis=2)

    group_weighted = lax.dynamic_slice_in_dim(weighted, first_beam, BEAMS, axis=1) + cache_weighted
    weighted = lax.dynamic_update_slice_in_dim(weighted, group_weighted, first_beam, axis=1)
    group_totals = lax.dynamic_slice_in_dim(totals, first_beam, BEAMS, axis=1) + cache_totals
    totals = lax.dynamic_update_slice_in_dim(totals, group_totals, first_beam, axis=1)
    own_weighted = lax.dynamic_index_in_dim(weighted, own_beam, axis=1, keepdims=True) + new_weighted[:, None]
    weighted = lax.dynamic_update_slice_in_dim(weighted, own_weighted, own_beam, axis=1)
    own_totals = lax.dynamic_index_in_dim(totals, own_beam, axis=1, keepdims=True) + new_totals[:, None]
    totals = lax.dynamic_update_slice_in_dim(totals, own_totals, own_beam, axis=1)

    packed = jnp.concatenate(
        [
            weighted.reshape(rows, feat_here),
            jnp.pad(totals.reshape(rows, heads_here), ((0, 0), (0, lanes - heads_here))),
        ],
        axis=1,
    )
    blk_stages = BLK_PARTS
    packed = scatter_sum(packed, blk_stages)
    part_rows = packed.shape[0]
    weighted = packed[:, :feat_here].reshape(part_rows, heads_here, HEAD_DIM)
    totals = packed[:, feat_here : feat_here + heads_here]
    attention = (weighted / totals[:, :, None]).reshape(part_rows, feat_here).astype(jnp.bfloat16)
    attention = gather_rows(attention, blk_stages)
    head_terms = jnp.dot(attention, w_out, preferred_element_type=jnp.float32)
    head_stages = ("head",)
    head_part = scatter_sum(head_terms, head_stages)
    hidden = gather_rows((head_part + b_out.astype(jnp.float32)[None, :]).astype(jnp.bfloat16), head_stages)
    hidden = hidden.reshape(steps, batch, -1)

    my_final_src = [anc[(t, steps - 1)][own_beam] - first_beam for t in range(steps)]
    write_rows = my_gen + step_ids
    hit = gen_rows[:, None] == write_rows[None, :]
    chosen = jnp.argmax(hit, axis=1)
    written = jnp.any(hit, axis=1)[:, None]

    def finish(cache, fresh):
        new_rows = jnp.stack([fresh[t, my_final_src[t]] for t in range(steps)])
        return jnp.where(written, jnp.take(new_rows, chosen, axis=0), cache)[None]

    final_keys = finish(back[0], key_new)
    final_values = finish(back[1], value_new)
    return hidden, final_keys, final_values


def solution(mesh):
    heads = mesh.shape["head"]
    blocks = mesh.shape["blk"]
    cores = 2
    group_chips = BEAMS // cores
    devices = np.asarray(mesh.devices).reshape(heads, blocks // BEAMS, group_chips, cores)
    fine = Mesh(devices, ("head",) + BLK_PARTS)
    blk = BLK_PARTS
    in_specs = (
        P(None, None, blk),
        P(blk),
        P(blk),
        P(blk, "head"),
        P(blk, "head"),
        P(blk, "head"),
        P("head"),
        P("head"),
        P("head"),
        P("head", blk),
        P(blk),
        P(blk, None, "head"),
        P(blk, None, "head"),
        P(blk, None, "head"),
        P(blk, None, "head"),
        P(),
        P(),
        P(),
        P(),
    )
    out_specs = (P(None, None, blk), P(blk, None, "head"), P(blk, None, "head"))
    return jax.shard_map(body, mesh=fine, in_specs=in_specs, out_specs=out_specs, check_vma=False)
```
